512 devices in a mesh: dp: 8 (over z_lo), seq: 4 (over z_hi, core), expert: 16 (over x, y).
Axes of the slice: x: 4, y: 4, z: 16 (z_hi: 2, z_lo: 8; z = z_hi * 8 + z_lo), core: 2. Of those that a mesh axis runs over, the one named last changes fastest.
Arguments:
- keys: bfloat16 [16, 4096, 512], P('expert', ('dp', 'seq')), may hold values from -4 to 4
- values: bfloat16 [16, 4096, 512], P('expert', ('dp', 'seq')), may hold values from -5 to 5
- queries: bfloat16 [16, 32, 4096], P('expert', ('dp', 'seq')), may hold values from -80 to 80
- residual: bfloat16 [16, 32, 2048], P('expert', ('dp', 'seq')), may hold values from -9 to 9
- out_proj: bfloat16 [4096, 2048], P(('dp', 'seq')), may hold values from -0.09375 to 0.09375
- norm_gain: bfloat16 [2048], replicated, may hold values from 0.25 to 1.75
- router: bfloat16 [2048, 128], replicated, may hold values from -8 to 8
- w_gate: bfloat16 [128, 2048, 768], P(('dp', 'expert'), None, 'seq'), may hold values from -0.125 to 0.125
- w_up: bfloat16 [128, 2048, 768], P(('dp', 'expert'), None, 'seq'), may hold values from -0.125 to 0.125
- w_down: bfloat16 [128, 768, 2048], P(('dp', 'expert'), 'seq'), may hold values from -0.21875 to 0.21875
- head_vec: bfloat16 [2048], replicated, may hold values from -0.09 to 0.09
- routes: int32 [16, 32, 8], P('expert', 'dp'), may hold values from 0 to 127, all different within a row; in each aligned block of 4 rows (0 to 3, 4 to 7, ..., all dimensions but the last counted through in order) at most 2 rows name the same one
- step_pos: int32 [16, 32], P('expert'), may hold values from 0 to 4095, as said below
- labels: int32 [16, 32], P('expert', ('dp', 'seq')), may hold values 0 or 1
- trace_len: int32 [16, 8], P('expert'), may hold values from 1 to 1024, 4096 in all within a row
Outputs:
- loss: float32 [], replicated
- grad_down: bfloat16 [128, 768, 2048], P(('dp', 'expert'), 'seq')
- grad_router: bfloat16 [2048, 128], P(('dp', 'seq', 'expert'))
The draws below stay inside these ranges and needn't reach their ends.
Inputs may be any that keep to these rules, and one draw needn't show every extreme that they name: `step_pos`: increasing along each pack; distinct. `routes`: in each aligned block of 4 step ends (those of one index of dp in one pack) no expert is named by more than 2 of them.
All inputs are finite; a program needn't handle non-finite values. No bound on the sum of `labels` on one device may be relied on, other than what follows from the above.
Results may differ from the reference program's by a relative error of at most 0.018.
Values may be sent and summed in bfloat16 or wider, within the bound.
No kernel may reach another device: no remote copies, remote signals or barrier semaphores. Data moves between devices by JAX's collectives and lax.ppermute only.
A program may use at most 64 MiB of HBM per device.

```python
import math
import jax
import jax.numpy as jnp
import numpy as np
from jax import lax

D = 2048
QUERY_HEADS = 32
KEY_VALUE_HEADS = 4
HEAD_WIDTH = 128
FF = 768
TOPK = 8
TRACES = 8
TOK_DEV = 128
PACK_COUNT = 16
PACK_TOKENS = 4096
STEPS = 32
EXPERTS = 128
BLOCK = 4
CAP = 2


def step_positions(key):
    window = min(PACK_TOKENS, max(2 * STEPS, TOK_DEV))
    forced = jax.random.randint(jax.random.fold_in(key, 5), (), 0, PACK_COUNT)
    coins = jax.random.randint(jax.random.fold_in(key, 6), (PACK_COUNT,), 0, 2)
    clustered = (coins == 1) | (jnp.arange(PACK_COUNT) == forced)

    def one_pack(pack_number):
        pack_key = jax.random.fold_in(key, pack_number)
        spread_out = jnp.sort(jax.random.permutation(pack_key, PACK_TOKENS)[:STEPS]).astype(jnp.int32)
        offset = jax.random.randint(jax.random.fold_in(pack_key, 71), (), 0, PACK_TOKENS - window + 1)
        inside = jnp.sort(jax.random.permutation(jax.random.fold_in(pack_key, 73), window)[:STEPS]).astype(jnp.int32)
        packed_close = (inside + offset).astype(jnp.int32)
        return jnp.where(clustered[pack_number], packed_close, spread_out).astype(jnp.int32)
    return jax.vmap(one_pack)(jnp.arange(PACK_COUNT))


def draw_step_pos(key, part):
    return step_positions(jax.random.fold_in(key, 11))


def draw_keys(key, part):
    gaussian_portion = jax.random.normal(jax.random.fold_in(key, 23), (PACK_COUNT, PACK_TOKENS, KEY_VALUE_HEADS * HEAD_WIDTH), jnp.float32)
    gaussian_portion = jnp.clip(gaussian_portion, -4.0, 4.0)
    return gaussian_portion.astype(jnp.bfloat16)


def draw_queries(key, part):
    gaussian_portion = jax.random.normal(jax.random.fold_in(key, 37), (PACK_COUNT, STEPS, QUERY_HEADS * HEAD_WIDTH), jnp.float32)
    gaussian_portion = jnp.clip(gaussian_portion, -5.0, 5.0)
    return gaussian_portion.astype(jnp.bfloat16)


def draw_router(key, part):
    spread = D ** (-0.5)
    gaussian_portion = jax.random.normal(jax.random.fold_in(key, 53), (D, EXPERTS), jnp.float32) * spread
    gaussian_portion = jnp.clip(gaussian_portion, -6.0 * spread, 6.0 * spread)
    return gaussian_portion.astype(jnp.bfloat16)


def head_direction(key):
    direction = jax.random.normal(jax.random.fold_in(key, 91), (D,), jnp.float32)
    return jnp.clip(direction, -3.0, 3.0)


def draw_head_vec(key, part):
    return (0.03 * head_direction(key)).astype(jnp.bfloat16)


def draw_residual(key, part):
    noise = jax.random.normal(jax.random.fold_in(key, 97), (PACK_COUNT, STEPS, D), jnp.float32)
    noise = jnp.clip(noise, -5.0, 5.0)
    reach = 10.0 / (0.03 * D)
    ramp = jnp.arange(STEPS, dtype=jnp.float32) / max(STEPS - 1, 1)
    direction = head_direction(key)
    combined = noise + reach * ramp[None, :, None] * direction[None, None, :]
    return jnp.clip(combined, -9.0, 9.0).astype(jnp.bfloat16)


def with_ends(result, own_key, smallest, largest):
    spot = [jax.random.randint(jax.random.fold_in(own_key, axis), (), 0, length) for axis, length in enumerate(result.shape)]
    main_axis = result.shape.index(max(result.shape))
    next_to = spot[:main_axis] + [(spot[main_axis] + 1) % result.shape[main_axis]] + spot[main_axis + 1:]
    return result.at[tuple(spot)].set(smallest).at[tuple(next_to)].set(largest)


def block_levels(key, shape, cuts, smallest, top_value):
    loudness = 1.0
    for position, blocks in cuts:
        draws = jax.random.uniform(jax.random.fold_in(jax.random.fold_in(key, 6), position), (blocks,), jnp.float32, smallest / len(cuts), top_value / len(cuts))
        loudness = loudness * jnp.repeat(jnp.exp(draws), shape[position] // blocks).reshape((-1,) + (1,) * (len(shape) - 1 - position))
    return loudness


def length_profile(number_of, total, bound, lean):
    loads = [(1 << 20) // math.isqrt(standing ** lean) + 1 for standing in range(2, number_of + 1)]
    surplus, given = total - bound - (number_of - 1), [1] * (number_of - 1)
    while surplus > 0:
        candidates = [i for i in range(number_of - 1) if given[i] < bound]
        mass, budget = sum([loads[i] for i in candidates]), surplus
        for i in candidates:
            addition = min(bound - given[i], max(1, budget * loads[i] // mass), surplus)
            given[i] = given[i] + addition
            surplus = surplus - addition
    return np.array([bound] + given)


def ragged(key, amount, total, limit, skew):
    if amount == 2:
        one = jax.random.randint(key, (), max(1, total - limit), min(limit, total - 1) + 1)
        return jnp.stack([one, total - one])
    tallies = jnp.asarray(length_profile(amount, total, limit, skew), jnp.int32)
    twos = (amount - 1) // 2
    donor, receiver = tallies[1:1 + 2 * twos:2], tallies[2:2 + 2 * twos:2]
    slack = jnp.minimum(donor - 1, limit - receiver)
    moved = jax.random.randint(jax.random.fold_in(key, 1), (twos,), 0, 1 << 20) % (slack + 1)
    tallies = tallies.at[1:1 + 2 * twos:2].set(donor - moved).at[2:2 + 2 * twos:2].set(receiver + moved)
    return tallies[jax.random.permutation(jax.random.fold_in(key, 2), amount)]


def assign_block(own_key, own, number, rows, count, top, most, skew):
    ranking = jax.random.permutation(own_key, count)
    crowded, common = shares(count, rows * top, most, skew, True), shares(count, rows * top, most, skew, False)
    places = jnp.arange(count)

    def named(sizes, rotation):
        used = int((sizes > 0).sum())
        fixed = max(1, used // 4)
        moved = fixed + (places - fixed + rotation * (used - fixed)) % max(1, count - fixed)
        return jnp.zeros((count,), jnp.int32).at[ranking[jnp.where(places < fixed, places, moved)]].set(jnp.asarray(sizes, jnp.int32))

    sizes = jnp.where(number % 4 == 0, named(crowded, number // 4), named(common, number - number // 4 - 1))
    mixed = jax.random.permutation(jax.random.fold_in(own, 3), count)
    giver, sink = mixed[0:count // 2 * 2:2], mixed[1:count // 2 * 2:2]
    slack = jnp.minimum(sizes[giver] - 1, most - sizes[sink]) // 2
    slack = jnp.where((giver == ranking[0]) | (sink == ranking[0]) | (sizes[sink] == 0), 0, jnp.maximum(slack, 0))
    moved = jax.random.randint(jax.random.fold_in(own, 4), (count // 2,), 0, 1 << 20) % (slack + 1)
    sizes = sizes.at[giver].add(-moved).at[sink].add(moved)
    items = jnp.searchsorted(jnp.cumsum(sizes), jnp.arange(rows * top), side="right").astype(jnp.int32)
    listing = items.reshape(top, rows).T
    listing = listing[jax.random.permutation(jax.random.fold_in(own, 1), rows)]
    rotation = jax.random.randint(jax.random.fold_in(own, 2), (rows, 1), 0, top)
    return jnp.take_along_axis(listing, (jnp.arange(top)[None, :] + rotation) % top, axis=1)


def shares(number_of, total, most, lean, full):
    weights = [(1 << 20) // math.isqrt(standing ** lean) + 1 for standing in range(1, number_of + 1)]
    largest = most if full else min(most, max(-(-total // number_of), total * weights[0] // sum(weights)))
    least = 1 if total - largest >= number_of - 1 else 0
    given, surplus = [largest] + [least] * (number_of - 1), total - largest - least * (number_of - 1)
    while surplus > 0:
        candidates = [i for i in range(1, number_of) if given[i] < largest] or [i for i in range(1, number_of) if given[i] < most]
        pool, remaining = sum([weights[i] for i in candidates]), surplus
        for i in candidates:
            more = min(most - given[i], max(1, remaining * weights[i] // pool), surplus)
            given[i] = given[i] + more
            surplus = surplus - more
    return np.array(given)


def centred(stream_key, extent, width, limit, cuts=(), kind=jnp.bfloat16):
    entries = width * jax.random.normal(stream_key, extent, jnp.float32)
    if cuts:
        entries = entries * block_levels(stream_key, extent, cuts, -0.22, 0.18)
    return jnp.clip(entries, -limit, limit).astype(kind)


def setup_inputs(seed: int = 0) -> dict:
    seeds = jax.random.split(jax.random.key(seed), 16)
    keys = draw_keys(jax.random.fold_in(seeds[15], 71), 0)
    values = centred(seeds[1], (PACK_COUNT, PACK_TOKENS, KEY_VALUE_HEADS * HEAD_WIDTH), 1.0, 5.0, ((0, 16), (1, 32)))
    queries = draw_queries(jax.random.fold_in(seeds[15], 71), 0)
    residual = draw_residual(jax.random.fold_in(seeds[15], 71), 0)
    out_proj = centred(seeds[4], (QUERY_HEADS * HEAD_WIDTH, D), (QUERY_HEADS * HEAD_WIDTH) ** -0.5, 0.09375, ((0, 32),))
    norm_gain = jnp.clip(1.0 + 0.15 * jax.random.normal(seeds[5], (D,), jnp.float32), 0.25, 1.75).astype(jnp.bfloat16)
    router = draw_router(jax.random.fold_in(seeds[15], 71), 0)
    w_gate = centred(seeds[7], (EXPERTS, D, FF), D ** -0.5, 0.125, ((0, 128), (2, 4)))
    w_up = centred(seeds[8], (EXPERTS, D, FF), D ** -0.5, 0.125, ((0, 128), (2, 4)))
    w_down = centred(seeds[9], (EXPERTS, FF, D), FF ** -0.5, 0.21875, ((0, 128), (1, 4)))
    head_vec = draw_head_vec(jax.random.fold_in(seeds[15], 71), 0)
    routes_keys = jax.random.split(jax.random.fold_in(seeds[11], 1), PACK_COUNT * STEPS // BLOCK)
    routes_turns = jax.random.permutation(jax.random.fold_in(seeds[11], 3), PACK_COUNT * STEPS // BLOCK)
    routes = jax.vmap(lambda own, number: assign_block(jax.random.fold_in(seeds[11], 2), own, number, BLOCK, EXPERTS, TOPK, CAP, 2))(routes_keys, routes_turns).reshape((PACK_COUNT, STEPS, TOPK))
    step_pos = draw_step_pos(jax.random.fold_in(seeds[15], 71), 0)
    labels = with_ends((jax.random.randint(seeds[13], (PACK_COUNT, STEPS), 0, 2) < 1).astype(jnp.int32), jax.random.fold_in(seeds[13], 1), 0, 1)
    trace_len = jax.vmap(lambda own: ragged(own, TRACES, PACK_TOKENS, PACK_TOKENS // 4, 2))(jax.random.split(seeds[14], PACK_COUNT)).reshape((PACK_COUNT, TRACES)).astype(jnp.int32)
    return dict(keys=keys, values=values, queries=queries, residual=residual, out_proj=out_proj, norm_gain=norm_gain, router=router, w_gate=w_gate, w_up=w_up, w_down=w_down, head_vec=head_vec, routes=routes, step_pos=step_pos, labels=labels, trace_len=trace_len)


MASKED = -1e+30
EPSILON = 1e-06

def rms_scale(stream):
    return lax.rsqrt(lax.optimization_barrier(jnp.mean(stream * stream, axis=-1, keepdims=True)) + EPSILON)

def attend(packed):
    pack_keys, pack_values, pack_queries, positions, lengths = packed
    trace_ends = jnp.cumsum(lengths)
    starts = lax.optimization_barrier(jnp.sum(jnp.where(trace_ends[None, :] <= positions[:, None], lengths[None, :], 0), axis=1))
    key_pos = jnp.arange(PACK_TOKENS, dtype=jnp.int32)
    allowed = (key_pos[None, :] <= positions[:, None]) & (key_pos[None, :] >= starts[:, None])
    query_groups = QUERY_HEADS // KEY_VALUE_HEADS
    results = []
    for head_cluster in range(KEY_VALUE_HEADS):
        query_part = pack_queries[:, head_cluster * query_groups * HEAD_WIDTH:(head_cluster + 1) * query_groups * HEAD_WIDTH].reshape(STEPS * query_groups, HEAD_WIDTH)
        key_part = pack_keys[:, head_cluster * HEAD_WIDTH:(head_cluster + 1) * HEAD_WIDTH]
        value_part = pack_values[:, head_cluster * HEAD_WIDTH:(head_cluster + 1) * HEAD_WIDTH]
        scores = jnp.dot(query_part, key_part.T, preferred_element_type=jnp.float32) * HEAD_WIDTH ** (-0.5)
        scores = scores.reshape(STEPS, query_groups, PACK_TOKENS)
        scores = jnp.where(allowed[:, None, :], scores, MASKED)
        peak_score = lax.optimization_barrier(jnp.max(scores, axis=2, keepdims=True))
        complete_weight_rows = jnp.where(allowed[:, None, :], jnp.exp(scores - peak_score), 0.0)
        totals = lax.optimization_barrier(jnp.sum(complete_weight_rows, axis=2, keepdims=True))
        weighted = jnp.dot(complete_weight_rows.astype(jnp.bfloat16).reshape(STEPS * query_groups, PACK_TOKENS), value_part, preferred_element_type=jnp.float32).reshape(STEPS, query_groups, HEAD_WIDTH)
        results.append(weighted / totals)
    return jnp.stack(results, axis=1).reshape(STEPS, QUERY_HEADS * HEAD_WIDTH).astype(jnp.bfloat16)

def head_logit(final, head_vec):
    return lax.optimization_barrier(jnp.sum(final * rms_scale(final) * head_vec.astype(jnp.float32)[None, :], axis=1))

def reference(keys, values, queries, residual, out_proj, norm_gain, router, w_gate, w_up, w_down, head_vec, routes, step_pos, labels, trace_len):
    attn = lax.map(attend, (keys, values, queries, step_pos, trace_len))
    row_count = PACK_COUNT * STEPS
    mixed = jnp.dot(attn.reshape(row_count, QUERY_HEADS * HEAD_WIDTH), out_proj, preferred_element_type=jnp.float32)
    stream = residual.reshape(row_count, D).astype(jnp.float32) + mixed
    normed = (stream * rms_scale(stream) * norm_gain.astype(jnp.float32)[None, :]).astype(jnp.bfloat16)
    logits = jnp.dot(normed, router, preferred_element_type=jnp.float32)
    route_ids = routes.reshape(row_count, TOPK)
    chosen = (route_ids[:, :, None] == jnp.arange(EXPERTS, dtype=jnp.int32)[None, None, :]).astype(jnp.float32)
    picked = lax.optimization_barrier(jnp.sum(chosen * logits[:, None, :], axis=2))
    gate_weight = jax.nn.softmax(picked, axis=-1)
    block_count = row_count // BLOCK
    flat_routes = route_ids.reshape(block_count, BLOCK * TOPK)
    onehot = (flat_routes[:, :, None] == jnp.arange(EXPERTS, dtype=jnp.int32)[None, None, :]).astype(jnp.int32)
    order_rank = lax.optimization_barrier(jnp.sum((jnp.cumsum(onehot, axis=1) - 1) * onehot, axis=2))
    slot_index = (jnp.arange(block_count, dtype=jnp.int32)[:, None] * CAP + order_rank).reshape(-1).astype(jnp.int32)
    destination = route_ids.reshape(-1)
    row_of = jnp.repeat(jnp.arange(row_count, dtype=jnp.int32), TOPK)
    span = block_count * CAP
    row_buffer = jnp.zeros((EXPERTS, span, D), jnp.bfloat16).at[destination, slot_index].set(normed[row_of])

    def expert_forward(packed):
        rows_e, gate_e, up_e, down_e = packed
        gate_act = jnp.dot(rows_e, gate_e, preferred_element_type=jnp.float32)
        up_act = jnp.dot(rows_e, up_e, preferred_element_type=jnp.float32)
        hidden = (jax.nn.silu(gate_act) * up_act).astype(jnp.bfloat16)
        return (hidden, jnp.dot(hidden, down_e, preferred_element_type=jnp.float32))
    hidden, out_buffer = lax.map(expert_forward, (row_buffer, w_gate, w_up, w_down))
    expert_out = out_buffer[destination, slot_index].reshape(row_count, TOPK, D)
    expert_mix = lax.optimization_barrier(jnp.sum(gate_weight[:, :, None] * expert_out, axis=1))
    final = stream + expert_mix
    reward, pull = jax.vjp(lambda value: head_logit(value, head_vec), final)
    target = labels.reshape(row_count).astype(jnp.float32)
    loss = jnp.sum(jax.nn.softplus(reward) - target * reward)
    logit_grad = jax.nn.sigmoid(reward) - target
    final_grad, = pull(logit_grad)
    d_mix = final_grad.astype(jnp.bfloat16)
    route_dot = lax.optimization_barrier(jnp.sum(d_mix.astype(jnp.float32)[:, None, :] * expert_out, axis=2))
    pick_grad = gate_weight * (route_dot - lax.optimization_barrier(jnp.sum(gate_weight * route_dot, axis=1, keepdims=True)))
    d_logits = lax.optimization_barrier(jnp.sum(chosen * pick_grad[:, :, None], axis=1))
    grad_router = jnp.dot(normed.astype(jnp.float32).T, d_logits, precision=lax.Precision.HIGHEST).astype(jnp.bfloat16)
    d_out = (gate_weight[:, :, None] * d_mix.astype(jnp.float32)[:, None, :]).astype(jnp.bfloat16).reshape(row_count * TOPK, D)
    grad_buffer = jnp.zeros((EXPERTS, span, D), jnp.bfloat16).at[destination, slot_index].set(d_out)

    def down_grad(packed):
        hidden_e, grads_e = packed
        return jnp.dot(hidden_e.T, grads_e, preferred_element_type=jnp.float32).astype(jnp.bfloat16)
    grad_down = lax.map(down_grad, (hidden, grad_buffer))
    return (loss, grad_down, grad_router)
```

```python
import jax
import jax.numpy as jnp
from jax import lax
from jax.sharding import Mesh
from jax.sharding import PartitionSpec as P

QUERY_HEADS = 32
KEY_VALUE_HEADS = 4
HEAD_WIDTH = 128
DP_EXPERT = ("dp", "expert_0", "expert_1")
DP_SEQ = ("dp", "seq_0", "seq_1")
SEQ = ("seq_0", "seq_1")
DP_SEQ_EXPERT = ("dp", "seq_0", "seq_1", "expert_0", "expert_1")
EXPERT = ("expert_0", "expert_1")
ROWS = DP_SEQ_EXPERT


MASKED = -1e30
EPSILON = 1e-06


def joined_along(blocks, dim):
    blocks = jnp.moveaxis(blocks, 0, dim)
    lengths = blocks.shape
    return blocks.reshape(*lengths[:dim], lengths[dim] * lengths[dim + 1], *lengths[dim + 2 :])


def from_everyone(array, axis):
    copies = jnp.broadcast_to(array, (lax.axis_size(axis), *array.shape))
    return lax.all_to_all(copies, axis, split_axis=0, concat_axis=0, tiled=True)


def gather_directly(array, axis, dim):
    return joined_along(from_everyone(array, axis), dim)


def in_blocks(array, dim, count):
    lengths = array.shape
    blocks = array.reshape(*lengths[:dim], count, lengths[dim] // count, *lengths[dim + 1 :])
    return jnp.moveaxis(blocks, dim, 0)


def sent_and_summed(array, axis, dim):
    count = lax.axis_size(axis)
    blocks = lax.all_to_all(in_blocks(array, dim, count), axis, 0, 0, tiled=True)
    return jnp.sum(blocks.astype(jnp.float32), axis=0)


def rms_scale(stream):
    return lax.rsqrt(jnp.mean(stream * stream, axis=-1, keepdims=True) + EPSILON)


def head_logit(final, head_vec):
    return jnp.sum(final * rms_scale(final) * head_vec.astype(jnp.float32)[None, :], axis=1)


def split_pair(value):
    high = value.astype(jnp.bfloat16)
    low = (value - high.astype(jnp.float32)).astype(jnp.bfloat16)
    return high, low


def join_pair(high, low):
    return high.astype(jnp.float32) + low.astype(jnp.float32)


def merge_heads(weighted_r, totals_r, peak_r):
    peak_all = jnp.max(peak_r, axis=0)
    factor = jnp.exp(peak_r - peak_all[None])
    weighted_sum = jnp.sum(weighted_r * factor[..., None], axis=0)
    totals_sum = jnp.sum(totals_r * factor, axis=0)
    merged = weighted_sum / totals_sum[..., None]
    return merged.reshape(merged.shape[0], -1).astype(jnp.bfloat16)


def shards(
    keys,
    values,
    queries,
    residual,
    out_proj,
    norm_gain,
    router,
    w_gate,
    w_up,
    w_down,
    head_vec,
    routes,
    step_pos,
    labels,
    trace_len,
):
    block_routes = lax.all_gather(routes[0], DP_EXPERT, axis=0)
    block_routes = block_routes.reshape(
        lax.axis_size("dp"), lax.axis_size(EXPERT), *routes.shape[1:]
    )
    routes_all = jnp.swapaxes(block_routes, 1, 2).reshape(-1, routes.shape[2])
    count_of_keys = keys.shape[1]
    query_groups = QUERY_HEADS // KEY_VALUE_HEADS
    query_all = gather_directly(queries, DP_SEQ, 1)[0]
    positions = step_pos[0]
    number_of_steps = positions.shape[0]
    lengths = trace_len[0]
    trace_ends = jnp.cumsum(lengths)
    starts = jnp.sum(
        jnp.where(trace_ends[None, :] <= positions[:, None], lengths[None, :], 0), axis=1
    )
    key_pos = lax.axis_index(DP_SEQ) * count_of_keys + jnp.arange(count_of_keys, dtype=jnp.int32)
    allowed = (key_pos[None, :] <= positions[:, None]) & (key_pos[None, :] >= starts[:, None])
    score_list = []
    for head_cluster in range(KEY_VALUE_HEADS):
        query_part = query_all[
            :,
            head_cluster
            * query_groups
            * HEAD_WIDTH : (head_cluster + 1)
            * query_groups
            * HEAD_WIDTH,
        ].reshape(number_of_steps * query_groups, HEAD_WIDTH)
        key_part = keys[0, :, head_cluster * HEAD_WIDTH : (head_cluster + 1) * HEAD_WIDTH]
        score_part = lax.dot_general(
            query_part, key_part, (((1,), (1,)), ((), ())), preferred_element_type=jnp.float32
        ) * HEAD_WIDTH ** (-0.5)
        score_part = score_part.reshape(number_of_steps, query_groups, count_of_keys)
        score_list.append(jnp.where(allowed[:, None, :], score_part, MASKED))
    scores = jnp.stack(score_list, axis=1).reshape(number_of_steps, QUERY_HEADS, count_of_keys)
    local_peak = jnp.max(scores, axis=2)
    heads_of_values = values[0].reshape(count_of_keys, KEY_VALUE_HEADS, HEAD_WIDTH)
    complete_weight_rows = jnp.where(
        allowed[:, None, :], jnp.exp(scores - local_peak[:, :, None]), 0.0
    )
    totals = jnp.sum(complete_weight_rows, axis=2)
    reduced_weight_rows = complete_weight_rows.astype(jnp.bfloat16).reshape(
        number_of_steps, KEY_VALUE_HEADS, query_groups, count_of_keys
    )
    weighted = jnp.einsum(
        "skgt,tkd->skgd", reduced_weight_rows, heads_of_values, preferred_element_type=jnp.float32
    ).reshape(number_of_steps, QUERY_HEADS, HEAD_WIDTH)
    totals_hi, totals_lo = split_pair(totals)
    peak_hi, peak_lo = split_pair(local_peak)
    packed = jnp.concatenate(
        [
            weighted.astype(jnp.bfloat16),
            totals_hi[..., None],
            totals_lo[..., None],
            peak_hi[..., None],
            peak_lo[..., None],
        ],
        axis=-1,
    )
    arrived = lax.all_to_all(
        packed.reshape(1, *packed.shape), DP_SEQ, split_axis=2, concat_axis=0, tiled=True
    )
    attn = merge_heads(
        arrived[..., :HEAD_WIDTH].astype(jnp.float32),
        join_pair(arrived[..., HEAD_WIDTH], arrived[..., HEAD_WIDTH + 1]),
        join_pair(arrived[..., HEAD_WIDTH + 2], arrived[..., HEAD_WIDTH + 3]),
    )
    mixed = sent_and_summed(
        jnp.dot(attn, out_proj, preferred_element_type=jnp.float32).astype(jnp.bfloat16), DP_SEQ, 0
    )
    stream = residual[0].astype(jnp.float32) + mixed
    normed = (stream * rms_scale(stream) * norm_gain.astype(jnp.float32)[None, :]).astype(
        jnp.bfloat16
    )
    normed_all = lax.all_gather(normed, ROWS, axis=0, tiled=True)
    experts = router.shape[1]
    logits = jnp.dot(normed_all, router, preferred_element_type=jnp.float32)
    chosen = (routes_all[:, :, None] == jnp.arange(experts, dtype=jnp.int32)[None, None, :]).astype(
        jnp.float32
    )
    picked = jnp.sum(chosen * logits[:, None, :], axis=2)
    gate_weight = jax.nn.softmax(picked, axis=-1)
    mine = routes_all == lax.axis_index(DP_EXPERT)
    coef = jnp.sum(jnp.where(mine, gate_weight, 0.0), axis=1)
    gate_act = jnp.dot(normed_all, w_gate[0], preferred_element_type=jnp.float32)
    up_act = jnp.dot(normed_all, w_up[0], preferred_element_type=jnp.float32)
    hidden = (jax.nn.silu(gate_act) * up_act).astype(jnp.bfloat16)
    expert_out = jnp.dot(hidden, w_down[0], preferred_element_type=jnp.float32)
    expert_mix = lax.psum_scatter(
        coef[:, None] * expert_out, ROWS, scatter_dimension=0, tiled=True
    )
    final = stream + expert_mix
    reward, pull = jax.vjp(lambda value: head_logit(value, head_vec), final)
    target = labels[0].astype(jnp.float32)
    loss_term = jax.nn.softplus(reward) - target * reward
    logit_grad = jax.nn.sigmoid(reward) - target
    (final_grad,) = pull(logit_grad)
    d_mix = final_grad.astype(jnp.bfloat16)
    d_mix_all = lax.all_gather(d_mix, ROWS, axis=0, tiled=True)
    d_mix_wide = d_mix_all.astype(jnp.float32)
    contract_rows = (((0,), (0,)), ((), ()))
    d_out = (coef[:, None] * d_mix_wide).astype(jnp.bfloat16)
    grad_down = lax.dot_general(hidden, d_out, contract_rows, preferred_element_type=jnp.float32)
    grad_down = grad_down.astype(jnp.bfloat16).reshape((1,) + grad_down.shape)
    share_dot = jnp.sum(d_mix_wide * expert_out, axis=1)
    row_count = normed_all.shape[0]
    own_row = jnp.arange(row_count, dtype=jnp.int32) == lax.axis_index(ROWS)
    payload = jnp.concatenate(
        [
            jnp.where(mine, share_dot[:, None], 0.0),
            jnp.where(own_row, loss_term, 0.0)[:, None],
        ],
        axis=1,
    )
    summed = lax.psum(payload, ROWS)
    route_dot = summed[:, :-1]
    loss = jnp.sum(summed[:, -1])
    pick_grad = gate_weight * (route_dot - jnp.sum(gate_weight * route_dot, axis=1, keepdims=True))
    d_logits = jnp.sum(chosen * pick_grad[:, :, None], axis=1)
    router_grad_all = lax.dot_general(
        normed_all.astype(jnp.float32), d_logits, contract_rows, precision=lax.Precision.HIGHEST
    )
    own_rows = router_grad_all.shape[0] // lax.axis_size(DP_SEQ_EXPERT)
    grad_router = lax.dynamic_slice_in_dim(
        router_grad_all, lax.axis_index(DP_SEQ_EXPERT) * own_rows, own_rows, axis=0
    ).astype(jnp.bfloat16)
    return (loss, grad_down, grad_router)


def solution(mesh):
    finer = Mesh(
        mesh.devices.reshape(mesh.shape["dp"], 2, 2, 4, 4),
        ("dp", "seq_0", "seq_1", "expert_0", "expert_1"),
    )
    return jax.shard_map(
        shards,
        mesh=finer,
        in_specs=(
            P(EXPERT, DP_SEQ, None),
            P(EXPERT, DP_SEQ, None),
            P(EXPERT, DP_SEQ, None),
            P(EXPERT, DP_SEQ, None),
            P(DP_SEQ, None),
            P(),
            P(),
            P(DP_EXPERT, None, SEQ),
            P(DP_EXPERT, None, SEQ),
            P(DP_EXPERT, SEQ, None),
            P(),
            P(EXPERT, "dp", None),
            P(EXPERT, None),
            P(EXPERT, DP_SEQ),
            P(EXPERT, None),
        ),
        out_specs=(P(), P(DP_EXPERT, SEQ, None), P(DP_SEQ_EXPERT, None)),
        check_vma=False,
    )
```

```python
import jax
import jax.numpy as jnp
from jax import lax
from jax.sharding import Mesh
from jax.sharding import PartitionSpec as P

QUERY_HEADS = 32
KEY_VALUE_HEADS = 4
HEAD_WIDTH = 128
DP_EXPERT = ("dp", "expert_0", "expert_1")
DP_SEQ = ("dp", "seq_0", "seq_1")
SEQ = ("seq_0", "seq_1")
DP_SEQ_EXPERT = ("dp", "seq_0", "seq_1", "expert_0", "expert_1")
EXPERT = ("expert_0", "expert_1")


MASKED = -1e30
EPSILON = 1e-06


def joined_along(blocks, dim):
    blocks = jnp.moveaxis(blocks, 0, dim)
    lengths = blocks.shape
    return blocks.reshape(*lengths[:dim], lengths[dim] * lengths[dim + 1], *lengths[dim + 2 :])


def from_everyone(array, axis):
    copies = jnp.broadcast_to(array, (lax.axis_size(axis), *array.shape))
    return lax.all_to_all(copies, axis, split_axis=0, concat_axis=0, tiled=True)


def gather_directly(array, axis, dim):
    return joined_along(from_everyone(array, axis), dim)


def in_blocks(array, dim, count):
    lengths = array.shape
    blocks = array.reshape(*lengths[:dim], count, lengths[dim] // count, *lengths[dim + 1 :])
    return jnp.moveaxis(blocks, dim, 0)


def sent_and_summed(array, axis, dim):
    count = lax.axis_size(axis)
    blocks = lax.all_to_all(in_blocks(array, dim, count), axis, 0, 0, tiled=True)
    return jnp.sum(blocks.astype(jnp.float32), axis=0)


def rms_scale(stream):
    return lax.rsqrt(jnp.mean(stream * stream, axis=-1, keepdims=True) + EPSILON)


def head_logit(final, head_vec):
    return jnp.sum(final * rms_scale(final) * head_vec.astype(jnp.float32)[None, :], axis=1)


def move_rows(buffer):
    return lax.all_to_all(buffer, DP_EXPERT, split_axis=0, concat_axis=0, tiled=True)


def split_pair(value):
    high = value.astype(jnp.bfloat16)
    low = (value - high.astype(jnp.float32)).astype(jnp.bfloat16)
    return high, low


def join_pair(high, low):
    return high.astype(jnp.float32) + low.astype(jnp.float32)


def merge_heads(weighted_r, totals_r, peak_r):
    peak_all = jnp.max(peak_r, axis=0)
    factor = jnp.exp(peak_r - peak_all[None])
    weighted_sum = jnp.sum(weighted_r * factor[..., None], axis=0)
    totals_sum = jnp.sum(totals_r * factor, axis=0)
    merged = weighted_sum / totals_sum[..., None]
    return merged.reshape(merged.shape[0], -1).astype(jnp.bfloat16)


def shards(
    keys,
    values,
    queries,
    residual,
    out_proj,
    norm_gain,
    router,
    w_gate,
    w_up,
    w_down,
    head_vec,
    routes,
    step_pos,
    labels,
    trace_len,
):
    count_of_keys = keys.shape[1]
    query_groups = QUERY_HEADS // KEY_VALUE_HEADS
    query_all = gather_directly(queries, DP_SEQ, 1)[0]
    positions = step_pos[0]
    number_of_steps = positions.shape[0]
    lengths = trace_len[0]
    trace_ends = jnp.cumsum(lengths)
    starts = jnp.sum(
        jnp.where(trace_ends[None, :] <= positions[:, None], lengths[None, :], 0), axis=1
    )
    key_pos = lax.axis_index(DP_SEQ) * count_of_keys + jnp.arange(count_of_keys, dtype=jnp.int32)
    allowed = (key_pos[None, :] <= positions[:, None]) & (key_pos[None, :] >= starts[:, None])
    score_list = []
    for head_cluster in range(KEY_VALUE_HEADS):
        query_part = query_all[
            :,
            head_cluster
            * query_groups
            * HEAD_WIDTH : (head_cluster + 1)
            * query_groups
            * HEAD_WIDTH,
        ].reshape(number_of_steps * query_groups, HEAD_WIDTH)
        key_part = keys[0, :, head_cluster * HEAD_WIDTH : (head_cluster + 1) * HEAD_WIDTH]
        score_part = lax.dot_general(
            query_part, key_part, (((1,), (1,)), ((), ())), preferred_element_type=jnp.float32
        ) * HEAD_WIDTH ** (-0.5)
        score_part = score_part.reshape(number_of_steps, query_groups, count_of_keys)
        score_list.append(jnp.where(allowed[:, None, :], score_part, MASKED))
    scores = jnp.stack(score_list, axis=1).reshape(number_of_steps, QUERY_HEADS, count_of_keys)
    local_peak = jnp.max(scores, axis=2)
    heads_of_values = values[0].reshape(count_of_keys, KEY_VALUE_HEADS, HEAD_WIDTH)
    complete_weight_rows = jnp.where(
        allowed[:, None, :], jnp.exp(scores - local_peak[:, :, None]), 0.0
    )
    totals = jnp.sum(complete_weight_rows, axis=2)
    reduced_weight_rows = complete_weight_rows.astype(jnp.bfloat16).reshape(
        number_of_steps, KEY_VALUE_HEADS, query_groups, count_of_keys
    )
    weighted = jnp.einsum(
        "skgt,tkd->skgd", reduced_weight_rows, heads_of_values, preferred_element_type=jnp.float32
    ).reshape(number_of_steps, QUERY_HEADS, HEAD_WIDTH)
    totals_hi, totals_lo = split_pair(totals)
    peak_hi, peak_lo = split_pair(local_peak)
    packed = jnp.concatenate(
        [
            weighted.astype(jnp.bfloat16),
            totals_hi[..., None],
            totals_lo[..., None],
            peak_hi[..., None],
            peak_lo[..., None],
        ],
        axis=-1,
    )
    arrived = lax.all_to_all(
        packed.reshape(1, *packed.shape), DP_SEQ, split_axis=2, concat_axis=0, tiled=True
    )
    attn = merge_heads(
        arrived[..., :HEAD_WIDTH].astype(jnp.float32),
        join_pair(arrived[..., HEAD_WIDTH], arrived[..., HEAD_WIDTH + 1]),
        join_pair(arrived[..., HEAD_WIDTH + 2], arrived[..., HEAD_WIDTH + 3]),
    )
    mixed = sent_and_summed(
        jnp.dot(attn, out_proj, preferred_element_type=jnp.float32).astype(jnp.bfloat16), DP_SEQ, 0
    )
    stream = residual[0].astype(jnp.float32) + mixed
    normed = (stream * rms_scale(stream) * norm_gain.astype(jnp.float32)[None, :]).astype(
        jnp.bfloat16
    )
    block_normed = gather_directly(normed, SEQ, 0)
    block_rows = routes.shape[1]
    topk = routes.shape[2]
    experts = router.shape[1]
    width = block_normed.shape[1]
    capacity = min(block_rows, 2 * ((block_rows * topk + experts - 1) // experts))
    route_ids = routes[0]
    logits = jnp.dot(block_normed, router, preferred_element_type=jnp.float32)
    chosen = (route_ids[:, :, None] == jnp.arange(experts, dtype=jnp.int32)[None, None, :]).astype(
        jnp.float32
    )
    picked = jnp.sum(chosen * logits[:, None, :], axis=2)
    gate_weight = jax.nn.softmax(picked, axis=-1)
    flat_routes = route_ids.reshape(-1)
    onehot = (flat_routes[:, None] == jnp.arange(experts, dtype=jnp.int32)[None, :]).astype(
        jnp.int32
    )
    order_rank = jnp.sum((jnp.cumsum(onehot, axis=0) - 1) * onehot, axis=1)
    slot_index = flat_routes * capacity + order_rank
    slot_map = (
        slot_index[:, None] == jnp.arange(experts * capacity, dtype=jnp.int32)[None, :]
    ).astype(jnp.float32)
    place_map = slot_map.reshape(block_rows, topk, experts * capacity)
    row_map = jnp.sum(place_map, axis=1)
    weight_map = jnp.sum(gate_weight[:, :, None] * place_map, axis=1)
    contract_rows = (((0,), (0,)), ((), ()))
    send_rows = lax.dot_general(
        row_map.astype(jnp.bfloat16),
        block_normed,
        contract_rows,
        preferred_element_type=jnp.float32,
    ).astype(jnp.bfloat16)
    arrived = move_rows(send_rows.reshape(experts, capacity, width))
    arrived = arrived.reshape(experts * capacity, width)
    gate_act = jnp.dot(arrived, w_gate[0], preferred_element_type=jnp.float32)
    up_act = jnp.dot(arrived, w_up[0], preferred_element_type=jnp.float32)
    hidden = (jax.nn.silu(gate_act) * up_act).astype(jnp.bfloat16)
    partial_value = jnp.dot(hidden, w_down[0], preferred_element_type=jnp.float32)
    returned = move_rows(partial_value.astype(jnp.bfloat16).reshape(experts, capacity, width))
    returned = returned.reshape(experts * capacity, width)
    route_part = jnp.dot(
        slot_map.astype(jnp.bfloat16), returned, preferred_element_type=jnp.float32
    ).astype(jnp.bfloat16)
    shares = lax.all_to_all(
        route_part.reshape(block_rows, topk, width), SEQ, split_axis=0, concat_axis=0, tiled=True
    )
    expert_out = jnp.sum(shares.astype(jnp.float32), axis=0)
    me = lax.axis_index(SEQ)
    own_gate = lax.dynamic_index_in_dim(gate_weight, me, 0, keepdims=False)
    expert_mix = jnp.sum(own_gate[:, None] * expert_out, axis=0, keepdims=True)
    final = stream + expert_mix
    reward, pull = jax.vjp(lambda value: head_logit(value, head_vec), final)
    target = labels[0].astype(jnp.float32)
    loss_term = jnp.sum(jax.nn.softplus(reward) - target * reward)
    logit_grad = jax.nn.sigmoid(reward) - target
    (final_grad,) = pull(logit_grad)
    d_mix = final_grad.astype(jnp.bfloat16)
    route_dot = jnp.sum(d_mix.astype(jnp.float32) * expert_out, axis=1)
    pick_grad = own_gate * (route_dot - jnp.sum(own_gate * route_dot))
    pick_hi, pick_lo = split_pair(pick_grad)
    loss_hi, loss_lo = split_pair(loss_term)
    side = jnp.concatenate([pick_hi, pick_lo, loss_hi[None], loss_lo[None]])
    side = jnp.pad(side, (0, width - side.shape[0]))
    bundle = jnp.stack([d_mix[0], side])
    block_bundle = from_everyone(bundle, SEQ)
    block_grads = block_bundle[:, 0, :]
    block_pick = join_pair(block_bundle[:, 1, :topk], block_bundle[:, 1, topk : 2 * topk])
    block_loss = jnp.sum(join_pair(block_bundle[:, 1, 2 * topk], block_bundle[:, 1, 2 * topk + 1]))
    d_out = lax.dot_general(
        weight_map, block_grads.astype(jnp.float32), contract_rows, precision=lax.Precision.HIGHEST
    ).astype(jnp.bfloat16)
    d_logits = jnp.sum(chosen * block_pick[:, :, None], axis=1)
    columns = block_normed.reshape(
        block_rows, lax.axis_size("dp"), lax.axis_size(SEQ), lax.axis_size(EXPERT), -1
    )
    my_columns = lax.dynamic_index_in_dim(columns, me, 2, keepdims=False).reshape(block_rows, -1)
    router_part = lax.dot_general(
        my_columns.astype(jnp.float32), d_logits, contract_rows, precision=lax.Precision.HIGHEST
    )
    owners = lax.axis_size(DP_EXPERT)
    router_chunks = router_part.reshape(owners, -1)
    chunk = router_chunks.shape[1]
    router_hi, router_lo = split_pair(router_chunks)
    block_hi, block_lo = split_pair(block_loss)
    extra_row = jnp.concatenate(
        [
            router_hi,
            router_lo,
            jnp.broadcast_to(block_hi, (owners, 1)),
            jnp.broadcast_to(block_lo, (owners, 1)),
            jnp.zeros((owners, width - 2 * chunk - 2), jnp.bfloat16),
        ],
        axis=1,
    )
    sent = jnp.concatenate([d_out.reshape(experts, capacity, width), extra_row[:, None, :]], axis=1)
    got = move_rows(sent)
    grads_arrived = got[:, :capacity].reshape(experts * capacity, width)
    grad_down = lax.dot_general(
        hidden, grads_arrived, contract_rows, preferred_element_type=jnp.float32
    )
    grad_down = grad_down.astype(jnp.bfloat16).reshape((1,) + grad_down.shape)
    router_sum = jnp.sum(join_pair(got[:, capacity, :chunk], got[:, capacity, chunk : 2 * chunk]), axis=0)
    grad_router = router_sum.reshape(-1, experts).astype(jnp.bfloat16)
    loss = jnp.sum(join_pair(got[:, capacity, 2 * chunk], got[:, capacity, 2 * chunk + 1]))
    return (loss, grad_down, grad_router)


def solution(mesh):
    finer = Mesh(
        mesh.devices.reshape(mesh.shape["dp"], 2, 2, 4, 4),
        ("dp", "seq_0", "seq_1", "expert_0", "expert_1"),
    )
    return jax.shard_map(
        shards,
        mesh=finer,
        in_specs=(
            P(EXPERT, DP_SEQ, None),
            P(EXPERT, DP_SEQ, None),
            P(EXPERT, DP_SEQ, None),
            P(EXPERT, DP_SEQ, None),
            P(DP_SEQ, None),
            P(),
            P(),
            P(DP_EXPERT, None, SEQ),
            P(DP_EXPERT, None, SEQ),
            P(DP_EXPERT, SEQ, None),
            P(),
            P(EXPERT, "dp", None),
            P(EXPERT, None),
            P(EXPERT, DP_SEQ),
            P(EXPERT, None),
        ),
        out_specs=(P(), P(DP_EXPERT, SEQ, None), P(DP_SEQ_EXPERT, None)),
        check_vma=False,
    )
```

```python
import jax
import jax.numpy as jnp
from jax import lax
from jax.sharding import Mesh
from jax.sharding import PartitionSpec as P

QUERY_HEADS = 32
KEY_VALUE_HEADS = 4
HEAD_WIDTH = 128
DP_EXPERT = ("dp", "expert_0", "expert_1")
DP_SEQ = ("dp", "seq_0", "seq_1")
SEQ = ("seq_0", "seq_1")
DP_SEQ_EXPERT = ("dp", "seq_0", "seq_1", "expert_0", "expert_1")
EXPERT = ("expert_0", "expert_1")


MASKED = -1e30
EPSILON = 1e-06


def joined_along(blocks, dim):
    blocks = jnp.moveaxis(blocks, 0, dim)
    lengths = blocks.shape
    return blocks.reshape(*lengths[:dim], lengths[dim] * lengths[dim + 1], *lengths[dim + 2 :])


def from_everyone(array, axis):
    copies = jnp.broadcast_to(array, (lax.axis_size(axis), *array.shape))
    return lax.all_to_all(copies, axis, split_axis=0, concat_axis=0, tiled=True)


def gather_directly(array, axis, dim):
    return joined_along(from_everyone(array, axis), dim)


def in_blocks(array, dim, count):
    lengths = array.shape
    blocks = array.reshape(*lengths[:dim], count, lengths[dim] // count, *lengths[dim + 1 :])
    return jnp.moveaxis(blocks, dim, 0)


def sent_and_summed(array, axis, dim):
    count = lax.axis_size(axis)
    blocks = lax.all_to_all(in_blocks(array, dim, count), axis, 0, 0, tiled=True)
    return jnp.sum(blocks.astype(jnp.float32), axis=0)


def rms_scale(stream):
    return lax.rsqrt(jnp.mean(stream * stream, axis=-1, keepdims=True) + EPSILON)


def head_logit(final, head_vec):
    return jnp.sum(final * rms_scale(final) * head_vec.astype(jnp.float32)[None, :], axis=1)


def across_group(buffer):
    return lax.all_to_all(buffer, EXPERT, split_axis=0, concat_axis=0, tiled=True)


def taken_together(array, axis):
    return from_everyone(array, axis).sum(axis=0)


def split_pair(value):
    high = value.astype(jnp.bfloat16)
    low = (value - high.astype(jnp.float32)).astype(jnp.bfloat16)
    return high, low


def join_pair(high, low):
    return high.astype(jnp.float32) + low.astype(jnp.float32)


def merge_heads(weighted_r, totals_r, peak_r):
    peak_all = jnp.max(peak_r, axis=0)
    factor = jnp.exp(peak_r - peak_all[None])
    weighted_sum = jnp.sum(weighted_r * factor[..., None], axis=0)
    totals_sum = jnp.sum(totals_r * factor, axis=0)
    merged = weighted_sum / totals_sum[..., None]
    return merged.reshape(merged.shape[0], -1).astype(jnp.bfloat16)


def shards(
    keys,
    values,
    queries,
    residual,
    out_proj,
    norm_gain,
    router,
    w_gate,
    w_up,
    w_down,
    head_vec,
    routes,
    step_pos,
    labels,
    trace_len,
):
    pack_routes = gather_directly(routes[0], "dp", 0)
    count_of_keys = keys.shape[1]
    query_groups = QUERY_HEADS // KEY_VALUE_HEADS
    query_all = gather_directly(queries, DP_SEQ, 1)[0]
    positions = step_pos[0]
    number_of_steps = positions.shape[0]
    lengths = trace_len[0]
    trace_ends = jnp.cumsum(lengths)
    starts = jnp.sum(
        jnp.where(trace_ends[None, :] <= positions[:, None], lengths[None, :], 0), axis=1
    )
    key_pos = lax.axis_index(DP_SEQ) * count_of_keys + jnp.arange(count_of_keys, dtype=jnp.int32)
    allowed = (key_pos[None, :] <= positions[:, None]) & (key_pos[None, :] >= starts[:, None])
    score_list = []
    for head_cluster in range(KEY_VALUE_HEADS):
        query_part = query_all[
            :,
            head_cluster
            * query_groups
            * HEAD_WIDTH : (head_cluster + 1)
            * query_groups
            * HEAD_WIDTH,
        ].reshape(number_of_steps * query_groups, HEAD_WIDTH)
        key_part = keys[0, :, head_cluster * HEAD_WIDTH : (head_cluster + 1) * HEAD_WIDTH]
        score_part = lax.dot_general(
            query_part, key_part, (((1,), (1,)), ((), ())), preferred_element_type=jnp.float32
        ) * HEAD_WIDTH ** (-0.5)
        score_part = score_part.reshape(number_of_steps, query_groups, count_of_keys)
        score_list.append(jnp.where(allowed[:, None, :], score_part, MASKED))
    scores = jnp.stack(score_list, axis=1).reshape(number_of_steps, QUERY_HEADS, count_of_keys)
    local_peak = jnp.max(scores, axis=2)
    heads_of_values = values[0].reshape(count_of_keys, KEY_VALUE_HEADS, HEAD_WIDTH)
    complete_weight_rows = jnp.where(
        allowed[:, None, :], jnp.exp(scores - local_peak[:, :, None]), 0.0
    )
    totals = jnp.sum(complete_weight_rows, axis=2)
    reduced_weight_rows = complete_weight_rows.astype(jnp.bfloat16).reshape(
        number_of_steps, KEY_VALUE_HEADS, query_groups, count_of_keys
    )
    weighted = jnp.einsum(
        "skgt,tkd->skgd", reduced_weight_rows, heads_of_values, preferred_element_type=jnp.float32
    ).reshape(number_of_steps, QUERY_HEADS, HEAD_WIDTH)
    totals_hi, totals_lo = split_pair(totals)
    peak_hi, peak_lo = split_pair(local_peak)
    packed = jnp.concatenate(
        [
            weighted.astype(jnp.bfloat16),
            totals_hi[..., None],
            totals_lo[..., None],
            peak_hi[..., None],
            peak_lo[..., None],
        ],
        axis=-1,
    )
    arrived = lax.all_to_all(
        packed.reshape(1, *packed.shape), DP_SEQ, split_axis=2, concat_axis=0, tiled=True
    )
    attn = merge_heads(
        arrived[..., :HEAD_WIDTH].astype(jnp.float32),
        join_pair(arrived[..., HEAD_WIDTH], arrived[..., HEAD_WIDTH + 1]),
        join_pair(arrived[..., HEAD_WIDTH + 2], arrived[..., HEAD_WIDTH + 3]),
    )
    mixed = sent_and_summed(
        jnp.dot(attn, out_proj, preferred_element_type=jnp.float32).astype(jnp.bfloat16), DP_SEQ, 0
    )
    stream = residual[0].astype(jnp.float32) + mixed
    normed = (stream * rms_scale(stream) * norm_gain.astype(jnp.float32)[None, :]).astype(
        jnp.bfloat16
    )
    pack_normed = gather_directly(normed, DP_SEQ, 0)
    rows = pack_normed.shape[0]
    width = pack_normed.shape[1]
    block_rows = routes.shape[1]
    topk = routes.shape[2]
    experts = router.shape[1]
    blocks = rows // block_rows
    group_size = lax.axis_size(EXPERT)
    capacity = min(block_rows, 2 * ((block_rows * topk + experts - 1) // experts))
    per_source = blocks * capacity
    slots = group_size * per_source
    logits = jnp.dot(pack_normed, router, preferred_element_type=jnp.float32)
    chosen = (pack_routes[:, :, None] == jnp.arange(experts, dtype=jnp.int32)[None, None, :]).astype(
        jnp.float32
    )
    picked = jnp.sum(chosen * logits[:, None, :], axis=2)
    gate_weight = jax.nn.softmax(picked, axis=-1)
    row_has = jnp.sum(chosen, axis=1).reshape(blocks, block_rows, experts)
    earlier = (jnp.cumsum(row_has, axis=1) - row_has).reshape(rows, experts)
    rank = jnp.sum(chosen * earlier[:, None, :], axis=2).astype(jnp.int32)
    block_of = (jnp.arange(rows, dtype=jnp.int32) // block_rows)[:, None]
    in_group = (pack_routes // group_size) == lax.axis_index("dp")
    dest_slot = (pack_routes % group_size) * per_source + block_of * capacity + rank
    slot_map = (
        (dest_slot[:, :, None] == jnp.arange(slots, dtype=jnp.int32)[None, None, :])
        & in_group[:, :, None]
    ).astype(jnp.float32)
    row_map = jnp.sum(slot_map, axis=1)
    weight_map = jnp.sum(gate_weight[:, :, None] * slot_map, axis=1)
    contract_rows = (((0,), (0,)), ((), ()))
    send_rows = lax.dot_general(
        row_map.astype(jnp.bfloat16), pack_normed, contract_rows, preferred_element_type=jnp.float32
    ).astype(jnp.bfloat16)
    arrived = across_group(send_rows.reshape(group_size, per_source, width)).reshape(slots, width)
    gate_act = jnp.dot(arrived, w_gate[0], preferred_element_type=jnp.float32)
    up_act = jnp.dot(arrived, w_up[0], preferred_element_type=jnp.float32)
    hidden = (jax.nn.silu(gate_act) * up_act).astype(jnp.bfloat16)
    partial_value = jnp.dot(hidden, w_down[0], preferred_element_type=jnp.float32)
    returned = across_group(
        partial_value.astype(jnp.bfloat16).reshape(group_size, per_source, width)
    ).reshape(slots, width)
    group_mix = lax.dot_general(
        weight_map,
        returned.astype(jnp.float32),
        (((1,), (0,)), ((), ())),
        precision=lax.Precision.HIGHEST,
    )
    expert_mix = sent_and_summed(group_mix.astype(jnp.bfloat16), DP_SEQ, 0)
    final = stream + expert_mix
    reward, pull = jax.vjp(lambda value: head_logit(value, head_vec), final)
    target = labels[0].astype(jnp.float32)
    loss_term = jnp.sum(jax.nn.softplus(reward) - target * reward)
    logit_grad = jax.nn.sigmoid(reward) - target
    (final_grad,) = pull(logit_grad)
    d_mix = final_grad.astype(jnp.bfloat16)
    pack_grads = gather_directly(d_mix, DP_SEQ, 0)
    d_out = lax.dot_general(
        weight_map, pack_grads.astype(jnp.float32), contract_rows, precision=lax.Precision.HIGHEST
    ).astype(jnp.bfloat16)
    grads_arrived = across_group(d_out.reshape(group_size, per_source, width)).reshape(slots, width)
    grad_down = lax.dot_general(
        hidden, grads_arrived, contract_rows, preferred_element_type=jnp.float32
    )
    grad_down = grad_down.astype(jnp.bfloat16).reshape((1,) + grad_down.shape)
    slot_grads = lax.dot_general(
        row_map.astype(jnp.bfloat16), pack_grads, contract_rows, preferred_element_type=jnp.float32
    )
    slot_dots = jnp.sum(slot_grads * returned.astype(jnp.float32), axis=1)
    dots_part = jnp.sum(slot_map * slot_dots[None, None, :], axis=2)
    own_row = jnp.arange(rows, dtype=jnp.int32) == lax.axis_index(DP_SEQ)
    payload = jnp.concatenate([dots_part, jnp.where(own_row, loss_term, 0.0)[:, None]], axis=1)
    summed = taken_together(payload, DP_SEQ)
    route_dot = summed[:, :topk]
    pack_loss = jnp.sum(summed[:, topk])
    pick_grad = gate_weight * (route_dot - jnp.sum(gate_weight * route_dot, axis=1, keepdims=True))
    d_logits = jnp.sum(chosen * pick_grad[:, :, None], axis=1)
    columns = pack_normed.reshape(rows, lax.axis_size(DP_SEQ), -1)
    my_columns = lax.dynamic_index_in_dim(columns, lax.axis_index(DP_SEQ), 1, keepdims=False)
    router_part = lax.dot_general(
        my_columns.astype(jnp.float32), d_logits, contract_rows, precision=lax.Precision.HIGHEST
    )
    router_part = router_part.reshape(group_size, -1)
    chunk = router_part.shape[1]
    sent = jnp.concatenate(
        [router_part, jnp.broadcast_to(pack_loss, (group_size, 1))], axis=1
    )
    got = across_group(sent)
    grad_router = jnp.sum(got[:, :chunk], axis=0).reshape(-1, experts).astype(jnp.bfloat16)
    loss = jnp.sum(got[:, chunk])
    return (loss, grad_down, grad_router)


def solution(mesh):
    finer = Mesh(
        mesh.devices.reshape(mesh.shape["dp"], 2, 2, 4, 4),
        ("dp", "seq_0", "seq_1", "expert_0", "expert_1"),
    )
    return jax.shard_map(
        shards,
        mesh=finer,
        in_specs=(
            P(EXPERT, DP_SEQ, None),
            P(EXPERT, DP_SEQ, None),
            P(EXPERT, DP_SEQ, None),
            P(EXPERT, DP_SEQ, None),
            P(DP_SEQ, None),
            P(),
            P(),
            P(DP_EXPERT, None, SEQ),
            P(DP_EXPERT, None, SEQ),
            P(DP_EXPERT, SEQ, None),
            P(),
            P(EXPERT, "dp", None),
            P(EXPERT, None),
            P(EXPERT, DP_SEQ),
            P(EXPERT, None),
        ),
        out_specs=(P(), P(DP_EXPERT, SEQ, None), P(DP_SEQ_EXPERT, None)),
        check_vma=False,
    )
```

```python
import jax
import jax.numpy as jnp
from jax import lax
from jax.sharding import Mesh
from jax.sharding import PartitionSpec as P

QUERY_HEADS = 32
KEY_VALUE_HEADS = 4
HEAD_WIDTH = 128
DP_EXPERT = ("dp", "expert_0", "expert_1")
DP_SEQ = ("dp", "seq_0", "seq_1")
SEQ = ("seq_0", "seq_1")
DP_SEQ_EXPERT = ("dp", "seq_0", "seq_1", "expert_0", "expert_1")
EXPERT = ("expert_0", "expert_1")


MASKED = -1e30
EPSILON = 1e-06


def joined_along(blocks, dim):
    blocks = jnp.moveaxis(blocks, 0, dim)
    lengths = blocks.shape
    return blocks.reshape(*lengths[:dim], lengths[dim] * lengths[dim + 1], *lengths[dim + 2 :])


def from_everyone(array, axis):
    copies = jnp.broadcast_to(array, (lax.axis_size(axis), *array.shape))
    return lax.all_to_all(copies, axis, split_axis=0, concat_axis=0, tiled=True)


def gather_directly(array, axis, dim):
    return joined_along(from_everyone(array, axis), dim)


def in_blocks(array, dim, count):
    lengths = array.shape
    blocks = array.reshape(*lengths[:dim], count, lengths[dim] // count, *lengths[dim + 1 :])
    return jnp.moveaxis(blocks, dim, 0)


def sent_and_summed(array, axis, dim):
    count = lax.axis_size(axis)
    blocks = lax.all_to_all(in_blocks(array, dim, count), axis, 0, 0, tiled=True)
    return jnp.sum(blocks.astype(jnp.float32), axis=0)


def rms_scale(stream):
    return lax.rsqrt(jnp.mean(stream * stream, axis=-1, keepdims=True) + EPSILON)


def head_logit(final, head_vec):
    return jnp.sum(final * rms_scale(final) * head_vec.astype(jnp.float32)[None, :], axis=1)


def across_group(buffer):
    return lax.all_to_all(buffer, EXPERT, split_axis=0, concat_axis=0, tiled=True)


def taken_together(array, axis):
    return from_everyone(array, axis).sum(axis=0)


def split_pair(value):
    high = value.astype(jnp.bfloat16)
    low = (value - high.astype(jnp.float32)).astype(jnp.bfloat16)
    return high, low


def join_pair(high, low):
    return high.astype(jnp.float32) + low.astype(jnp.float32)


def merge_heads(weighted_r, totals_r, peak_r):
    peak_all = jnp.max(peak_r, axis=0)
    factor = jnp.exp(peak_r - peak_all[None])
    weighted_sum = jnp.sum(weighted_r * factor[..., None], axis=0)
    totals_sum = jnp.sum(totals_r * factor, axis=0)
    merged = weighted_sum / totals_sum[..., None]
    return merged.reshape(merged.shape[0], -1).astype(jnp.bfloat16)


def shards(
    keys,
    values,
    queries,
    residual,
    out_proj,
    norm_gain,
    router,
    w_gate,
    w_up,
    w_down,
    head_vec,
    routes,
    step_pos,
    labels,
    trace_len,
):
    count_of_keys = keys.shape[1]
    query_groups = QUERY_HEADS // KEY_VALUE_HEADS
    query_width = queries.shape[2]
    own_routes = lax.dynamic_index_in_dim(routes[0], lax.axis_index(SEQ), 0, keepdims=False)
    query_row = jnp.concatenate(
        [
            queries[0],
            own_routes.astype(jnp.bfloat16)[None, :],
            jnp.zeros((1, HEAD_WIDTH - own_routes.shape[0]), jnp.bfloat16),
        ],
        axis=1,
    )
    query_rows = gather_directly(query_row, DP_SEQ, 0)
    query_all = query_rows[:, :query_width]
    pack_routes = query_rows[:, query_width : query_width + routes.shape[2]].astype(jnp.int32)
    positions = step_pos[0]
    number_of_steps = positions.shape[0]
    lengths = trace_len[0]
    trace_ends = jnp.cumsum(lengths)
    starts = jnp.sum(
        jnp.where(trace_ends[None, :] <= positions[:, None], lengths[None, :], 0), axis=1
    )
    key_pos = lax.axis_index(DP_SEQ) * count_of_keys + jnp.arange(count_of_keys, dtype=jnp.int32)
    allowed = (key_pos[None, :] <= positions[:, None]) & (key_pos[None, :] >= starts[:, None])
    score_list = []
    for head_cluster in range(KEY_VALUE_HEADS):
        query_part = query_all[
            :,
            head_cluster
            * query_groups
            * HEAD_WIDTH : (head_cluster + 1)
            * query_groups
            * HEAD_WIDTH,
        ].reshape(number_of_steps * query_groups, HEAD_WIDTH)
        key_part = keys[0, :, head_cluster * HEAD_WIDTH : (head_cluster + 1) * HEAD_WIDTH]
        score_part = lax.dot_general(
            query_part, key_part, (((1,), (1,)), ((), ())), preferred_element_type=jnp.float32
        ) * HEAD_WIDTH ** (-0.5)
        score_part = score_part.reshape(number_of_steps, query_groups, count_of_keys)
        score_list.append(jnp.where(allowed[:, None, :], score_part, MASKED))
    scores = jnp.stack(score_list, axis=1).reshape(number_of_steps, QUERY_HEADS, count_of_keys)
    local_peak = jnp.max(scores, axis=2)
    heads_of_values = values[0].reshape(count_of_keys, KEY_VALUE_HEADS, HEAD_WIDTH)
    complete_weight_rows = jnp.where(
        allowed[:, None, :], jnp.exp(scores - local_peak[:, :, None]), 0.0
    )
    totals = jnp.sum(complete_weight_rows, axis=2)
    reduced_weight_rows = complete_weight_rows.astype(jnp.bfloat16).reshape(
        number_of_steps, KEY_VALUE_HEADS, query_groups, count_of_keys
    )
    weighted = jnp.einsum(
        "skgt,tkd->skgd", reduced_weight_rows, heads_of_values, preferred_element_type=jnp.float32
    ).reshape(number_of_steps, QUERY_HEADS, HEAD_WIDTH)
    totals_hi, totals_lo = split_pair(totals)
    peak_hi, peak_lo = split_pair(local_peak)
    packed = jnp.concatenate(
        [
            weighted.astype(jnp.bfloat16),
            totals_hi[..., None],
            totals_lo[..., None],
            peak_hi[..., None],
            peak_lo[..., None],
        ],
        axis=-1,
    )
    arrived = lax.all_to_all(
        packed.reshape(1, *packed.shape), DP_SEQ, split_axis=2, concat_axis=0, tiled=True
    )
    attn = merge_heads(
        arrived[..., :HEAD_WIDTH].astype(jnp.float32),
        join_pair(arrived[..., HEAD_WIDTH], arrived[..., HEAD_WIDTH + 1]),
        join_pair(arrived[..., HEAD_WIDTH + 2], arrived[..., HEAD_WIDTH + 3]),
    )
    mixed = sent_and_summed(
        jnp.dot(attn, out_proj, preferred_element_type=jnp.float32).astype(jnp.bfloat16), DP_SEQ, 0
    )
    stream = residual[0].astype(jnp.float32) + mixed
    normed = (stream * rms_scale(stream) * norm_gain.astype(jnp.float32)[None, :]).astype(
        jnp.bfloat16
    )
    pack_normed = gather_directly(normed, DP_SEQ, 0)
    rows = pack_normed.shape[0]
    width = pack_normed.shape[1]
    block_rows = routes.shape[1]
    topk = routes.shape[2]
    experts = router.shape[1]
    blocks = rows // block_rows
    group_size = lax.axis_size(EXPERT)
    capacity = min(block_rows, 2 * ((block_rows * topk + experts - 1) // experts))
    per_source = blocks * capacity
    slots = group_size * per_source
    logits = jnp.dot(pack_normed, router, preferred_element_type=jnp.float32)
    chosen = (pack_routes[:, :, None] == jnp.arange(experts, dtype=jnp.int32)[None, None, :]).astype(
        jnp.float32
    )
    picked = jnp.sum(chosen * logits[:, None, :], axis=2)
    gate_weight = jax.nn.softmax(picked, axis=-1)
    row_has = jnp.sum(chosen, axis=1).reshape(blocks, block_rows, experts)
    earlier = (jnp.cumsum(row_has, axis=1) - row_has).reshape(rows, experts)
    rank = jnp.sum(chosen * earlier[:, None, :], axis=2).astype(jnp.int32)
    block_of = (jnp.arange(rows, dtype=jnp.int32) // block_rows)[:, None]
    in_group = (pack_routes // group_size) == lax.axis_index("dp")
    dest_slot = (pack_routes % group_size) * per_source + block_of * capacity + rank
    slot_map = (
        (dest_slot[:, :, None] == jnp.arange(slots, dtype=jnp.int32)[None, None, :])
        & in_group[:, :, None]
    ).astype(jnp.float32)
    row_map = jnp.sum(slot_map, axis=1)
    weight_map = jnp.sum(gate_weight[:, :, None] * slot_map, axis=1)
    contract_rows = (((0,), (0,)), ((), ()))
    send_rows = lax.dot_general(
        row_map.astype(jnp.bfloat16), pack_normed, contract_rows, preferred_element_type=jnp.float32
    ).astype(jnp.bfloat16)
    arrived = across_group(send_rows.reshape(group_size, per_source, width)).reshape(slots, width)
    gate_act = jnp.dot(arrived, w_gate[0], preferred_element_type=jnp.float32)
    up_act = jnp.dot(arrived, w_up[0], preferred_element_type=jnp.float32)
    hidden = (jax.nn.silu(gate_act) * up_act).astype(jnp.bfloat16)
    partial_value = jnp.dot(hidden, w_down[0], preferred_element_type=jnp.float32)
    returned = across_group(
        partial_value.astype(jnp.bfloat16).reshape(group_size, per_source, width)
    ).reshape(slots, width)
    group_mix = lax.dot_general(
        weight_map,
        returned.astype(jnp.float32),
        (((1,), (0,)), ((), ())),
        precision=lax.Precision.HIGHEST,
    )
    expert_mix = sent_and_summed(group_mix.astype(jnp.bfloat16), DP_SEQ, 0)
    final = stream + expert_mix
    reward, pull = jax.vjp(lambda value: head_logit(value, head_vec), final)
    target = labels[0].astype(jnp.float32)
    loss_term = jnp.sum(jax.nn.softplus(reward) - target * reward)
    logit_grad = jax.nn.sigmoid(reward) - target
    (final_grad,) = pull(logit_grad)
    d_mix = final_grad.astype(jnp.bfloat16)
    pack_grads = gather_directly(d_mix, DP_SEQ, 0)
    d_out = lax.dot_general(
        weight_map, pack_grads.astype(jnp.float32), contract_rows, precision=lax.Precision.HIGHEST
    ).astype(jnp.bfloat16)
    slot_grads = lax.dot_general(
        row_map.astype(jnp.bfloat16), pack_grads, contract_rows, preferred_element_type=jnp.float32
    )
    slot_dots = jnp.sum(slot_grads * returned.astype(jnp.float32), axis=1)
    dots_part = jnp.sum(slot_map * slot_dots[None, None, :], axis=2)
    own_row = jnp.arange(rows, dtype=jnp.int32) == lax.axis_index(DP_SEQ)
    payload = jnp.concatenate([dots_part, jnp.where(own_row, loss_term, 0.0)[:, None]], axis=1)
    summed = taken_together(payload, DP_SEQ)
    route_dot = summed[:, :topk]
    pack_loss = jnp.sum(summed[:, topk])
    pick_grad = gate_weight * (route_dot - jnp.sum(gate_weight * route_dot, axis=1, keepdims=True))
    d_logits = jnp.sum(chosen * pick_grad[:, :, None], axis=1)
    columns = pack_normed.reshape(rows, lax.axis_size(DP_SEQ), -1)
    my_columns = lax.dynamic_index_in_dim(columns, lax.axis_index(DP_SEQ), 1, keepdims=False)
    router_part = lax.dot_general(
        my_columns.astype(jnp.float32), d_logits, contract_rows, precision=lax.Precision.HIGHEST
    )
    router_part = router_part.reshape(group_size, -1)
    chunk = router_part.shape[1]
    router_hi, router_lo = split_pair(router_part)
    loss_hi, loss_lo = split_pair(pack_loss)
    extra_row = jnp.concatenate(
        [
            router_hi,
            router_lo,
            jnp.broadcast_to(loss_hi, (group_size, 1)),
            jnp.broadcast_to(loss_lo, (group_size, 1)),
            jnp.zeros((group_size, width - 2 * chunk - 2), jnp.bfloat16),
        ],
        axis=1,
    )
    sent = jnp.concatenate(
        [d_out.reshape(group_size, per_source, width), extra_row[:, None, :]], axis=1
    )
    got = across_group(sent)
    grads_arrived = got[:, :per_source].reshape(slots, width)
    grad_down = lax.dot_general(
        hidden, grads_arrived, contract_rows, preferred_element_type=jnp.float32
    )
    grad_down = grad_down.astype(jnp.bfloat16).reshape((1,) + grad_down.shape)
    tail = got[:, per_source]
    grad_router = jnp.sum(join_pair(tail[:, :chunk], tail[:, chunk : 2 * chunk]), axis=0)
    grad_router = grad_router.reshape(-1, experts).astype(jnp.bfloat16)
    loss = jnp.sum(join_pair(tail[:, 2 * chunk], tail[:, 2 * chunk + 1]))
    return (loss, grad_down, grad_router)


def solution(mesh):
    finer = Mesh(
        mesh.devices.reshape(mesh.shape["dp"], 2, 2, 4, 4),
        ("dp", "seq_0", "seq_1", "expert_0", "expert_1"),
    )
    return jax.shard_map(
        shards,
        mesh=finer,
        in_specs=(
            P(EXPERT, DP_SEQ, None),
            P(EXPERT, DP_SEQ, None),
            P(EXPERT, DP_SEQ, None),
            P(EXPERT, DP_SEQ, None),
            P(DP_SEQ, None),
            P(),
            P(),
            P(DP_EXPERT, None, SEQ),
            P(DP_EXPERT, None, SEQ),
            P(DP_EXPERT, SEQ, None),
            P(),
            P(EXPERT, "dp", None),
            P(EXPERT, None),
            P(EXPERT, DP_SEQ),
            P(EXPERT, None),
        ),
        out_specs=(P(), P(DP_EXPERT, SEQ, None), P(DP_SEQ_EXPERT, None)),
        check_vma=False,
    )
```

```python
import jax
import jax.numpy as jnp
from jax import lax
from jax.sharding import Mesh
from jax.sharding import PartitionSpec as P

QUERY_HEADS = 32
KEY_VALUE_HEADS = 4
HEAD_WIDTH = 128
DP_EXPERT = ("dp", "expert_0", "expert_1")
DP_SEQ = ("dp", "seq_0", "seq_1")
SEQ = ("seq_0", "seq_1")
DP_SEQ_EXPERT = ("dp", "seq_0", "seq_1", "expert_0", "expert_1")
EXPERT = ("expert_0", "expert_1")


MASKED = -1e30
EPSILON = 1e-06


def joined_along(blocks, dim):
    blocks = jnp.moveaxis(blocks, 0, dim)
    lengths = blocks.shape
    return blocks.reshape(*lengths[:dim], lengths[dim] * lengths[dim + 1], *lengths[dim + 2 :])


def from_everyone(array, axis):
    copies = jnp.broadcast_to(array, (lax.axis_size(axis), *array.shape))
    return lax.all_to_all(copies, axis, split_axis=0, concat_axis=0, tiled=True)


def gather_directly(array, axis, dim):
    return joined_along(from_everyone(array, axis), dim)


def in_blocks(array, dim, count):
    lengths = array.shape
    blocks = array.reshape(*lengths[:dim], count, lengths[dim] // count, *lengths[dim + 1 :])
    return jnp.moveaxis(blocks, dim, 0)


def sent_and_summed(array, axis, dim):
    count = lax.axis_size(axis)
    blocks = lax.all_to_all(in_blocks(array, dim, count), axis, 0, 0, tiled=True)
    return jnp.sum(blocks.astype(jnp.float32), axis=0)


def rms_scale(stream):
    return lax.rsqrt(jnp.mean(stream * stream, axis=-1, keepdims=True) + EPSILON)


def head_logit(final, head_vec):
    return jnp.sum(final * rms_scale(final) * head_vec.astype(jnp.float32)[None, :], axis=1)


def across_group(buffer):
    return lax.all_to_all(buffer, EXPERT, split_axis=0, concat_axis=0, tiled=True)


def taken_together(array, axis):
    return from_everyone(array, axis).sum(axis=0)


def split_pair(value):
    high = value.astype(jnp.bfloat16)
    low = (value - high.astype(jnp.float32)).astype(jnp.bfloat16)
    return high, low


def join_pair(high, low):
    return high.astype(jnp.float32) + low.astype(jnp.float32)


def merge_heads(weighted_r, totals_r, peak_r):
    peak_all = jnp.max(peak_r, axis=0)
    factor = jnp.exp(peak_r - peak_all[None])
    weighted_sum = jnp.sum(weighted_r * factor[..., None], axis=0)
    totals_sum = jnp.sum(totals_r * factor, axis=0)
    merged = weighted_sum / totals_sum[..., None]
    return merged.reshape(merged.shape[0], -1).astype(jnp.bfloat16)


def shards(
    keys,
    values,
    queries,
    residual,
    out_proj,
    norm_gain,
    router,
    w_gate,
    w_up,
    w_down,
    head_vec,
    routes,
    step_pos,
    labels,
    trace_len,
):
    count_of_keys = keys.shape[1]
    query_groups = QUERY_HEADS // KEY_VALUE_HEADS
    query_width = queries.shape[2]
    own_routes = lax.dynamic_index_in_dim(routes[0], lax.axis_index(SEQ), 0, keepdims=False)
    query_row = jnp.concatenate(
        [
            queries[0],
            own_routes.astype(jnp.bfloat16)[None, :],
            jnp.zeros((1, HEAD_WIDTH - own_routes.shape[0]), jnp.bfloat16),
        ],
        axis=1,
    )
    query_rows = gather_directly(query_row, DP_SEQ, 0)
    query_all = query_rows[:, :query_width]
    pack_routes = query_rows[:, query_width : query_width + routes.shape[2]].astype(jnp.int32)
    positions = step_pos[0]
    number_of_steps = positions.shape[0]
    lengths = trace_len[0]
    trace_ends = jnp.cumsum(lengths)
    starts = jnp.sum(
        jnp.where(trace_ends[None, :] <= positions[:, None], lengths[None, :], 0), axis=1
    )
    key_pos = lax.axis_index(DP_SEQ) * count_of_keys + jnp.arange(count_of_keys, dtype=jnp.int32)
    allowed = (key_pos[None, :] <= positions[:, None]) & (key_pos[None, :] >= starts[:, None])
    score_list = []
    for head_cluster in range(KEY_VALUE_HEADS):
        query_part = query_all[
            :,
            head_cluster
            * query_groups
            * HEAD_WIDTH : (head_cluster + 1)
            * query_groups
            * HEAD_WIDTH,
        ].reshape(number_of_steps * query_groups, HEAD_WIDTH)
        key_part = keys[0, :, head_cluster * HEAD_WIDTH : (head_cluster + 1) * HEAD_WIDTH]
        score_part = lax.dot_general(
            query_part, key_part, (((1,), (1,)), ((), ())), preferred_element_type=jnp.float32
        ) * HEAD_WIDTH ** (-0.5)
        score_part = score_part.reshape(number_of_steps, query_groups, count_of_keys)
        score_list.append(jnp.where(allowed[:, None, :], score_part, MASKED))
    scores = jnp.stack(score_list, axis=1).reshape(number_of_steps, QUERY_HEADS, count_of_keys)
    local_peak = jnp.max(scores, axis=2)
    heads_of_values = values[0].reshape(count_of_keys, KEY_VALUE_HEADS, HEAD_WIDTH)
    complete_weight_rows = jnp.where(
        allowed[:, None, :], jnp.exp(scores - local_peak[:, :, None]), 0.0
    )
    totals = jnp.sum(complete_weight_rows, axis=2)
    reduced_weight_rows = complete_weight_rows.astype(jnp.bfloat16).reshape(
        number_of_steps, KEY_VALUE_HEADS, query_groups, count_of_keys
    )
    weighted = jnp.einsum(
        "skgt,tkd->skgd", reduced_weight_rows, heads_of_values, preferred_element_type=jnp.float32
    ).reshape(number_of_steps, QUERY_HEADS, HEAD_WIDTH)
    totals_hi, totals_lo = split_pair(totals)
    peak_hi, peak_lo = split_pair(local_peak)
    stats = jnp.stack([totals_hi, totals_lo, peak_hi, peak_lo], axis=-1)
    stats = jnp.swapaxes(stats, 0, 1).reshape(1, QUERY_HEADS, -1)
    packed = jnp.concatenate([weighted.astype(jnp.bfloat16), stats], axis=0)
    arrived = lax.all_to_all(
        packed.reshape(1, *packed.shape), DP_SEQ, split_axis=2, concat_axis=0, tiled=True
    )
    got_stats = arrived[:, number_of_steps].reshape(arrived.shape[0], number_of_steps, 1, 4)
    attn = merge_heads(
        arrived[:, :number_of_steps].astype(jnp.float32),
        join_pair(got_stats[..., 0], got_stats[..., 1]),
        join_pair(got_stats[..., 2], got_stats[..., 3]),
    )
    mixed = sent_and_summed(
        jnp.dot(attn, out_proj, preferred_element_type=jnp.float32).astype(jnp.bfloat16), DP_SEQ, 0
    )
    stream = residual[0].astype(jnp.float32) + mixed
    normed = (stream * rms_scale(stream) * norm_gain.astype(jnp.float32)[None, :]).astype(
        jnp.bfloat16
    )
    pack_normed = gather_directly(normed, DP_SEQ, 0)
    rows = pack_normed.shape[0]
    width = pack_normed.shape[1]
    block_rows = routes.shape[1]
    topk = routes.shape[2]
    experts = router.shape[1]
    blocks = rows // block_rows
    group_size = lax.axis_size(EXPERT)
    capacity = min(block_rows, 2 * ((block_rows * topk + experts - 1) // experts))
    per_source = blocks * capacity
    slots = group_size * per_source
    logits = jnp.dot(pack_normed, router, preferred_element_type=jnp.float32)
    chosen = (pack_routes[:, :, None] == jnp.arange(experts, dtype=jnp.int32)[None, None, :]).astype(
        jnp.float32
    )
    picked = jnp.sum(chosen * logits[:, None, :], axis=2)
    gate_weight = jax.nn.softmax(picked, axis=-1)
    row_has = jnp.sum(chosen, axis=1).reshape(blocks, block_rows, experts)
    earlier = (jnp.cumsum(row_has, axis=1) - row_has).reshape(rows, experts)
    rank = jnp.sum(chosen * earlier[:, None, :], axis=2).astype(jnp.int32)
    block_of = (jnp.arange(rows, dtype=jnp.int32) // block_rows)[:, None]
    in_group = (pack_routes // group_size) == lax.axis_index("dp")
    dest_slot = (pack_routes % group_size) * per_source + block_of * capacity + rank
    slot_map = (
        (dest_slot[:, :, None] == jnp.arange(slots, dtype=jnp.int32)[None, None, :])
        & in_group[:, :, None]
    ).astype(jnp.float32)
    row_map = jnp.sum(slot_map, axis=1)
    weight_map = jnp.sum(gate_weight[:, :, None] * slot_map, axis=1)
    contract_rows = (((0,), (0,)), ((), ()))
    send_rows = lax.dot_general(
        row_map.astype(jnp.bfloat16), pack_normed, contract_rows, preferred_element_type=jnp.float32
    ).astype(jnp.bfloat16)
    arrived = across_group(send_rows.reshape(group_size, per_source, width)).reshape(slots, width)
    gate_act = jnp.dot(arrived, w_gate[0], preferred_element_type=jnp.float32)
    up_act = jnp.dot(arrived, w_up[0], preferred_element_type=jnp.float32)
    hidden = (jax.nn.silu(gate_act) * up_act).astype(jnp.bfloat16)
    partial_value = jnp.dot(hidden, w_down[0], preferred_element_type=jnp.float32)
    returned = across_group(
        partial_value.astype(jnp.bfloat16).reshape(group_size, per_source, width)
    ).reshape(slots, width)
    group_mix = lax.dot_general(
        weight_map,
        returned.astype(jnp.float32),
        (((1,), (0,)), ((), ())),
        precision=lax.Precision.HIGHEST,
    )
    expert_mix = sent_and_summed(group_mix.astype(jnp.bfloat16), DP_SEQ, 0)
    final = stream + expert_mix
    reward, pull = jax.vjp(lambda value: head_logit(value, head_vec), final)
    target = labels[0].astype(jnp.float32)
    loss_term = jnp.sum(jax.nn.softplus(reward) - target * reward)
    logit_grad = jax.nn.sigmoid(reward) - target
    (final_grad,) = pull(logit_grad)
    d_mix = final_grad.astype(jnp.bfloat16)
    pack_grads = gather_directly(d_mix, DP_SEQ, 0)
    d_out = lax.dot_general(
        weight_map, pack_grads.astype(jnp.float32), contract_rows, precision=lax.Precision.HIGHEST
    ).astype(jnp.bfloat16)
    slot_grads = lax.dot_general(
        row_map.astype(jnp.bfloat16), pack_grads, contract_rows, preferred_element_type=jnp.float32
    )
    slot_dots = jnp.sum(slot_grads * returned.astype(jnp.float32), axis=1)
    dots_part = jnp.sum(slot_map * slot_dots[None, None, :], axis=2)
    own_row = jnp.arange(rows, dtype=jnp.int32) == lax.axis_index(DP_SEQ)
    payload = jnp.concatenate([dots_part, jnp.where(own_row, loss_term, 0.0)[:, None]], axis=1)
    summed = taken_together(payload, DP_SEQ)
    route_dot = summed[:, :topk]
    pack_loss = jnp.sum(summed[:, topk])
    pick_grad = gate_weight * (route_dot - jnp.sum(gate_weight * route_dot, axis=1, keepdims=True))
    d_logits = jnp.sum(chosen * pick_grad[:, :, None], axis=1)
    columns = pack_normed.reshape(rows, lax.axis_size(DP_SEQ), -1)
    my_columns = lax.dynamic_index_in_dim(columns, lax.axis_index(DP_SEQ), 1, keepdims=False)
    router_part = lax.dot_general(
        my_columns.astype(jnp.float32), d_logits, contract_rows, precision=lax.Precision.HIGHEST
    )
    router_part = router_part.reshape(group_size, -1)
    chunk = router_part.shape[1]
    router_hi, router_lo = split_pair(router_part)
    loss_hi, loss_lo = split_pair(pack_loss)
    extra_row = jnp.concatenate(
        [
            router_hi,
            router_lo,
            jnp.broadcast_to(loss_hi, (group_size, 1)),
            jnp.broadcast_to(loss_lo, (group_size, 1)),
            jnp.zeros((group_size, width - 2 * chunk - 2), jnp.bfloat16),
        ],
        axis=1,
    )
    sent = jnp.concatenate(
        [d_out.reshape(group_size, per_source, width), extra_row[:, None, :]], axis=1
    )
    got = across_group(sent)
    grads_arrived = got[:, :per_source].reshape(slots, width)
    grad_down = lax.dot_general(
        hidden, grads_arrived, contract_rows, preferred_element_type=jnp.float32
    )
    grad_down = grad_down.astype(jnp.bfloat16).reshape((1,) + grad_down.shape)
    tail = got[:, per_source]
    grad_router = jnp.sum(join_pair(tail[:, :chunk], tail[:, chunk : 2 * chunk]), axis=0)
    grad_router = grad_router.reshape(-1, experts).astype(jnp.bfloat16)
    loss = jnp.sum(join_pair(tail[:, 2 * chunk], tail[:, 2 * chunk + 1]))
    return (loss, grad_down, grad_router)


def solution(mesh):
    finer = Mesh(
        mesh.devices.reshape(mesh.shape["dp"], 2, 2, 4, 4),
        ("dp", "seq_0", "seq_1", "expert_0", "expert_1"),
    )
    return jax.shard_map(
        shards,
        mesh=finer,
        in_specs=(
            P(EXPERT, DP_SEQ, None),
            P(EXPERT, DP_SEQ, None),
            P(EXPERT, DP_SEQ, None),
            P(EXPERT, DP_SEQ, None),
            P(DP_SEQ, None),
            P(),
            P(),
            P(DP_EXPERT, None, SEQ),
            P(DP_EXPERT, None, SEQ),
            P(DP_EXPERT, SEQ, None),
            P(),
            P(EXPERT, "dp", None),
            P(EXPERT, None),
            P(EXPERT, DP_SEQ),
            P(EXPERT, None),
        ),
        out_specs=(P(), P(DP_EXPERT, SEQ, None), P(DP_SEQ_EXPERT, None)),
        check_vma=False,
    )
```

```python
import jax
import jax.numpy as jnp
from jax import lax
from jax.sharding import Mesh
from jax.sharding import PartitionSpec as P

QUERY_HEADS = 32
KEY_VALUE_HEADS = 4
HEAD_WIDTH = 128
DP_EXPERT = ("dp", "expert_0", "expert_1")
DP_SEQ = ("dp", "seq_0", "seq_1")
SEQ = ("seq_0", "seq_1")
DP_SEQ_EXPERT = ("dp", "seq_0", "seq_1", "expert_0", "expert_1")
EXPERT = ("expert_0", "expert_1")


MASKED = -1e30
EPSILON = 1e-06


def joined_along(blocks, dim):
    blocks = jnp.moveaxis(blocks, 0, dim)
    lengths = blocks.shape
    return blocks.reshape(*lengths[:dim], lengths[dim] * lengths[dim + 1], *lengths[dim + 2 :])


def from_everyone(array, axis):
    copies = jnp.broadcast_to(array, (lax.axis_size(axis), *array.shape))
    return lax.all_to_all(copies, axis, split_axis=0, concat_axis=0, tiled=True)


def gather_directly(array, axis, dim):
    return joined_along(from_everyone(array, axis), dim)


def in_blocks(array, dim, count):
    lengths = array.shape
    blocks = array.reshape(*lengths[:dim], count, lengths[dim] // count, *lengths[dim + 1 :])
    return jnp.moveaxis(blocks, dim, 0)


def sent_and_summed(array, axis, dim):
    count = lax.axis_size(axis)
    blocks = lax.all_to_all(in_blocks(array, dim, count), axis, 0, 0, tiled=True)
    return jnp.sum(blocks.astype(jnp.float32), axis=0)


def rms_scale(stream):
    return lax.rsqrt(jnp.mean(stream * stream, axis=-1, keepdims=True) + EPSILON)


def head_logit(final, head_vec):
    return jnp.sum(final * rms_scale(final) * head_vec.astype(jnp.float32)[None, :], axis=1)


def across_group(buffer):
    return lax.all_to_all(buffer, EXPERT, split_axis=0, concat_axis=0, tiled=True)


def taken_together(array, axis):
    return from_everyone(array, axis).sum(axis=0)


def split_pair(value):
    high = value.astype(jnp.bfloat16)
    low = (value - high.astype(jnp.float32)).astype(jnp.bfloat16)
    return high, low


def join_pair(high, low):
    return high.astype(jnp.float32) + low.astype(jnp.float32)


def merge_heads(weighted_r, totals_r, peak_r):
    peak_all = jnp.max(peak_r, axis=0)
    factor = jnp.exp(peak_r - peak_all[None])
    weighted_sum = jnp.sum(weighted_r * factor[..., None], axis=0)
    totals_sum = jnp.sum(totals_r * factor, axis=0)
    merged = weighted_sum / totals_sum[..., None]
    return merged.reshape(merged.shape[0], -1).astype(jnp.bfloat16)


def shards(
    keys,
    values,
    queries,
    residual,
    out_proj,
    norm_gain,
    router,
    w_gate,
    w_up,
    w_down,
    head_vec,
    routes,
    step_pos,
    labels,
    trace_len,
):
    count_of_keys = keys.shape[1]
    query_groups = QUERY_HEADS // KEY_VALUE_HEADS
    query_width = queries.shape[2]
    own_routes = lax.dynamic_index_in_dim(routes[0], lax.axis_index(SEQ), 0, keepdims=False)
    query_row = jnp.concatenate(
        [
            queries[0],
            own_routes.astype(jnp.bfloat16)[None, :],
            jnp.zeros((1, HEAD_WIDTH - own_routes.shape[0]), jnp.bfloat16),
        ],
        axis=1,
    )
    query_rows = gather_directly(query_row, DP_SEQ, 0)
    query_all = query_rows[:, :query_width]
    pack_routes = query_rows[:, query_width : query_width + routes.shape[2]].astype(jnp.int32)
    positions = step_pos[0]
    number_of_steps = positions.shape[0]
    lengths = trace_len[0]
    trace_ends = jnp.cumsum(lengths)
    starts = jnp.sum(
        jnp.where(trace_ends[None, :] <= positions[:, None], lengths[None, :], 0), axis=1
    )
    key_pos = lax.axis_index(DP_SEQ) * count_of_keys + jnp.arange(count_of_keys, dtype=jnp.int32)
    allowed = (key_pos[None, :] <= positions[:, None]) & (key_pos[None, :] >= starts[:, None])
    score_list = []
    for head_cluster in range(KEY_VALUE_HEADS):
        query_part = query_all[
            :,
            head_cluster
            * query_groups
            * HEAD_WIDTH : (head_cluster + 1)
            * query_groups
            * HEAD_WIDTH,
        ].reshape(number_of_steps * query_groups, HEAD_WIDTH)
        key_part = keys[0, :, head_cluster * HEAD_WIDTH : (head_cluster + 1) * HEAD_WIDTH]
        score_part = lax.dot_general(
            query_part, key_part, (((1,), (1,)), ((), ())), preferred_element_type=jnp.float32
        ) * HEAD_WIDTH ** (-0.5)
        score_part = score_part.reshape(number_of_steps, query_groups, count_of_keys)
        score_list.append(jnp.where(allowed[:, None, :], score_part, MASKED))
    scores = jnp.stack(score_list, axis=1).reshape(number_of_steps, QUERY_HEADS, count_of_keys)
    local_peak = jnp.max(scores, axis=2)
    heads_of_values = values[0].reshape(count_of_keys, KEY_VALUE_HEADS, HEAD_WIDTH)
    complete_weight_rows = jnp.where(
        allowed[:, None, :], jnp.exp(scores - local_peak[:, :, None]), 0.0
    )
    totals = jnp.sum(complete_weight_rows, axis=2)
    reduced_weight_rows = complete_weight_rows.astype(jnp.bfloat16).reshape(
        number_of_steps, KEY_VALUE_HEADS, query_groups, count_of_keys
    )
    weighted = jnp.einsum(
        "skgt,tkd->skgd", reduced_weight_rows, heads_of_values, preferred_element_type=jnp.float32
    ).reshape(number_of_steps, QUERY_HEADS, HEAD_WIDTH)
    totals_hi, totals_lo = split_pair(totals)
    peak_hi, peak_lo = split_pair(local_peak)
    stats = jnp.stack([totals_hi, totals_lo, peak_hi, peak_lo], axis=-1)
    stats = jnp.swapaxes(stats, 0, 1).reshape(1, QUERY_HEADS, -1)
    packed = jnp.concatenate([weighted.astype(jnp.bfloat16), stats], axis=0)
    packed = jnp.swapaxes(packed, 0, 1).reshape(1, QUERY_HEADS, -1)
    arrived = lax.all_to_all(packed, DP_SEQ, split_axis=1, concat_axis=0, tiled=True)
    arrived = arrived.reshape(arrived.shape[0], number_of_steps + 1, 1, HEAD_WIDTH)
    got_stats = arrived[:, number_of_steps].reshape(arrived.shape[0], number_of_steps, 1, 4)
    attn = merge_heads(
        arrived[:, :number_of_steps].astype(jnp.float32),
        join_pair(got_stats[..., 0], got_stats[..., 1]),
        join_pair(got_stats[..., 2], got_stats[..., 3]),
    )
    mixed = sent_and_summed(
        jnp.dot(attn, out_proj, preferred_element_type=jnp.float32).astype(jnp.bfloat16), DP_SEQ, 0
    )
    stream = residual[0].astype(jnp.float32) + mixed
    normed = (stream * rms_scale(stream) * norm_gain.astype(jnp.float32)[None, :]).astype(
        jnp.bfloat16
    )
    pack_normed = gather_directly(normed, DP_SEQ, 0)
    rows = pack_normed.shape[0]
    width = pack_normed.shape[1]
    block_rows = routes.shape[1]
    topk = routes.shape[2]
    experts = router.shape[1]
    blocks = rows // block_rows
    group_size = lax.axis_size(EXPERT)
    capacity = min(block_rows, 2 * ((block_rows * topk + experts - 1) // experts))
    per_source = blocks * capacity
    slots = group_size * per_source
    logits = jnp.dot(pack_normed, router, preferred_element_type=jnp.float32)
    chosen = (pack_routes[:, :, None] == jnp.arange(experts, dtype=jnp.int32)[None, None, :]).astype(
        jnp.float32
    )
    picked = jnp.sum(chosen * logits[:, None, :], axis=2)
    gate_weight = jax.nn.softmax(picked, axis=-1)
    row_has = jnp.sum(chosen, axis=1).reshape(blocks, block_rows, experts)
    earlier = (jnp.cumsum(row_has, axis=1) - row_has).reshape(rows, experts)
    rank = jnp.sum(chosen * earlier[:, None, :], axis=2).astype(jnp.int32)
    block_of = (jnp.arange(rows, dtype=jnp.int32) // block_rows)[:, None]
    in_group = (pack_routes // group_size) == lax.axis_index("dp")
    dest_slot = (pack_routes % group_size) * per_source + block_of * capacity + rank
    slot_map = (
        (dest_slot[:, :, None] == jnp.arange(slots, dtype=jnp.int32)[None, None, :])
        & in_group[:, :, None]
    ).astype(jnp.float32)
    row_map = jnp.sum(slot_map, axis=1)
    weight_map = jnp.sum(gate_weight[:, :, None] * slot_map, axis=1)
    contract_rows = (((0,), (0,)), ((), ()))
    send_rows = lax.dot_general(
        row_map.astype(jnp.bfloat16), pack_normed, contract_rows, preferred_element_type=jnp.float32
    ).astype(jnp.bfloat16)
    arrived = across_group(send_rows.reshape(group_size, per_source, width)).reshape(slots, width)
    gate_act = jnp.dot(arrived, w_gate[0], preferred_element_type=jnp.float32)
    up_act = jnp.dot(arrived, w_up[0], preferred_element_type=jnp.float32)
    hidden = (jax.nn.silu(gate_act) * up_act).astype(jnp.bfloat16)
    partial_value = jnp.dot(hidden, w_down[0], preferred_element_type=jnp.float32)
    returned = across_group(
        partial_value.astype(jnp.bfloat16).reshape(group_size, per_source, width)
    ).reshape(slots, width)
    group_mix = lax.dot_general(
        weight_map,
        returned.astype(jnp.float32),
        (((1,), (0,)), ((), ())),
        precision=lax.Precision.HIGHEST,
    )
    expert_mix = sent_and_summed(group_mix.astype(jnp.bfloat16), DP_SEQ, 0)
    final = stream + expert_mix
    reward, pull = jax.vjp(lambda value: head_logit(value, head_vec), final)
    target = labels[0].astype(jnp.float32)
    loss_term = jnp.sum(jax.nn.softplus(reward) - target * reward)
    logit_grad = jax.nn.sigmoid(reward) - target
    (final_grad,) = pull(logit_grad)
    d_mix = final_grad.astype(jnp.bfloat16)
    pack_grads = gather_directly(d_mix, DP_SEQ, 0)
    d_out = lax.dot_general(
        weight_map, pack_grads.astype(jnp.float32), contract_rows, precision=lax.Precision.HIGHEST
    ).astype(jnp.bfloat16)
    slot_grads = lax.dot_general(
        row_map.astype(jnp.bfloat16), pack_grads, contract_rows, preferred_element_type=jnp.float32
    )
    slot_dots = jnp.sum(slot_grads * returned.astype(jnp.float32), axis=1)
    dots_part = jnp.sum(slot_map * slot_dots[None, None, :], axis=2)
    own_row = jnp.arange(rows, dtype=jnp.int32) == lax.axis_index(DP_SEQ)
    payload = jnp.concatenate([dots_part, jnp.where(own_row, loss_term, 0.0)[:, None]], axis=1)
    summed = taken_together(payload, DP_SEQ)
    route_dot = summed[:, :topk]
    pack_loss = jnp.sum(summed[:, topk])
    pick_grad = gate_weight * (route_dot - jnp.sum(gate_weight * route_dot, axis=1, keepdims=True))
    d_logits = jnp.sum(chosen * pick_grad[:, :, None], axis=1)
    columns = pack_normed.reshape(rows, lax.axis_size(DP_SEQ), -1)
    my_columns = lax.dynamic_index_in_dim(columns, lax.axis_index(DP_SEQ), 1, keepdims=False)
    router_part = lax.dot_general(
        my_columns.astype(jnp.float32), d_logits, contract_rows, precision=lax.Precision.HIGHEST
    )
    router_part = router_part.reshape(group_size, -1)
    chunk = router_part.shape[1]
    router_hi, router_lo = split_pair(router_part)
    loss_hi, loss_lo = split_pair(pack_loss)
    side = jnp.concatenate(
        [
            router_hi,
            router_lo,
            jnp.broadcast_to(loss_hi, (group_size, 1)),
            jnp.broadcast_to(loss_lo, (group_size, 1)),
        ],
        axis=1,
    )
    side_width = -(-side.shape[1] // (per_source * HEAD_WIDTH)) * HEAD_WIDTH
    side = jnp.pad(side, ((0, 0), (0, per_source * side_width - side.shape[1])))
    sent = jnp.concatenate(
        [
            d_out.reshape(group_size, per_source, width),
            side.reshape(group_size, per_source, side_width),
        ],
        axis=2,
    )
    got = across_group(sent)
    grads_arrived = got[:, :, :width].reshape(slots, width)
    grad_down = lax.dot_general(
        hidden, grads_arrived, contract_rows, preferred_element_type=jnp.float32
    )
    grad_down = grad_down.astype(jnp.bfloat16).reshape((1,) + grad_down.shape)
    tail = got[:, :, width:].reshape(group_size, -1)
    grad_router = jnp.sum(join_pair(tail[:, :chunk], tail[:, chunk : 2 * chunk]), axis=0)
    grad_router = grad_router.reshape(-1, experts).astype(jnp.bfloat16)
    loss = jnp.sum(join_pair(tail[:, 2 * chunk], tail[:, 2 * chunk + 1]))
    return (loss, grad_down, grad_router)


def solution(mesh):
    finer = Mesh(
        mesh.devices.reshape(mesh.shape["dp"], 2, 2, 4, 4),
        ("dp", "seq_0", "seq_1", "expert_0", "expert_1"),
    )
    return jax.shard_map(
        shards,
        mesh=finer,
        in_specs=(
            P(EXPERT, DP_SEQ, None),
            P(EXPERT, DP_SEQ, None),
            P(EXPERT, DP_SEQ, None),
            P(EXPERT, DP_SEQ, None),
            P(DP_SEQ, None),
            P(),
            P(),
            P(DP_EXPERT, None, SEQ),
            P(DP_EXPERT, None, SEQ),
            P(DP_EXPERT, SEQ, None),
            P(),
            P(EXPERT, "dp", None),
            P(EXPERT, None),
            P(EXPERT, DP_SEQ),
            P(EXPERT, None),
        ),
        out_specs=(P(), P(DP_EXPERT, SEQ, None), P(DP_SEQ_EXPERT, None)),
        check_vma=False,
    )
```

```python
import jax
import jax.numpy as jnp
from jax import lax
from jax.sharding import Mesh
from jax.sharding import PartitionSpec as P

QUERY_HEADS = 32
KEY_VALUE_HEADS = 4
HEAD_WIDTH = 128
DP_EXPERT = ("dp", "expert_0", "expert_1")
DP_SEQ = ("dp", "seq_0", "seq_1")
SEQ = ("seq_0", "seq_1")
DP_SEQ_EXPERT = ("dp", "seq_0", "seq_1", "expert_0", "expert_1")
EXPERT = ("expert_0", "expert_1")


MASKED = -1e30
EPSILON = 1e-06


def joined_along(blocks, dim):
    blocks = jnp.moveaxis(blocks, 0, dim)
    lengths = blocks.shape
    return blocks.reshape(*lengths[:dim], lengths[dim] * lengths[dim + 1], *lengths[dim + 2 :])


def from_everyone(array, axis):
    copies = jnp.broadcast_to(array, (lax.axis_size(axis), *array.shape))
    return lax.all_to_all(copies, axis, split_axis=0, concat_axis=0, tiled=True)


def gather_directly(array, axis, dim):
    return joined_along(from_everyone(array, axis), dim)


def in_blocks(array, dim, count):
    lengths = array.shape
    blocks = array.reshape(*lengths[:dim], count, lengths[dim] // count, *lengths[dim + 1 :])
    return jnp.moveaxis(blocks, dim, 0)


def sent_and_summed(array, axis, dim):
    count = lax.axis_size(axis)
    blocks = lax.all_to_all(in_blocks(array, dim, count), axis, 0, 0, tiled=True)
    return jnp.sum(blocks.astype(jnp.float32), axis=0)


def rms_scale(stream):
    return lax.rsqrt(jnp.mean(stream * stream, axis=-1, keepdims=True) + EPSILON)


def head_logit(final, head_vec):
    return jnp.sum(final * rms_scale(final) * head_vec.astype(jnp.float32)[None, :], axis=1)


def across_group(buffer):
    return lax.all_to_all(buffer, EXPERT, split_axis=0, concat_axis=0, tiled=True)


def taken_together(array, axis):
    return from_everyone(array, axis).sum(axis=0)


def split_pair(value):
    high = value.astype(jnp.bfloat16)
    low = (value - high.astype(jnp.float32)).astype(jnp.bfloat16)
    return high, low


def join_pair(high, low):
    return high.astype(jnp.float32) + low.astype(jnp.float32)


def merge_heads(weighted_r, totals_r, peak_r):
    peak_all = jnp.max(peak_r, axis=0)
    factor = jnp.exp(peak_r - peak_all[None])
    weighted_sum = jnp.sum(weighted_r * factor[..., None], axis=0)
    totals_sum = jnp.sum(totals_r * factor, axis=0)
    merged = weighted_sum / totals_sum[..., None]
    return merged.reshape(merged.shape[0], -1).astype(jnp.bfloat16)


def shards(
    keys,
    values,
    queries,
    residual,
    out_proj,
    norm_gain,
    router,
    w_gate,
    w_up,
    w_down,
    head_vec,
    routes,
    step_pos,
    labels,
    trace_len,
):
    count_of_keys = keys.shape[1]
    query_groups = QUERY_HEADS // KEY_VALUE_HEADS
    query_width = queries.shape[2]
    own_routes = lax.dynamic_index_in_dim(routes[0], lax.axis_index(SEQ), 0, keepdims=False)
    query_row = jnp.concatenate(
        [
            queries[0],
            own_routes.astype(jnp.bfloat16)[None, :],
            jnp.zeros((1, HEAD_WIDTH - own_routes.shape[0]), jnp.bfloat16),
        ],
        axis=1,
    )
    query_rows = gather_directly(query_row, DP_SEQ, 0)
    query_all = query_rows[:, :query_width]
    pack_routes = query_rows[:, query_width : query_width + routes.shape[2]].astype(jnp.int32)
    positions = step_pos[0]
    number_of_steps = positions.shape[0]
    lengths = trace_len[0]
    trace_ends = jnp.cumsum(lengths)
    starts = jnp.sum(
        jnp.where(trace_ends[None, :] <= positions[:, None], lengths[None, :], 0), axis=1
    )
    key_pos = lax.axis_index(DP_SEQ) * count_of_keys + jnp.arange(count_of_keys, dtype=jnp.int32)
    allowed = (key_pos[None, :] <= positions[:, None]) & (key_pos[None, :] >= starts[:, None])
    score_list = []
    for head_cluster in range(KEY_VALUE_HEADS):
        query_part = query_all[
            :,
            head_cluster
            * query_groups
            * HEAD_WIDTH : (head_cluster + 1)
            * query_groups
            * HEAD_WIDTH,
        ].reshape(number_of_steps * query_groups, HEAD_WIDTH)
        key_part = keys[0, :, head_cluster * HEAD_WIDTH : (head_cluster + 1) * HEAD_WIDTH]
        score_part = lax.dot_general(
            query_part, key_part, (((1,), (1,)), ((), ())), preferred_element_type=jnp.float32
        ) * HEAD_WIDTH ** (-0.5)
        score_part = score_part.reshape(number_of_steps, query_groups, count_of_keys)
        score_list.append(jnp.where(allowed[:, None, :], score_part, MASKED))
    scores = jnp.stack(score_list, axis=1).reshape(number_of_steps, QUERY_HEADS, count_of_keys)
    local_peak = jnp.max(scores, axis=2)
    heads_of_values = values[0].reshape(count_of_keys, KEY_VALUE_HEADS, HEAD_WIDTH)
    shift = local_peak.astype(jnp.bfloat16)
    complete_weight_rows = jnp.where(
        allowed[:, None, :], jnp.exp(scores - shift.astype(jnp.float32)[:, :, None]), 0.0
    )
    totals = jnp.sum(complete_weight_rows, axis=2)
    reduced_weight_rows = complete_weight_rows.astype(jnp.bfloat16).reshape(
        number_of_steps, KEY_VALUE_HEADS, query_groups, count_of_keys
    )
    weighted = jnp.einsum(
        "skgt,tkd->skgd", reduced_weight_rows, heads_of_values, preferred_element_type=jnp.float32
    ).reshape(number_of_steps, QUERY_HEADS, HEAD_WIDTH)
    totals_hi, totals_lo = split_pair(totals)
    stats = jnp.stack([totals_hi, totals_lo, shift, jnp.zeros_like(shift)], axis=-1)
    stats = jnp.swapaxes(stats, 0, 1).reshape(1, QUERY_HEADS, -1)
    packed = jnp.concatenate([weighted.astype(jnp.bfloat16), stats], axis=0)
    packed = jnp.swapaxes(packed, 0, 1).reshape(1, QUERY_HEADS, -1)
    arrived = lax.all_to_all(packed, DP_SEQ, split_axis=1, concat_axis=0, tiled=True)
    arrived = arrived.reshape(arrived.shape[0], number_of_steps + 1, 1, HEAD_WIDTH)
    got_stats = arrived[:, number_of_steps].reshape(arrived.shape[0], number_of_steps, 1, 4)
    attn = merge_heads(
        arrived[:, :number_of_steps].astype(jnp.float32),
        join_pair(got_stats[..., 0], got_stats[..., 1]),
        got_stats[..., 2].astype(jnp.float32),
    )
    mixed = sent_and_summed(
        jnp.dot(attn, out_proj, preferred_element_type=jnp.float32).astype(jnp.bfloat16), DP_SEQ, 0
    )
    stream = residual[0].astype(jnp.float32) + mixed
    normed = (stream * rms_scale(stream) * norm_gain.astype(jnp.float32)[None, :]).astype(
        jnp.bfloat16
    )
    pack_normed = gather_directly(normed, DP_SEQ, 0)
    rows = pack_normed.shape[0]
    width = pack_normed.shape[1]
    block_rows = routes.shape[1]
    topk = routes.shape[2]
    experts = router.shape[1]
    blocks = rows // block_rows
    group_size = lax.axis_size(EXPERT)
    capacity = min(block_rows, 2 * ((block_rows * topk + experts - 1) // experts))
    per_source = blocks * capacity
    slots = group_size * per_source
    logits = jnp.dot(pack_normed, router, preferred_element_type=jnp.float32)
    chosen = (pack_routes[:, :, None] == jnp.arange(experts, dtype=jnp.int32)[None, None, :]).astype(
        jnp.float32
    )
    picked = jnp.sum(chosen * logits[:, None, :], axis=2)
    gate_weight = jax.nn.softmax(picked, axis=-1)
    row_has = jnp.sum(chosen, axis=1).reshape(blocks, block_rows, experts)
    earlier = (jnp.cumsum(row_has, axis=1) - row_has).reshape(rows, experts)
    rank = jnp.sum(chosen * earlier[:, None, :], axis=2).astype(jnp.int32)
    block_of = (jnp.arange(rows, dtype=jnp.int32) // block_rows)[:, None]
    in_group = (pack_routes // group_size) == lax.axis_index("dp")
    dest_slot = (pack_routes % group_size) * per_source + block_of * capacity + rank
    slot_map = (
        (dest_slot[:, :, None] == jnp.arange(slots, dtype=jnp.int32)[None, None, :])
        & in_group[:, :, None]
    ).astype(jnp.float32)
    row_map = jnp.sum(slot_map, axis=1)
    weight_map = jnp.sum(gate_weight[:, :, None] * slot_map, axis=1)
    contract_rows = (((0,), (0,)), ((), ()))
    send_rows = lax.dot_general(
        row_map.astype(jnp.bfloat16), pack_normed, contract_rows, preferred_element_type=jnp.float32
    ).astype(jnp.bfloat16)
    arrived = across_group(send_rows.reshape(group_size, per_source, width)).reshape(slots, width)
    gate_act = jnp.dot(arrived, w_gate[0], preferred_element_type=jnp.float32)
    up_act = jnp.dot(arrived, w_up[0], preferred_element_type=jnp.float32)
    hidden = (jax.nn.silu(gate_act) * up_act).astype(jnp.bfloat16)
    partial_value = jnp.dot(hidden, w_down[0], preferred_element_type=jnp.float32)
    returned = across_group(
        partial_value.astype(jnp.bfloat16).reshape(group_size, per_source, width)
    ).reshape(slots, width)
    group_mix = lax.dot_general(
        weight_map,
        returned.astype(jnp.float32),
        (((1,), (0,)), ((), ())),
        precision=lax.Precision.HIGHEST,
    )
    expert_mix = sent_and_summed(group_mix.astype(jnp.bfloat16), DP_SEQ, 0)
    final = stream + expert_mix
    reward, pull = jax.vjp(lambda value: head_logit(value, head_vec), final)
    target = labels[0].astype(jnp.float32)
    loss_term = jnp.sum(jax.nn.softplus(reward) - target * reward)
    logit_grad = jax.nn.sigmoid(reward) - target
    (final_grad,) = pull(logit_grad)
    d_mix = final_grad.astype(jnp.bfloat16)
    pack_grads = gather_directly(d_mix, DP_SEQ, 0)
    d_out = lax.dot_general(
        weight_map, pack_grads.astype(jnp.float32), contract_rows, precision=lax.Precision.HIGHEST
    ).astype(jnp.bfloat16)
    slot_grads = lax.dot_general(
        row_map.astype(jnp.bfloat16), pack_grads, contract_rows, preferred_element_type=jnp.float32
    )
    slot_dots = jnp.sum(slot_grads * returned.astype(jnp.float32), axis=1)
    dots_part = jnp.sum(slot_map * slot_dots[None, None, :], axis=2)
    own_row = jnp.arange(rows, dtype=jnp.int32) == lax.axis_index(DP_SEQ)
    payload = jnp.concatenate([dots_part, jnp.where(own_row, loss_term, 0.0)[:, None]], axis=1)
    summed = taken_together(payload, DP_SEQ)
    route_dot = summed[:, :topk]
    pack_loss = jnp.sum(summed[:, topk])
    pick_grad = gate_weight * (route_dot - jnp.sum(gate_weight * route_dot, axis=1, keepdims=True))
    d_logits = jnp.sum(chosen * pick_grad[:, :, None], axis=1)
    columns = pack_normed.reshape(rows, lax.axis_size(DP_SEQ), -1)
    my_columns = lax.dynamic_index_in_dim(columns, lax.axis_index(DP_SEQ), 1, keepdims=False)
    router_part = lax.dot_general(
        my_columns.astype(jnp.float32), d_logits, contract_rows, precision=lax.Precision.HIGHEST
    )
    router_part = router_part.reshape(group_size, -1)
    chunk = router_part.shape[1]
    router_hi, router_lo = split_pair(router_part)
    loss_hi, loss_lo = split_pair(pack_loss)
    side = jnp.concatenate(
        [
            router_hi,
            router_lo,
            jnp.broadcast_to(loss_hi, (group_size, 1)),
            jnp.broadcast_to(loss_lo, (group_size, 1)),
        ],
        axis=1,
    )
    side_width = -(-side.shape[1] // (per_source * HEAD_WIDTH)) * HEAD_WIDTH
    side = jnp.pad(side, ((0, 0), (0, per_source * side_width - side.shape[1])))
    sent = jnp.concatenate(
        [
            d_out.reshape(group_size, per_source, width),
            side.reshape(group_size, per_source, side_width),
        ],
        axis=2,
    )
    got = across_group(sent)
    grads_arrived = got[:, :, :width].reshape(slots, width)
    grad_down = lax.dot_general(
        hidden, grads_arrived, contract_rows, preferred_element_type=jnp.float32
    )
    grad_down = grad_down.astype(jnp.bfloat16).reshape((1,) + grad_down.shape)
    tail = got[:, :, width:].reshape(group_size, -1)
    grad_router = jnp.sum(join_pair(tail[:, :chunk], tail[:, chunk : 2 * chunk]), axis=0)
    grad_router = grad_router.reshape(-1, experts).astype(jnp.bfloat16)
    loss = jnp.sum(join_pair(tail[:, 2 * chunk], tail[:, 2 * chunk + 1]))
    return (loss, grad_down, grad_router)


def solution(mesh):
    finer = Mesh(
        mesh.devices.reshape(mesh.shape["dp"], 2, 2, 4, 4),
        ("dp", "seq_0", "seq_1", "expert_0", "expert_1"),
    )
    return jax.shard_map(
        shards,
        mesh=finer,
        in_specs=(
            P(EXPERT, DP_SEQ, None),
            P(EXPERT, DP_SEQ, None),
            P(EXPERT, DP_SEQ, None),
            P(EXPERT, DP_SEQ, None),
            P(DP_SEQ, None),
            P(),
            P(),
            P(DP_EXPERT, None, SEQ),
            P(DP_EXPERT, None, SEQ),
            P(DP_EXPERT, SEQ, None),
            P(),
            P(EXPERT, "dp", None),
            P(EXPERT, None),
            P(EXPERT, DP_SEQ),
            P(EXPERT, None),
        ),
        out_specs=(P(), P(DP_EXPERT, SEQ, None), P(DP_SEQ_EXPERT, None)),
        check_vma=False,
    )
```

```python
import jax
import jax.numpy as jnp
from jax import lax
from jax.sharding import Mesh
from jax.sharding import PartitionSpec as P

QUERY_HEADS = 32
KEY_VALUE_HEADS = 4
HEAD_WIDTH = 128
DP_EXPERT = ("dp", "expert_0", "expert_1")
DP_SEQ = ("dp", "seq_0", "seq_1")
SEQ = ("seq_0", "seq_1")
DP_SEQ_EXPERT = ("dp", "seq_0", "seq_1", "expert_0", "expert_1")
EXPERT = ("expert_0", "expert_1")


MASKED = -1e30
EPSILON = 1e-06


def joined_along(blocks, dim):
    blocks = jnp.moveaxis(blocks, 0, dim)
    lengths = blocks.shape
    return blocks.reshape(*lengths[:dim], lengths[dim] * lengths[dim + 1], *lengths[dim + 2 :])


def from_everyone(array, axis):
    copies = jnp.broadcast_to(array, (lax.axis_size(axis), *array.shape))
    return lax.all_to_all(copies, axis, split_axis=0, concat_axis=0, tiled=True)


def gather_directly(array, axis, dim):
    return joined_along(from_everyone(array, axis), dim)


def in_blocks(array, dim, count):
    lengths = array.shape
    blocks = array.reshape(*lengths[:dim], count, lengths[dim] // count, *lengths[dim + 1 :])
    return jnp.moveaxis(blocks, dim, 0)


def sent_and_summed(array, axis, dim):
    count = lax.axis_size(axis)
    blocks = lax.all_to_all(in_blocks(array, dim, count), axis, 0, 0, tiled=True)
    return jnp.sum(blocks.astype(jnp.float32), axis=0)


def rms_scale(stream):
    return lax.rsqrt(jnp.mean(stream * stream, axis=-1, keepdims=True) + EPSILON)


def head_logit(final, head_vec):
    return jnp.sum(final * rms_scale(final) * head_vec.astype(jnp.float32)[None, :], axis=1)


def across_group(buffer):
    return lax.all_to_all(buffer, EXPERT, split_axis=0, concat_axis=0, tiled=True)


def taken_together(array, axis):
    return from_everyone(array, axis).sum(axis=0)


def split_pair(value):
    high = value.astype(jnp.bfloat16)
    low = (value - high.astype(jnp.float32)).astype(jnp.bfloat16)
    return high, low


def join_pair(high, low):
    return high.astype(jnp.float32) + low.astype(jnp.float32)


def merge_heads(weighted_r, totals_r, peak_r):
    peak_all = jnp.max(peak_r, axis=0)
    factor = jnp.exp(peak_r - peak_all[None])
    weighted_sum = jnp.sum(weighted_r * factor[..., None], axis=0)
    totals_sum = jnp.sum(totals_r * factor, axis=0)
    merged = weighted_sum / totals_sum[..., None]
    return merged.reshape(merged.shape[0], -1).astype(jnp.bfloat16)


def shards(
    keys,
    values,
    queries,
    residual,
    out_proj,
    norm_gain,
    router,
    w_gate,
    w_up,
    w_down,
    head_vec,
    routes,
    step_pos,
    labels,
    trace_len,
):
    count_of_keys = keys.shape[1]
    query_groups = QUERY_HEADS // KEY_VALUE_HEADS
    query_width = queries.shape[2]
    own_routes = lax.dynamic_index_in_dim(routes[0], lax.axis_index(SEQ), 0, keepdims=False)
    query_row = jnp.concatenate(
        [
            queries[0],
            own_routes.astype(jnp.bfloat16)[None, :],
            jnp.zeros((1, HEAD_WIDTH - own_routes.shape[0]), jnp.bfloat16),
        ],
        axis=1,
    )
    query_rows = gather_directly(query_row, DP_SEQ, 0)
    query_all = query_rows[:, :query_width]
    pack_routes = query_rows[:, query_width : query_width + routes.shape[2]].astype(jnp.int32)
    positions = step_pos[0]
    number_of_steps = positions.shape[0]
    lengths = trace_len[0]
    trace_ends = jnp.cumsum(lengths)
    starts = jnp.sum(
        jnp.where(trace_ends[None, :] <= positions[:, None], lengths[None, :], 0), axis=1
    )
    key_pos = lax.axis_index(DP_SEQ) * count_of_keys + jnp.arange(count_of_keys, dtype=jnp.int32)
    allowed = (key_pos[None, :] <= positions[:, None]) & (key_pos[None, :] >= starts[:, None])
    score_list = []
    for head_cluster in range(KEY_VALUE_HEADS):
        query_part = query_all[
            :,
            head_cluster
            * query_groups
            * HEAD_WIDTH : (head_cluster + 1)
            * query_groups
            * HEAD_WIDTH,
        ].reshape(number_of_steps * query_groups, HEAD_WIDTH)
        key_part = keys[0, :, head_cluster * HEAD_WIDTH : (head_cluster + 1) * HEAD_WIDTH]
        score_part = lax.dot_general(
            query_part, key_part, (((1,), (1,)), ((), ())), preferred_element_type=jnp.float32
        ) * HEAD_WIDTH ** (-0.5)
        score_part = score_part.reshape(number_of_steps, query_groups, count_of_keys)
        score_list.append(jnp.where(allowed[:, None, :], score_part, MASKED))
    scores = jnp.stack(score_list, axis=1).reshape(number_of_steps, QUERY_HEADS, count_of_keys)
    local_peak = jnp.max(scores, axis=2)
    heads_of_values = values[0].reshape(count_of_keys, KEY_VALUE_HEADS, HEAD_WIDTH)
    shift = local_peak.astype(jnp.bfloat16)
    complete_weight_rows = jnp.where(
        allowed[:, None, :], jnp.exp(scores - shift.astype(jnp.float32)[:, :, None]), 0.0
    )
    totals = jnp.sum(complete_weight_rows, axis=2)
    reduced_weight_rows = complete_weight_rows.astype(jnp.bfloat16).reshape(
        number_of_steps, KEY_VALUE_HEADS, query_groups, count_of_keys
    )
    weighted = jnp.einsum(
        "skgt,tkd->kgsd", reduced_weight_rows, heads_of_values, preferred_element_type=jnp.float32
    ).reshape(QUERY_HEADS, number_of_steps, HEAD_WIDTH)
    totals_hi, totals_lo = split_pair(totals)
    stats = jnp.stack([totals_hi, totals_lo, shift, jnp.zeros_like(shift)], axis=-1)
    stats = jnp.swapaxes(stats, 0, 1).reshape(QUERY_HEADS, 1, -1)
    packed = jnp.concatenate([weighted.astype(jnp.bfloat16), stats], axis=1)
    packed = packed.reshape(1, QUERY_HEADS, -1)
    arrived = lax.all_to_all(packed, DP_SEQ, split_axis=1, concat_axis=0, tiled=True)
    arrived = arrived.reshape(arrived.shape[0], number_of_steps + 1, 1, HEAD_WIDTH)
    got_stats = arrived[:, number_of_steps].reshape(arrived.shape[0], number_of_steps, 1, 4)
    attn = merge_heads(
        arrived[:, :number_of_steps].astype(jnp.float32),
        join_pair(got_stats[..., 0], got_stats[..., 1]),
        got_stats[..., 2].astype(jnp.float32),
    )
    mixed = sent_and_summed(
        jnp.dot(attn, out_proj, preferred_element_type=jnp.float32).astype(jnp.bfloat16), DP_SEQ, 0
    )
    stream = residual[0].astype(jnp.float32) + mixed
    normed = (stream * rms_scale(stream) * norm_gain.astype(jnp.float32)[None, :]).astype(
        jnp.bfloat16
    )
    pack_normed = gather_directly(normed, DP_SEQ, 0)
    rows = pack_normed.shape[0]
    width = pack_normed.shape[1]
    block_rows = routes.shape[1]
    topk = routes.shape[2]
    experts = router.shape[1]
    blocks = rows // block_rows
    group_size = lax.axis_size(EXPERT)
    capacity = min(block_rows, 2 * ((block_rows * topk + experts - 1) // experts))
    per_source = blocks * capacity
    slots = group_size * per_source
    logits = jnp.dot(pack_normed, router, preferred_element_type=jnp.float32)
    chosen = (pack_routes[:, :, None] == jnp.arange(experts, dtype=jnp.int32)[None, None, :]).astype(
        jnp.float32
    )
    picked = jnp.sum(chosen * logits[:, None, :], axis=2)
    gate_weight = jax.nn.softmax(picked, axis=-1)
    row_has = jnp.sum(chosen, axis=1).reshape(blocks, block_rows, experts)
    earlier = (jnp.cumsum(row_has, axis=1) - row_has).reshape(rows, experts)
    rank = jnp.sum(chosen * earlier[:, None, :], axis=2).astype(jnp.int32)
    block_of = (jnp.arange(rows, dtype=jnp.int32) // block_rows)[:, None]
    in_group = (pack_routes // group_size) == lax.axis_index("dp")
    dest_slot = (pack_routes % group_size) * per_source + block_of * capacity + rank
    slot_map = (
        (dest_slot[:, :, None] == jnp.arange(slots, dtype=jnp.int32)[None, None, :])
        & in_group[:, :, None]
    ).astype(jnp.float32)
    row_map = jnp.sum(slot_map, axis=1)
    weight_map = jnp.sum(gate_weight[:, :, None] * slot_map, axis=1)
    contract_rows = (((0,), (0,)), ((), ()))
    send_rows = lax.dot_general(
        row_map.astype(jnp.bfloat16), pack_normed, contract_rows, preferred_element_type=jnp.float32
    ).astype(jnp.bfloat16)
    arrived = across_group(send_rows.reshape(group_size, per_source, width)).reshape(slots, width)
    gate_act = jnp.dot(arrived, w_gate[0], preferred_element_type=jnp.float32)
    up_act = jnp.dot(arrived, w_up[0], preferred_element_type=jnp.float32)
    hidden = (jax.nn.silu(gate_act) * up_act).astype(jnp.bfloat16)
    partial_value = jnp.dot(hidden, w_down[0], preferred_element_type=jnp.float32)
    returned = across_group(
        partial_value.astype(jnp.bfloat16).reshape(group_size, per_source, width)
    ).reshape(slots, width)
    group_mix = lax.dot_general(
        weight_map,
        returned.astype(jnp.float32),
        (((1,), (0,)), ((), ())),
        precision=lax.Precision.HIGHEST,
    )
    expert_mix = sent_and_summed(group_mix.astype(jnp.bfloat16), DP_SEQ, 0)
    final = stream + expert_mix
    reward, pull = jax.vjp(lambda value: head_logit(value, head_vec), final)
    target = labels[0].astype(jnp.float32)
    loss_term = jnp.sum(jax.nn.softplus(reward) - target * reward)
    logit_grad = jax.nn.sigmoid(reward) - target
    (final_grad,) = pull(logit_grad)
    d_mix = final_grad.astype(jnp.bfloat16)
    pack_grads = gather_directly(d_mix, DP_SEQ, 0)
    d_out = lax.dot_general(
        weight_map, pack_grads.astype(jnp.float32), contract_rows, precision=lax.Precision.HIGHEST
    ).astype(jnp.bfloat16)
    slot_grads = lax.dot_general(
        row_map.astype(jnp.bfloat16), pack_grads, contract_rows, preferred_element_type=jnp.float32
    )
    slot_dots = jnp.sum(slot_grads * returned.astype(jnp.float32), axis=1)
    dots_part = jnp.sum(slot_map * slot_dots[None, None, :], axis=2)
    own_row = jnp.arange(rows, dtype=jnp.int32) == lax.axis_index(DP_SEQ)
    payload = jnp.concatenate([dots_part, jnp.where(own_row, loss_term, 0.0)[:, None]], axis=1)
    summed = taken_together(payload, DP_SEQ)
    route_dot = summed[:, :topk]
    pack_loss = jnp.sum(summed[:, topk])
    pick_grad = gate_weight * (route_dot - jnp.sum(gate_weight * route_dot, axis=1, keepdims=True))
    d_logits = jnp.sum(chosen * pick_grad[:, :, None], axis=1)
    columns = pack_normed.reshape(rows, lax.axis_size(DP_SEQ), -1)
    my_columns = lax.dynamic_index_in_dim(columns, lax.axis_index(DP_SEQ), 1, keepdims=False)
    router_part = lax.dot_general(
        my_columns.astype(jnp.float32), d_logits, contract_rows, precision=lax.Precision.HIGHEST
    )
    router_part = router_part.reshape(group_size, -1)
    chunk = router_part.shape[1]
    router_hi, router_lo = split_pair(router_part)
    loss_hi, loss_lo = split_pair(pack_loss)
    side = jnp.concatenate(
        [
            router_hi,
            router_lo,
            jnp.broadcast_to(loss_hi, (group_size, 1)),
            jnp.broadcast_to(loss_lo, (group_size, 1)),
        ],
        axis=1,
    )
    side_width = -(-side.shape[1] // (per_source * HEAD_WIDTH)) * HEAD_WIDTH
    side = jnp.pad(side, ((0, 0), (0, per_source * side_width - side.shape[1])))
    sent = jnp.concatenate(
        [
            d_out.reshape(group_size, per_source, width),
            side.reshape(group_size, per_source, side_width),
        ],
        axis=2,
    )
    got = across_group(sent)
    grads_arrived = got[:, :, :width].reshape(slots, width)
    grad_down = lax.dot_general(
        hidden, grads_arrived, contract_rows, preferred_element_type=jnp.float32
    )
    grad_down = grad_down.astype(jnp.bfloat16).reshape((1,) + grad_down.shape)
    tail = got[:, :, width:].reshape(group_size, -1)
    grad_router = jnp.sum(join_pair(tail[:, :chunk], tail[:, chunk : 2 * chunk]), axis=0)
    grad_router = grad_router.reshape(-1, experts).astype(jnp.bfloat16)
    loss = jnp.sum(join_pair(tail[:, 2 * chunk], tail[:, 2 * chunk + 1]))
    return (loss, grad_down, grad_router)


def solution(mesh):
    finer = Mesh(
        mesh.devices.reshape(mesh.shape["dp"], 2, 2, 4, 4),
        ("dp", "seq_0", "seq_1", "expert_0", "expert_1"),
    )
    return jax.shard_map(
        shards,
        mesh=finer,
        in_specs=(
            P(EXPERT, DP_SEQ, None),
            P(EXPERT, DP_SEQ, None),
            P(EXPERT, DP_SEQ, None),
            P(EXPERT, DP_SEQ, None),
            P(DP_SEQ, None),
            P(),
            P(),
            P(DP_EXPERT, None, SEQ),
            P(DP_EXPERT, None, SEQ),
            P(DP_EXPERT, SEQ, None),
            P(),
            P(EXPERT, "dp", None),
            P(EXPERT, None),
            P(EXPERT, DP_SEQ),
            P(EXPERT, None),
        ),
        out_specs=(P(), P(DP_EXPERT, SEQ, None), P(DP_SEQ_EXPERT, None)),
        check_vma=False,
    )
```

```python
import jax
import jax.numpy as jnp
from jax import lax
from jax.sharding import Mesh
from jax.sharding import PartitionSpec as P

QUERY_HEADS = 32
KEY_VALUE_HEADS = 4
HEAD_WIDTH = 128
DP_EXPERT = ("dp", "expert_0", "expert_1")
DP_SEQ = ("dp", "seq_0", "seq_1")
SEQ = ("seq_0", "seq_1")
DP_SEQ_EXPERT = ("dp", "seq_0", "seq_1", "expert_0", "expert_1")
EXPERT = ("expert_0", "expert_1")


MASKED = -1e30
EPSILON = 1e-06


def joined_along(blocks, dim):
    blocks = jnp.moveaxis(blocks, 0, dim)
    lengths = blocks.shape
    return blocks.reshape(*lengths[:dim], lengths[dim] * lengths[dim + 1], *lengths[dim + 2 :])


def from_everyone(array, axis):
    copies = jnp.broadcast_to(array, (lax.axis_size(axis), *array.shape))
    return lax.all_to_all(copies, axis, split_axis=0, concat_axis=0, tiled=True)


def gather_directly(array, axis, dim):
    return joined_along(from_everyone(array, axis), dim)


def in_blocks(array, dim, count):
    lengths = array.shape
    blocks = array.reshape(*lengths[:dim], count, lengths[dim] // count, *lengths[dim + 1 :])
    return jnp.moveaxis(blocks, dim, 0)


def sent_and_summed(array, axis, dim):
    count = lax.axis_size(axis)
    blocks = lax.all_to_all(in_blocks(array, dim, count), axis, 0, 0, tiled=True)
    return jnp.sum(blocks.astype(jnp.float32), axis=0)


def rms_scale(stream):
    return lax.rsqrt(jnp.mean(stream * stream, axis=-1, keepdims=True) + EPSILON)


def head_logit(final, head_vec):
    return jnp.sum(final * rms_scale(final) * head_vec.astype(jnp.float32)[None, :], axis=1)


def across_group(buffer):
    return lax.all_to_all(buffer, EXPERT, split_axis=0, concat_axis=0, tiled=True)


def taken_together(array, axis):
    return from_everyone(array, axis).sum(axis=0)


def split_pair(value):
    high = value.astype(jnp.bfloat16)
    low = (value - high.astype(jnp.float32)).astype(jnp.bfloat16)
    return high, low


def join_pair(high, low):
    return high.astype(jnp.float32) + low.astype(jnp.float32)


def merge_heads(weighted_r, totals_r, peak_r):
    peak_all = jnp.max(peak_r, axis=0)
    factor = jnp.exp(peak_r - peak_all[None])
    weighted_sum = jnp.sum(weighted_r * factor[..., None], axis=0)
    totals_sum = jnp.sum(totals_r * factor, axis=0)
    merged = weighted_sum / totals_sum[..., None]
    return merged.reshape(merged.shape[0], -1).astype(jnp.bfloat16)


def shards(
    keys,
    values,
    queries,
    residual,
    out_proj,
    norm_gain,
    router,
    w_gate,
    w_up,
    w_down,
    head_vec,
    routes,
    step_pos,
    labels,
    trace_len,
):
    count_of_keys = keys.shape[1]
    query_groups = QUERY_HEADS // KEY_VALUE_HEADS
    query_width = queries.shape[2]
    own_routes = lax.dynamic_index_in_dim(routes[0], lax.axis_index(SEQ), 0, keepdims=False)
    query_row = jnp.concatenate(
        [
            queries[0],
            own_routes.astype(jnp.bfloat16)[None, :],
            jnp.zeros((1, 2 * HEAD_WIDTH - own_routes.shape[0]), jnp.bfloat16),
        ],
        axis=1,
    )
    query_rows = from_everyone(query_row.reshape(2, -1), DP_SEQ).reshape(lax.axis_size(DP_SEQ), -1)
    query_all = query_rows[:, :query_width]
    pack_routes = query_rows[:, query_width : query_width + routes.shape[2]].astype(jnp.int32)
    positions = step_pos[0]
    number_of_steps = positions.shape[0]
    lengths = trace_len[0]
    trace_ends = jnp.cumsum(lengths)
    starts = jnp.sum(
        jnp.where(trace_ends[None, :] <= positions[:, None], lengths[None, :], 0), axis=1
    )
    key_pos = lax.axis_index(DP_SEQ) * count_of_keys + jnp.arange(count_of_keys, dtype=jnp.int32)
    allowed = (key_pos[None, :] <= positions[:, None]) & (key_pos[None, :] >= starts[:, None])
    score_list = []
    for head_cluster in range(KEY_VALUE_HEADS):
        query_part = query_all[
            :,
            head_cluster
            * query_groups
            * HEAD_WIDTH : (head_cluster + 1)
            * query_groups
            * HEAD_WIDTH,
        ].reshape(number_of_steps * query_groups, HEAD_WIDTH)
        key_part = keys[0, :, head_cluster * HEAD_WIDTH : (head_cluster + 1) * HEAD_WIDTH]
        score_part = lax.dot_general(
            query_part, key_part, (((1,), (1,)), ((), ())), preferred_element_type=jnp.float32
        ) * HEAD_WIDTH ** (-0.5)
        score_part = score_part.reshape(number_of_steps, query_groups, count_of_keys)
        score_list.append(jnp.where(allowed[:, None, :], score_part, MASKED))
    scores = jnp.stack(score_list, axis=1).reshape(number_of_steps, QUERY_HEADS, count_of_keys)
    local_peak = jnp.max(scores, axis=2)
    heads_of_values = values[0].reshape(count_of_keys, KEY_VALUE_HEADS, HEAD_WIDTH)
    shift = local_peak.astype(jnp.bfloat16)
    complete_weight_rows = jnp.where(
        allowed[:, None, :], jnp.exp(scores - shift.astype(jnp.float32)[:, :, None]), 0.0
    )
    totals = jnp.sum(complete_weight_rows, axis=2)
    reduced_weight_rows = complete_weight_rows.astype(jnp.bfloat16).reshape(
        number_of_steps, KEY_VALUE_HEADS, query_groups, count_of_keys
    )
    weighted = jnp.einsum(
        "skgt,tkd->kgsd", reduced_weight_rows, heads_of_values, preferred_element_type=jnp.float32
    ).reshape(QUERY_HEADS, number_of_steps, HEAD_WIDTH)
    totals_hi, totals_lo = split_pair(totals)
    stats = jnp.stack([totals_hi, totals_lo, shift, jnp.zeros_like(shift)], axis=-1)
    stats = jnp.swapaxes(stats, 0, 1).reshape(QUERY_HEADS, 1, -1)
    filler = jnp.zeros((QUERY_HEADS, 1, HEAD_WIDTH), jnp.bfloat16)
    packed = jnp.concatenate([weighted.astype(jnp.bfloat16), stats, filler], axis=1)
    packed = packed.reshape(QUERY_HEADS, 2, -1)
    arrived = lax.all_to_all(packed, DP_SEQ, split_axis=0, concat_axis=0, tiled=True)
    arrived = arrived.reshape(arrived.shape[0], number_of_steps + 2, 1, HEAD_WIDTH)
    got_stats = arrived[:, number_of_steps].reshape(arrived.shape[0], number_of_steps, 1, 4)
    attn = merge_heads(
        arrived[:, :number_of_steps].astype(jnp.float32),
        join_pair(got_stats[..., 0], got_stats[..., 1]),
        got_stats[..., 2].astype(jnp.float32),
    )
    mixed = sent_and_summed(
        jnp.dot(attn, out_proj, preferred_element_type=jnp.float32).astype(jnp.bfloat16), DP_SEQ, 0
    )
    stream = residual[0].astype(jnp.float32) + mixed
    normed = (stream * rms_scale(stream) * norm_gain.astype(jnp.float32)[None, :]).astype(
        jnp.bfloat16
    )
    pack_normed = gather_directly(normed, DP_SEQ, 0)
    rows = pack_normed.shape[0]
    width = pack_normed.shape[1]
    block_rows = routes.shape[1]
    topk = routes.shape[2]
    experts = router.shape[1]
    blocks = rows // block_rows
    group_size = lax.axis_size(EXPERT)
    capacity = min(block_rows, 2 * ((block_rows * topk + experts - 1) // experts))
    per_source = blocks * capacity
    slots = group_size * per_source
    logits = jnp.dot(pack_normed, router, preferred_element_type=jnp.float32)
    chosen = (pack_routes[:, :, None] == jnp.arange(experts, dtype=jnp.int32)[None, None, :]).astype(
        jnp.float32
    )
    picked = jnp.sum(chosen * logits[:, None, :], axis=2)
    gate_weight = jax.nn.softmax(picked, axis=-1)
    row_has = jnp.sum(chosen, axis=1).reshape(blocks, block_rows, experts)
    earlier = (jnp.cumsum(row_has, axis=1) - row_has).reshape(rows, experts)
    rank = jnp.sum(chosen * earlier[:, None, :], axis=2).astype(jnp.int32)
    block_of = (jnp.arange(rows, dtype=jnp.int32) // block_rows)[:, None]
    in_group = (pack_routes // group_size) == lax.axis_index("dp")
    dest_slot = (pack_routes % group_size) * per_source + block_of * capacity + rank
    slot_map = (
        (dest_slot[:, :, None] == jnp.arange(slots, dtype=jnp.int32)[None, None, :])
        & in_group[:, :, None]
    ).astype(jnp.float32)
    row_map = jnp.sum(slot_map, axis=1)
    weight_map = jnp.sum(gate_weight[:, :, None] * slot_map, axis=1)
    contract_rows = (((0,), (0,)), ((), ()))
    send_rows = lax.dot_general(
        row_map.astype(jnp.bfloat16), pack_normed, contract_rows, preferred_element_type=jnp.float32
    ).astype(jnp.bfloat16)
    arrived = across_group(send_rows.reshape(group_size, per_source, width)).reshape(slots, width)
    gate_act = jnp.dot(arrived, w_gate[0], preferred_element_type=jnp.float32)
    up_act = jnp.dot(arrived, w_up[0], preferred_element_type=jnp.float32)
    hidden = (jax.nn.silu(gate_act) * up_act).astype(jnp.bfloat16)
    partial_value = jnp.dot(hidden, w_down[0], preferred_element_type=jnp.float32)
    returned = across_group(
        partial_value.astype(jnp.bfloat16).reshape(group_size, per_source, width)
    ).reshape(slots, width)
    group_mix = lax.dot_general(
        weight_map,
        returned.astype(jnp.float32),
        (((1,), (0,)), ((), ())),
        precision=lax.Precision.HIGHEST,
    )
    expert_mix = sent_and_summed(group_mix.astype(jnp.bfloat16), DP_SEQ, 0)
    final = stream + expert_mix
    reward, pull = jax.vjp(lambda value: head_logit(value, head_vec), final)
    target = labels[0].astype(jnp.float32)
    loss_term = jnp.sum(jax.nn.softplus(reward) - target * reward)
    logit_grad = jax.nn.sigmoid(reward) - target
    (final_grad,) = pull(logit_grad)
    d_mix = final_grad.astype(jnp.bfloat16)
    pack_grads = gather_directly(d_mix, DP_SEQ, 0)
    d_out = lax.dot_general(
        weight_map, pack_grads.astype(jnp.float32), contract_rows, precision=lax.Precision.HIGHEST
    ).astype(jnp.bfloat16)
    slot_grads = lax.dot_general(
        row_map.astype(jnp.bfloat16), pack_grads, contract_rows, preferred_element_type=jnp.float32
    )
    slot_dots = jnp.sum(slot_grads * returned.astype(jnp.float32), axis=1)
    dots_part = jnp.sum(slot_map * slot_dots[None, None, :], axis=2)
    own_row = jnp.arange(rows, dtype=jnp.int32) == lax.axis_index(DP_SEQ)
    payload = jnp.concatenate([dots_part, jnp.where(own_row, loss_term, 0.0)[:, None]], axis=1)
    summed = taken_together(payload, DP_SEQ)
    route_dot = summed[:, :topk]
    pack_loss = jnp.sum(summed[:, topk])
    pick_grad = gate_weight * (route_dot - jnp.sum(gate_weight * route_dot, axis=1, keepdims=True))
    d_logits = jnp.sum(chosen * pick_grad[:, :, None], axis=1)
    columns = pack_normed.reshape(rows, lax.axis_size(DP_SEQ), -1)
    my_columns = lax.dynamic_index_in_dim(columns, lax.axis_index(DP_SEQ), 1, keepdims=False)
    router_part = lax.dot_general(
        my_columns.astype(jnp.float32), d_logits, contract_rows, precision=lax.Precision.HIGHEST
    )
    router_part = router_part.reshape(group_size, -1)
    chunk = router_part.shape[1]
    router_hi, router_lo = split_pair(router_part)
    loss_hi, loss_lo = split_pair(pack_loss)
    side = jnp.concatenate(
        [
            router_hi,
            router_lo,
            jnp.broadcast_to(loss_hi, (group_size, 1)),
            jnp.broadcast_to(loss_lo, (group_size, 1)),
        ],
        axis=1,
    )
    side_width = -(-side.shape[1] // (per_source * HEAD_WIDTH)) * HEAD_WIDTH
    side = jnp.pad(side, ((0, 0), (0, per_source * side_width - side.shape[1])))
    sent = jnp.concatenate(
        [
            d_out.reshape(group_size, per_source, width),
            side.reshape(group_size, per_source, side_width),
        ],
        axis=2,
    )
    got = across_group(sent)
    grads_arrived = got[:, :, :width].reshape(slots, width)
    grad_down = lax.dot_general(
        hidden, grads_arrived, contract_rows, preferred_element_type=jnp.float32
    )
    grad_down = grad_down.astype(jnp.bfloat16).reshape((1,) + grad_down.shape)
    tail = got[:, :, width:].reshape(group_size, -1)
    grad_router = jnp.sum(join_pair(tail[:, :chunk], tail[:, chunk : 2 * chunk]), axis=0)
    grad_router = grad_router.reshape(-1, experts).astype(jnp.bfloat16)
    loss = jnp.sum(join_pair(tail[:, 2 * chunk], tail[:, 2 * chunk + 1]))
    return (loss, grad_down, grad_router)


def solution(mesh):
    finer = Mesh(
        mesh.devices.reshape(mesh.shape["dp"], 2, 2, 4, 4),
        ("dp", "seq_0", "seq_1", "expert_0", "expert_1"),
    )
    return jax.shard_map(
        shards,
        mesh=finer,
        in_specs=(
            P(EXPERT, DP_SEQ, None),
            P(EXPERT, DP_SEQ, None),
            P(EXPERT, DP_SEQ, None),
            P(EXPERT, DP_SEQ, None),
            P(DP_SEQ, None),
            P(),
            P(),
            P(DP_EXPERT, None, SEQ),
            P(DP_EXPERT, None, SEQ),
            P(DP_EXPERT, SEQ, None),
            P(),
            P(EXPERT, "dp", None),
            P(EXPERT, None),
            P(EXPERT, DP_SEQ),
            P(EXPERT, None),
        ),
        out_specs=(P(), P(DP_EXPERT, SEQ, None), P(DP_SEQ_EXPERT, None)),
        check_vma=False,
    )
```

```python
import jax
import jax.numpy as jnp
from jax import lax
from jax.sharding import Mesh
from jax.sharding import PartitionSpec as P

QUERY_HEADS = 32
KEY_VALUE_HEADS = 4
HEAD_WIDTH = 128
DP_EXPERT = ("dp", "expert_0", "expert_1")
DP_SEQ = ("dp", "seq_0", "seq_1")
SEQ = ("seq_0", "seq_1")
DP_SEQ_EXPERT = ("dp", "seq_0", "seq_1", "expert_0", "expert_1")
EXPERT = ("expert_0", "expert_1")


MASKED = -1e30
EPSILON = 1e-06


def joined_along(blocks, dim):
    blocks = jnp.moveaxis(blocks, 0, dim)
    lengths = blocks.shape
    return blocks.reshape(*lengths[:dim], lengths[dim] * lengths[dim + 1], *lengths[dim + 2 :])


def from_everyone(array, axis):
    copies = jnp.broadcast_to(array, (lax.axis_size(axis), *array.shape))
    return lax.all_to_all(copies, axis, split_axis=0, concat_axis=0, tiled=True)


def gather_directly(array, axis, dim):
    return joined_along(from_everyone(array, axis), dim)


def in_blocks(array, dim, count):
    lengths = array.shape
    blocks = array.reshape(*lengths[:dim], count, lengths[dim] // count, *lengths[dim + 1 :])
    return jnp.moveaxis(blocks, dim, 0)


def sent_and_summed(array, axis, dim):
    count = lax.axis_size(axis)
    blocks = lax.all_to_all(in_blocks(array, dim, count), axis, 0, 0, tiled=True)
    return jnp.sum(blocks.astype(jnp.float32), axis=0)


def rows_summed(array, axis):
    count = lax.axis_size(axis)
    blocks = lax.all_to_all(array.reshape(count, 2, -1), axis, 0, 0, tiled=True)
    return jnp.sum(blocks.astype(jnp.float32), axis=0).reshape(1, -1)


def rows_gathered(row, axis):
    return from_everyone(row.reshape(2, -1), axis).reshape(lax.axis_size(axis), -1)


def rms_scale(stream):
    return lax.rsqrt(jnp.mean(stream * stream, axis=-1, keepdims=True) + EPSILON)


def head_logit(final, head_vec):
    return jnp.sum(final * rms_scale(final) * head_vec.astype(jnp.float32)[None, :], axis=1)


def across_group(buffer):
    return lax.all_to_all(buffer, EXPERT, split_axis=0, concat_axis=0, tiled=True)


def taken_together(array, axis):
    return from_everyone(array, axis).sum(axis=0)


def split_pair(value):
    high = value.astype(jnp.bfloat16)
    low = (value - high.astype(jnp.float32)).astype(jnp.bfloat16)
    return high, low


def join_pair(high, low):
    return high.astype(jnp.float32) + low.astype(jnp.float32)


def merge_heads(weighted_r, totals_r, peak_r):
    peak_all = jnp.max(peak_r, axis=0)
    factor = jnp.exp(peak_r - peak_all[None])
    weighted_sum = jnp.sum(weighted_r * factor[..., None], axis=0)
    totals_sum = jnp.sum(totals_r * factor, axis=0)
    merged = weighted_sum / totals_sum[..., None]
    return merged.reshape(merged.shape[0], -1).astype(jnp.bfloat16)


def shards(
    keys,
    values,
    queries,
    residual,
    out_proj,
    norm_gain,
    router,
    w_gate,
    w_up,
    w_down,
    head_vec,
    routes,
    step_pos,
    labels,
    trace_len,
):
    count_of_keys = keys.shape[1]
    query_groups = QUERY_HEADS // KEY_VALUE_HEADS
    query_width = queries.shape[2]
    own_routes = lax.dynamic_index_in_dim(routes[0], lax.axis_index(SEQ), 0, keepdims=False)
    query_row = jnp.concatenate(
        [
            queries[0],
            own_routes.astype(jnp.bfloat16)[None, :],
            jnp.zeros((1, 2 * HEAD_WIDTH - own_routes.shape[0]), jnp.bfloat16),
        ],
        axis=1,
    )
    query_rows = from_everyone(query_row.reshape(2, -1), DP_SEQ).reshape(lax.axis_size(DP_SEQ), -1)
    query_all = query_rows[:, :query_width]
    pack_routes = query_rows[:, query_width : query_width + routes.shape[2]].astype(jnp.int32)
    positions = step_pos[0]
    number_of_steps = positions.shape[0]
    lengths = trace_len[0]
    trace_ends = jnp.cumsum(lengths)
    starts = jnp.sum(
        jnp.where(trace_ends[None, :] <= positions[:, None], lengths[None, :], 0), axis=1
    )
    key_pos = lax.axis_index(DP_SEQ) * count_of_keys + jnp.arange(count_of_keys, dtype=jnp.int32)
    allowed = (key_pos[None, :] <= positions[:, None]) & (key_pos[None, :] >= starts[:, None])
    score_list = []
    for head_cluster in range(KEY_VALUE_HEADS):
        query_part = query_all[
            :,
            head_cluster
            * query_groups
            * HEAD_WIDTH : (head_cluster + 1)
            * query_groups
            * HEAD_WIDTH,
        ].reshape(number_of_steps * query_groups, HEAD_WIDTH)
        key_part = keys[0, :, head_cluster * HEAD_WIDTH : (head_cluster + 1) * HEAD_WIDTH]
        score_part = lax.dot_general(
            query_part, key_part, (((1,), (1,)), ((), ())), preferred_element_type=jnp.float32
        ) * HEAD_WIDTH ** (-0.5)
        score_part = score_part.reshape(number_of_steps, query_groups, count_of_keys)
        score_list.append(jnp.where(allowed[:, None, :], score_part, MASKED))
    scores = jnp.stack(score_list, axis=1).reshape(number_of_steps, QUERY_HEADS, count_of_keys)
    local_peak = jnp.max(scores, axis=2)
    heads_of_values = values[0].reshape(count_of_keys, KEY_VALUE_HEADS, HEAD_WIDTH)
    shift = local_peak.astype(jnp.bfloat16)
    complete_weight_rows = jnp.where(
        allowed[:, None, :], jnp.exp(scores - shift.astype(jnp.float32)[:, :, None]), 0.0
    )
    totals = jnp.sum(complete_weight_rows, axis=2)
    reduced_weight_rows = complete_weight_rows.astype(jnp.bfloat16).reshape(
        number_of_steps, KEY_VALUE_HEADS, query_groups, count_of_keys
    )
    weighted = jnp.einsum(
        "skgt,tkd->kgsd", reduced_weight_rows, heads_of_values, preferred_element_type=jnp.float32
    ).reshape(QUERY_HEADS, number_of_steps, HEAD_WIDTH)
    totals_hi, totals_lo = split_pair(totals)
    stats = jnp.stack([totals_hi, totals_lo, shift, jnp.zeros_like(shift)], axis=-1)
    stats = jnp.swapaxes(stats, 0, 1).reshape(QUERY_HEADS, 1, -1)
    filler = jnp.zeros((QUERY_HEADS, 1, HEAD_WIDTH), jnp.bfloat16)
    packed = jnp.concatenate([weighted.astype(jnp.bfloat16), stats, filler], axis=1)
    packed = packed.reshape(QUERY_HEADS, 2, -1)
    arrived = lax.all_to_all(packed, DP_SEQ, split_axis=0, concat_axis=0, tiled=True)
    arrived = arrived.reshape(arrived.shape[0], number_of_steps + 2, 1, HEAD_WIDTH)
    got_stats = arrived[:, number_of_steps].reshape(arrived.shape[0], number_of_steps, 1, 4)
    attn = merge_heads(
        arrived[:, :number_of_steps].astype(jnp.float32),
        join_pair(got_stats[..., 0], got_stats[..., 1]),
        got_stats[..., 2].astype(jnp.float32),
    )
    mixed = rows_summed(
        jnp.dot(attn, out_proj, preferred_element_type=jnp.float32).astype(jnp.bfloat16), DP_SEQ
    )
    stream = residual[0].astype(jnp.float32) + mixed
    normed = (stream * rms_scale(stream) * norm_gain.astype(jnp.float32)[None, :]).astype(
        jnp.bfloat16
    )
    pack_normed = rows_gathered(normed, DP_SEQ)
    rows = pack_normed.shape[0]
    width = pack_normed.shape[1]
    block_rows = routes.shape[1]
    topk = routes.shape[2]
    experts = router.shape[1]
    blocks = rows // block_rows
    group_size = lax.axis_size(EXPERT)
    capacity = min(block_rows, 2 * ((block_rows * topk + experts - 1) // experts))
    per_source = blocks * capacity
    slots = group_size * per_source
    logits = jnp.dot(pack_normed, router, preferred_element_type=jnp.float32)
    chosen = (pack_routes[:, :, None] == jnp.arange(experts, dtype=jnp.int32)[None, None, :]).astype(
        jnp.float32
    )
    picked = jnp.sum(chosen * logits[:, None, :], axis=2)
    gate_weight = jax.nn.softmax(picked, axis=-1)
    row_has = jnp.sum(chosen, axis=1).reshape(blocks, block_rows, experts)
    earlier = (jnp.cumsum(row_has, axis=1) - row_has).reshape(rows, experts)
    rank = jnp.sum(chosen * earlier[:, None, :], axis=2).astype(jnp.int32)
    block_of = (jnp.arange(rows, dtype=jnp.int32) // block_rows)[:, None]
    in_group = (pack_routes // group_size) == lax.axis_index("dp")
    dest_slot = (pack_routes % group_size) * per_source + block_of * capacity + rank
    slot_map = (
        (dest_slot[:, :, None] == jnp.arange(slots, dtype=jnp.int32)[None, None, :])
        & in_group[:, :, None]
    ).astype(jnp.float32)
    row_map = jnp.sum(slot_map, axis=1)
    weight_map = jnp.sum(gate_weight[:, :, None] * slot_map, axis=1)
    contract_rows = (((0,), (0,)), ((), ()))
    send_rows = lax.dot_general(
        row_map.astype(jnp.bfloat16), pack_normed, contract_rows, preferred_element_type=jnp.float32
    ).astype(jnp.bfloat16)
    arrived = across_group(send_rows.reshape(group_size, per_source, width)).reshape(slots, width)
    gate_act = jnp.dot(arrived, w_gate[0], preferred_element_type=jnp.float32)
    up_act = jnp.dot(arrived, w_up[0], preferred_element_type=jnp.float32)
    hidden = (jax.nn.silu(gate_act) * up_act).astype(jnp.bfloat16)
    partial_value = jnp.dot(hidden, w_down[0], preferred_element_type=jnp.float32)
    returned = across_group(
        partial_value.astype(jnp.bfloat16).reshape(group_size, per_source, width)
    ).reshape(slots, width)
    group_mix = lax.dot_general(
        weight_map,
        returned.astype(jnp.float32),
        (((1,), (0,)), ((), ())),
        precision=lax.Precision.HIGHEST,
    )
    expert_mix = rows_summed(group_mix.astype(jnp.bfloat16), DP_SEQ)
    final = stream + expert_mix
    reward, pull = jax.vjp(lambda value: head_logit(value, head_vec), final)
    target = labels[0].astype(jnp.float32)
    loss_term = jnp.sum(jax.nn.softplus(reward) - target * reward)
    logit_grad = jax.nn.sigmoid(reward) - target
    (final_grad,) = pull(logit_grad)
    d_mix = final_grad.astype(jnp.bfloat16)
    pack_grads = rows_gathered(d_mix, DP_SEQ)
    d_out = lax.dot_general(
        weight_map, pack_grads.astype(jnp.float32), contract_rows, precision=lax.Precision.HIGHEST
    ).astype(jnp.bfloat16)
    slot_grads = lax.dot_general(
        row_map.astype(jnp.bfloat16), pack_grads, contract_rows, preferred_element_type=jnp.float32
    )
    slot_dots = jnp.sum(slot_grads * returned.astype(jnp.float32), axis=1)
    dots_part = jnp.sum(slot_map * slot_dots[None, None, :], axis=2)
    own_row = jnp.arange(rows, dtype=jnp.int32) == lax.axis_index(DP_SEQ)
    payload = jnp.concatenate([dots_part, jnp.where(own_row, loss_term, 0.0)[:, None]], axis=1)
    summed = taken_together(payload, DP_SEQ)
    route_dot = summed[:, :topk]
    pack_loss = jnp.sum(summed[:, topk])
    pick_grad = gate_weight * (route_dot - jnp.sum(gate_weight * route_dot, axis=1, keepdims=True))
    d_logits = jnp.sum(chosen * pick_grad[:, :, None], axis=1)
    columns = pack_normed.reshape(rows, lax.axis_size(DP_SEQ), -1)
    my_columns = lax.dynamic_index_in_dim(columns, lax.axis_index(DP_SEQ), 1, keepdims=False)
    router_part = lax.dot_general(
        my_columns.astype(jnp.float32), d_logits, contract_rows, precision=lax.Precision.HIGHEST
    )
    router_part = router_part.reshape(group_size, -1)
    chunk = router_part.shape[1]
    router_hi, router_lo = split_pair(router_part)
    loss_hi, loss_lo = split_pair(pack_loss)
    side = jnp.concatenate(
        [
            router_hi,
            router_lo,
            jnp.broadcast_to(loss_hi, (group_size, 1)),
            jnp.broadcast_to(loss_lo, (group_size, 1)),
        ],
        axis=1,
    )
    side_width = -(-side.shape[1] // (per_source * HEAD_WIDTH)) * HEAD_WIDTH
    side = jnp.pad(side, ((0, 0), (0, per_source * side_width - side.shape[1])))
    sent = jnp.concatenate(
        [
            d_out.reshape(group_size, per_source, width),
            side.reshape(group_size, per_source, side_width),
        ],
        axis=2,
    )
    got = across_group(sent)
    grads_arrived = got[:, :, :width].reshape(slots, width)
    grad_down = lax.dot_general(
        hidden, grads_arrived, contract_rows, preferred_element_type=jnp.float32
    )
    grad_down = grad_down.astype(jnp.bfloat16).reshape((1,) + grad_down.shape)
    tail = got[:, :, width:].reshape(group_size, -1)
    grad_router = jnp.sum(join_pair(tail[:, :chunk], tail[:, chunk : 2 * chunk]), axis=0)
    grad_router = grad_router.reshape(-1, experts).astype(jnp.bfloat16)
    loss = jnp.sum(join_pair(tail[:, 2 * chunk], tail[:, 2 * chunk + 1]))
    return (loss, grad_down, grad_router)


def solution(mesh):
    finer = Mesh(
        mesh.devices.reshape(mesh.shape["dp"], 2, 2, 4, 4),
        ("dp", "seq_0", "seq_1", "expert_0", "expert_1"),
    )
    return jax.shard_map(
        shards,
        mesh=finer,
        in_specs=(
            P(EXPERT, DP_SEQ, None),
            P(EXPERT, DP_SEQ, None),
            P(EXPERT, DP_SEQ, None),
            P(EXPERT, DP_SEQ, None),
            P(DP_SEQ, None),
            P(),
            P(),
            P(DP_EXPERT, None, SEQ),
            P(DP_EXPERT, None, SEQ),
            P(DP_EXPERT, SEQ, None),
            P(),
            P(EXPERT, "dp", None),
            P(EXPERT, None),
            P(EXPERT, DP_SEQ),
            P(EXPERT, None),
        ),
        out_specs=(P(), P(DP_EXPERT, SEQ, None), P(DP_SEQ_EXPERT, None)),
        check_vma=False,
    )
```

```python
import jax
import jax.numpy as jnp
from jax import lax
from jax.sharding import Mesh
from jax.sharding import PartitionSpec as P

QUERY_HEADS = 32
KEY_VALUE_HEADS = 4
HEAD_WIDTH = 128
DP_EXPERT = ("dp", "expert_0", "expert_1")
DP_SEQ = ("dp", "seq_0", "seq_1")
SEQ = ("seq_0", "seq_1")
DP_SEQ_EXPERT = ("dp", "seq_0", "seq_1", "expert_0", "expert_1")
EXPERT = ("expert_0", "expert_1")


MASKED = -1e30
EPSILON = 1e-06


def joined_along(blocks, dim):
    blocks = jnp.moveaxis(blocks, 0, dim)
    lengths = blocks.shape
    return blocks.reshape(*lengths[:dim], lengths[dim] * lengths[dim + 1], *lengths[dim + 2 :])


def from_everyone(array, axis):
    copies = jnp.broadcast_to(array, (lax.axis_size(axis), *array.shape))
    return lax.all_to_all(copies, axis, split_axis=0, concat_axis=0, tiled=True)


def gather_directly(array, axis, dim):
    return joined_along(from_everyone(array, axis), dim)


def in_blocks(array, dim, count):
    lengths = array.shape
    blocks = array.reshape(*lengths[:dim], count, lengths[dim] // count, *lengths[dim + 1 :])
    return jnp.moveaxis(blocks, dim, 0)


def sent_and_summed(array, axis, dim):
    count = lax.axis_size(axis)
    blocks = lax.all_to_all(in_blocks(array, dim, count), axis, 0, 0, tiled=True)
    return jnp.sum(blocks.astype(jnp.float32), axis=0)


def rows_summed(array, axis):
    count = lax.axis_size(axis)
    blocks = lax.all_to_all(array.reshape(count, 2, -1), axis, 0, 0, tiled=True)
    return jnp.sum(blocks.astype(jnp.float32), axis=0).reshape(1, -1)


def rows_gathered(row, axis):
    return from_everyone(row.reshape(2, -1), axis).reshape(lax.axis_size(axis), -1)


def rms_scale(stream):
    return lax.rsqrt(jnp.mean(stream * stream, axis=-1, keepdims=True) + EPSILON)


def head_logit(final, head_vec):
    return jnp.sum(final * rms_scale(final) * head_vec.astype(jnp.float32)[None, :], axis=1)


def across_group(buffer):
    return lax.all_to_all(buffer, EXPERT, split_axis=0, concat_axis=0, tiled=True)


def taken_together(array, axis):
    return from_everyone(array, axis).sum(axis=0)


def split_pair(value):
    high = value.astype(jnp.bfloat16)
    low = (value - high.astype(jnp.float32)).astype(jnp.bfloat16)
    return high, low


def join_pair(high, low):
    return high.astype(jnp.float32) + low.astype(jnp.float32)


def merge_heads(weighted_r, totals_r, peak_r):
    peak_all = jnp.max(peak_r, axis=0)
    factor = jnp.exp(peak_r - peak_all[None])
    weighted_sum = jnp.sum(weighted_r * factor[..., None], axis=0)
    totals_sum = jnp.sum(totals_r * factor, axis=0)
    merged = weighted_sum / totals_sum[..., None]
    return merged.reshape(merged.shape[0], -1).astype(jnp.bfloat16)


def shards(
    keys,
    values,
    queries,
    residual,
    out_proj,
    norm_gain,
    router,
    w_gate,
    w_up,
    w_down,
    head_vec,
    routes,
    step_pos,
    labels,
    trace_len,
):
    count_of_keys = keys.shape[1]
    query_groups = QUERY_HEADS // KEY_VALUE_HEADS
    query_width = queries.shape[2]
    own_routes = lax.dynamic_index_in_dim(routes[0], lax.axis_index(SEQ), 0, keepdims=False)
    query_row = jnp.concatenate(
        [
            queries[0],
            own_routes.astype(jnp.bfloat16)[None, :],
            jnp.zeros((1, 2 * HEAD_WIDTH - own_routes.shape[0]), jnp.bfloat16),
        ],
        axis=1,
    )
    query_rows = from_everyone(query_row.reshape(2, -1), DP_SEQ).reshape(lax.axis_size(DP_SEQ), -1)
    query_all = query_rows[:, :query_width]
    pack_routes = query_rows[:, query_width : query_width + routes.shape[2]].astype(jnp.int32)
    positions = step_pos[0]
    number_of_steps = positions.shape[0]
    lengths = trace_len[0]
    trace_ends = jnp.cumsum(lengths)
    starts = jnp.sum(
        jnp.where(trace_ends[None, :] <= positions[:, None], lengths[None, :], 0), axis=1
    )
    key_pos = lax.axis_index(DP_SEQ) * count_of_keys + jnp.arange(count_of_keys, dtype=jnp.int32)
    allowed = (key_pos[None, :] <= positions[:, None]) & (key_pos[None, :] >= starts[:, None])
    score_list = []
    for head_cluster in range(KEY_VALUE_HEADS):
        query_part = query_all[
            :,
            head_cluster
            * query_groups
            * HEAD_WIDTH : (head_cluster + 1)
            * query_groups
            * HEAD_WIDTH,
        ].reshape(number_of_steps * query_groups, HEAD_WIDTH)
        key_part = keys[0, :, head_cluster * HEAD_WIDTH : (head_cluster + 1) * HEAD_WIDTH]
        score_part = lax.dot_general(
            query_part, key_part, (((1,), (1,)), ((), ())), preferred_element_type=jnp.float32
        ) * HEAD_WIDTH ** (-0.5)
        score_part = score_part.reshape(number_of_steps, query_groups, count_of_keys)
        score_list.append(jnp.where(allowed[:, None, :], score_part, MASKED))
    scores = jnp.stack(score_list, axis=1).reshape(number_of_steps, QUERY_HEADS, count_of_keys)
    local_peak = jnp.max(scores, axis=2)
    heads_of_values = values[0].reshape(count_of_keys, KEY_VALUE_HEADS, HEAD_WIDTH)
    shift = local_peak.astype(jnp.bfloat16)
    complete_weight_rows = jnp.where(
        allowed[:, None, :], jnp.exp(scores - shift.astype(jnp.float32)[:, :, None]), 0.0
    )
    totals = jnp.sum(complete_weight_rows, axis=2)
    reduced_weight_rows = complete_weight_rows.astype(jnp.bfloat16).reshape(
        number_of_steps, KEY_VALUE_HEADS, query_groups, count_of_keys
    )
    weighted = jnp.einsum(
        "skgt,tkd->kgsd", reduced_weight_rows, heads_of_values, preferred_element_type=jnp.float32
    ).reshape(QUERY_HEADS, number_of_steps, HEAD_WIDTH)
    totals_hi, totals_lo = split_pair(totals)
    stats = jnp.stack([totals_hi, totals_lo, shift, jnp.zeros_like(shift)], axis=-1)
    stats = jnp.swapaxes(stats, 0, 1).reshape(QUERY_HEADS, 1, -1)
    filler = jnp.zeros((QUERY_HEADS, 1, HEAD_WIDTH), jnp.bfloat16)
    packed = jnp.concatenate([weighted.astype(jnp.bfloat16), stats, filler], axis=1)
    packed = packed.reshape(QUERY_HEADS, 2, -1)
    arrived = lax.all_to_all(packed, DP_SEQ, split_axis=0, concat_axis=0, tiled=True)
    arrived = arrived.reshape(arrived.shape[0], number_of_steps + 2, 1, HEAD_WIDTH)
    got_stats = arrived[:, number_of_steps].reshape(arrived.shape[0], number_of_steps, 1, 4)
    attn = merge_heads(
        arrived[:, :number_of_steps].astype(jnp.float32),
        join_pair(got_stats[..., 0], got_stats[..., 1]),
        got_stats[..., 2].astype(jnp.float32),
    )
    mixed = rows_summed(
        jnp.dot(attn, out_proj, preferred_element_type=jnp.float32).astype(jnp.bfloat16), DP_SEQ
    )
    stream = residual[0].astype(jnp.float32) + mixed
    normed = (stream * rms_scale(stream) * norm_gain.astype(jnp.float32)[None, :]).astype(
        jnp.bfloat16
    )
    pack_normed = rows_gathered(normed, DP_SEQ)
    rows = pack_normed.shape[0]
    width = pack_normed.shape[1]
    block_rows = routes.shape[1]
    topk = routes.shape[2]
    experts = router.shape[1]
    blocks = rows // block_rows
    group_size = lax.axis_size(EXPERT)
    capacity = min(block_rows, 2 * ((block_rows * topk + experts - 1) // experts))
    per_source = blocks * capacity
    slots = group_size * per_source
    logits = jnp.dot(pack_normed, router, preferred_element_type=jnp.float32)
    chosen = (pack_routes[:, :, None] == jnp.arange(experts, dtype=jnp.int32)[None, None, :]).astype(
        jnp.float32
    )
    picked = jnp.sum(chosen * logits[:, None, :], axis=2)
    gate_weight = jax.nn.softmax(picked, axis=-1)
    row_has = jnp.sum(chosen, axis=1).reshape(blocks, block_rows, experts)
    earlier = (jnp.cumsum(row_has, axis=1) - row_has).reshape(rows, experts)
    rank = jnp.sum(chosen * earlier[:, None, :], axis=2).astype(jnp.int32)
    block_of = (jnp.arange(rows, dtype=jnp.int32) // block_rows)[:, None]
    in_group = (pack_routes // group_size) == lax.axis_index("dp")
    dest_slot = (pack_routes % group_size) * per_source + block_of * capacity + rank
    slot_map = (
        (dest_slot[:, :, None] == jnp.arange(slots, dtype=jnp.int32)[None, None, :])
        & in_group[:, :, None]
    ).astype(jnp.float32)
    row_map = jnp.sum(slot_map, axis=1)
    weight_map = jnp.sum(gate_weight[:, :, None] * slot_map, axis=1)
    contract_rows = (((0,), (0,)), ((), ()))
    send_rows = lax.dot_general(
        row_map.astype(jnp.bfloat16), pack_normed, contract_rows, preferred_element_type=jnp.float32
    ).astype(jnp.bfloat16)
    arrived = across_group(send_rows.reshape(group_size, per_source, width)).reshape(slots, width)
    gate_act = jnp.dot(arrived, w_gate[0], preferred_element_type=jnp.float32)
    up_act = jnp.dot(arrived, w_up[0], preferred_element_type=jnp.float32)
    hidden = (jax.nn.silu(gate_act) * up_act).astype(jnp.bfloat16)
    partial_value = jnp.dot(hidden, w_down[0], preferred_element_type=jnp.float32)
    returned = across_group(
        partial_value.astype(jnp.bfloat16).reshape(group_size, per_source, width)
    ).reshape(slots, width)
    group_mix = lax.dot_general(
        weight_map,
        returned.astype(jnp.float32),
        (((1,), (0,)), ((), ())),
        precision=lax.Precision.HIGHEST,
    )
    expert_mix = rows_summed(group_mix.astype(jnp.bfloat16), DP_SEQ)
    final = stream + expert_mix
    reward, pull = jax.vjp(lambda value: head_logit(value, head_vec), final)
    target = labels[0].astype(jnp.float32)
    loss_term = jnp.sum(jax.nn.softplus(reward) - target * reward)
    logit_grad = jax.nn.sigmoid(reward) - target
    (final_grad,) = pull(logit_grad)
    d_mix = final_grad.astype(jnp.bfloat16)
    pack_grads = rows_gathered(d_mix, DP_SEQ)
    d_out = lax.dot_general(
        weight_map, pack_grads.astype(jnp.float32), contract_rows, precision=lax.Precision.HIGHEST
    ).astype(jnp.bfloat16)
    slot_grads = lax.dot_general(
        row_map.astype(jnp.bfloat16), pack_grads, contract_rows, preferred_element_type=jnp.float32
    )
    slot_dots = jnp.sum(slot_grads * returned.astype(jnp.float32), axis=1)
    dots_part = jnp.sum(slot_map * slot_dots[None, None, :], axis=2)
    own_row = jnp.arange(rows, dtype=jnp.int32) == lax.axis_index(DP_SEQ)
    payload = jnp.concatenate(
        [
            dots_part,
            jnp.where(own_row, loss_term, 0.0)[:, None],
            jnp.zeros((rows, HEAD_WIDTH // 8 - topk - 1), jnp.float32),
        ],
        axis=1,
    )
    summed = jnp.sum(
        from_everyone(payload.reshape(2, -1), DP_SEQ).reshape(lax.axis_size(DP_SEQ), rows, -1), axis=0
    )
    route_dot = summed[:, :topk]
    pack_loss = jnp.sum(summed[:, topk])
    pick_grad = gate_weight * (route_dot - jnp.sum(gate_weight * route_dot, axis=1, keepdims=True))
    d_logits = jnp.sum(chosen * pick_grad[:, :, None], axis=1)
    columns = pack_normed.reshape(rows, lax.axis_size(DP_SEQ), -1)
    my_columns = lax.dynamic_index_in_dim(columns, lax.axis_index(DP_SEQ), 1, keepdims=False)
    router_part = lax.dot_general(
        my_columns.astype(jnp.float32), d_logits, contract_rows, precision=lax.Precision.HIGHEST
    )
    router_part = router_part.reshape(group_size, -1)
    chunk = router_part.shape[1]
    router_hi, router_lo = split_pair(router_part)
    loss_hi, loss_lo = split_pair(pack_loss)
    side = jnp.concatenate(
        [
            router_hi,
            router_lo,
            jnp.broadcast_to(loss_hi, (group_size, 1)),
            jnp.broadcast_to(loss_lo, (group_size, 1)),
        ],
        axis=1,
    )
    side_width = -(-side.shape[1] // (per_source * HEAD_WIDTH)) * HEAD_WIDTH
    side = jnp.pad(side, ((0, 0), (0, per_source * side_width - side.shape[1])))
    sent = jnp.concatenate(
        [
            d_out.reshape(group_size, per_source, width),
            side.reshape(group_size, per_source, side_width),
        ],
        axis=2,
    )
    got = across_group(sent)
    grads_arrived = got[:, :, :width].reshape(slots, width)
    grad_down = lax.dot_general(
        hidden, grads_arrived, contract_rows, preferred_element_type=jnp.float32
    )
    grad_down = grad_down.astype(jnp.bfloat16).reshape((1,) + grad_down.shape)
    tail = got[:, :, width:].reshape(group_size, -1)
    grad_router = jnp.sum(join_pair(tail[:, :chunk], tail[:, chunk : 2 * chunk]), axis=0)
    grad_router = grad_router.reshape(-1, experts).astype(jnp.bfloat16)
    loss = jnp.sum(join_pair(tail[:, 2 * chunk], tail[:, 2 * chunk + 1]))
    return (loss, grad_down, grad_router)


def solution(mesh):
    finer = Mesh(
        mesh.devices.reshape(mesh.shape["dp"], 2, 2, 4, 4),
        ("dp", "seq_0", "seq_1", "expert_0", "expert_1"),
    )
    return jax.shard_map(
        shards,
        mesh=finer,
        in_specs=(
            P(EXPERT, DP_SEQ, None),
            P(EXPERT, DP_SEQ, None),
            P(EXPERT, DP_SEQ, None),
            P(EXPERT, DP_SEQ, None),
            P(DP_SEQ, None),
            P(),
            P(),
            P(DP_EXPERT, None, SEQ),
            P(DP_EXPERT, None, SEQ),
            P(DP_EXPERT, SEQ, None),
            P(),
            P(EXPERT, "dp", None),
            P(EXPERT, None),
            P(EXPERT, DP_SEQ),
            P(EXPERT, None),
        ),
        out_specs=(P(), P(DP_EXPERT, SEQ, None), P(DP_SEQ_EXPERT, None)),
        check_vma=False,
    )
```

```python
import jax
import jax.numpy as jnp
from jax import lax
from jax.sharding import Mesh
from jax.sharding import PartitionSpec as P

QUERY_HEADS = 32
KEY_VALUE_HEADS = 4
HEAD_WIDTH = 128
DP_EXPERT = ("dp", "expert_0", "expert_1")
DP_SEQ = ("dp", "seq_0", "seq_1")
SEQ = ("seq_0", "seq_1")
DP_SEQ_EXPERT = ("dp", "seq_0", "seq_1", "expert_0", "expert_1")
EXPERT = ("expert_0", "expert_1")


MASKED = -1e30
EPSILON = 1e-06


def joined_along(blocks, dim):
    blocks = jnp.moveaxis(blocks, 0, dim)
    lengths = blocks.shape
    return blocks.reshape(*lengths[:dim], lengths[dim] * lengths[dim + 1], *lengths[dim + 2 :])


def from_everyone(array, axis):
    copies = jnp.broadcast_to(array, (lax.axis_size(axis), *array.shape))
    return lax.all_to_all(copies, axis, split_axis=0, concat_axis=0, tiled=True)


def gather_directly(array, axis, dim):
    return joined_along(from_everyone(array, axis), dim)


def in_blocks(array, dim, count):
    lengths = array.shape
    blocks = array.reshape(*lengths[:dim], count, lengths[dim] // count, *lengths[dim + 1 :])
    return jnp.moveaxis(blocks, dim, 0)


def sent_and_summed(array, axis, dim):
    count = lax.axis_size(axis)
    blocks = lax.all_to_all(in_blocks(array, dim, count), axis, 0, 0, tiled=True)
    return jnp.sum(blocks.astype(jnp.float32), axis=0)


def rows_summed(array, axis):
    count = lax.axis_size(axis)
    blocks = lax.all_to_all(array.reshape(count, 2, -1), axis, 0, 0, tiled=True)
    return jnp.sum(blocks.astype(jnp.float32), axis=0).reshape(1, -1)


def rows_gathered(row, axis):
    return from_everyone(row.reshape(2, -1), axis).reshape(lax.axis_size(axis), -1)


def rms_scale(stream):
    return lax.rsqrt(jnp.mean(stream * stream, axis=-1, keepdims=True) + EPSILON)


def head_logit(final, head_vec):
    return jnp.sum(final * rms_scale(final) * head_vec.astype(jnp.float32)[None, :], axis=1)


def across_group(buffer):
    return lax.all_to_all(buffer, EXPERT, split_axis=0, concat_axis=0, tiled=True)


def taken_together(array, axis):
    return from_everyone(array, axis).sum(axis=0)


def split_pair(value):
    high = value.astype(jnp.bfloat16)
    low = (value - high.astype(jnp.float32)).astype(jnp.bfloat16)
    return high, low


def join_pair(high, low):
    return high.astype(jnp.float32) + low.astype(jnp.float32)


def merge_heads(weighted_r, totals_r, peak_r):
    peak_all = jnp.max(peak_r, axis=0)
    factor = jnp.exp(peak_r - peak_all[None])
    weighted_sum = jnp.sum(weighted_r * factor[..., None], axis=0)
    totals_sum = jnp.sum(totals_r * factor, axis=0)
    merged = weighted_sum / totals_sum[..., None]
    return merged.reshape(merged.shape[0], -1).astype(jnp.bfloat16)


def shards(
    keys,
    values,
    queries,
    residual,
    out_proj,
    norm_gain,
    router,
    w_gate,
    w_up,
    w_down,
    head_vec,
    routes,
    step_pos,
    labels,
    trace_len,
):
    count_of_keys = keys.shape[1]
    query_groups = QUERY_HEADS // KEY_VALUE_HEADS
    query_width = queries.shape[2]
    own_routes = lax.dynamic_index_in_dim(routes[0], lax.axis_index(SEQ), 0, keepdims=False)
    query_row = jnp.concatenate(
        [
            queries[0],
            own_routes.astype(jnp.bfloat16)[None, :],
            jnp.zeros((1, 2 * HEAD_WIDTH - own_routes.shape[0]), jnp.bfloat16),
        ],
        axis=1,
    )
    query_rows = from_everyone(query_row.reshape(2, -1), DP_SEQ).reshape(lax.axis_size(DP_SEQ), -1)
    query_all = query_rows[:, :query_width]
    pack_routes = query_rows[:, query_width : query_width + routes.shape[2]].astype(jnp.int32)
    positions = step_pos[0]
    number_of_steps = positions.shape[0]
    lengths = trace_len[0]
    trace_ends = jnp.cumsum(lengths)
    starts = jnp.sum(
        jnp.where(trace_ends[None, :] <= positions[:, None], lengths[None, :], 0), axis=1
    )
    key_pos = lax.axis_index(DP_SEQ) * count_of_keys + jnp.arange(count_of_keys, dtype=jnp.int32)
    allowed = (key_pos[None, :] <= positions[:, None]) & (key_pos[None, :] >= starts[:, None])
    score_list = []
    for head_cluster in range(KEY_VALUE_HEADS):
        query_part = query_all[
            :,
            head_cluster
            * query_groups
            * HEAD_WIDTH : (head_cluster + 1)
            * query_groups
            * HEAD_WIDTH,
        ].reshape(number_of_steps * query_groups, HEAD_WIDTH)
        key_part = keys[0, :, head_cluster * HEAD_WIDTH : (head_cluster + 1) * HEAD_WIDTH]
        score_part = lax.dot_general(
            query_part, key_part, (((1,), (1,)), ((), ())), preferred_element_type=jnp.float32
        ) * HEAD_WIDTH ** (-0.5)
        score_part = score_part.reshape(number_of_steps, query_groups, count_of_keys)
        score_list.append(jnp.where(allowed[:, None, :], score_part, MASKED))
    scores = jnp.stack(score_list, axis=1).reshape(number_of_steps, QUERY_HEADS, count_of_keys)
    local_peak = jnp.max(scores, axis=2)
    heads_of_values = values[0].reshape(count_of_keys, KEY_VALUE_HEADS, HEAD_WIDTH)
    shift = local_peak.astype(jnp.bfloat16)
    complete_weight_rows = jnp.where(
        allowed[:, None, :], jnp.exp(scores - shift.astype(jnp.float32)[:, :, None]), 0.0
    )
    totals = jnp.sum(complete_weight_rows, axis=2)
    reduced_weight_rows = complete_weight_rows.astype(jnp.bfloat16).reshape(
        number_of_steps, KEY_VALUE_HEADS, query_groups, count_of_keys
    )
    weighted = jnp.einsum(
        "skgt,tkd->kgsd", reduced_weight_rows, heads_of_values, preferred_element_type=jnp.float32
    ).reshape(QUERY_HEADS, number_of_steps, HEAD_WIDTH)
    totals_hi, totals_lo = split_pair(totals)
    stats = jnp.stack([totals_hi, totals_lo, shift, jnp.zeros_like(shift)], axis=-1)
    stats = jnp.swapaxes(stats, 0, 1).reshape(QUERY_HEADS, 1, -1)
    filler = jnp.zeros((QUERY_HEADS, 1, HEAD_WIDTH), jnp.bfloat16)
    packed = jnp.concatenate([weighted.astype(jnp.bfloat16), stats, filler], axis=1)
    packed = packed.reshape(QUERY_HEADS, 2, -1)
    arrived = lax.all_to_all(packed, DP_SEQ, split_axis=0, concat_axis=0, tiled=True)
    arrived = arrived.reshape(arrived.shape[0], number_of_steps + 2, 1, HEAD_WIDTH)
    got_stats = arrived[:, number_of_steps].reshape(arrived.shape[0], number_of_steps, 1, 4)
    attn = merge_heads(
        arrived[:, :number_of_steps].astype(jnp.float32),
        join_pair(got_stats[..., 0], got_stats[..., 1]),
        got_stats[..., 2].astype(jnp.float32),
    )
    mixed = rows_summed(
        jnp.dot(attn, out_proj, preferred_element_type=jnp.float32).astype(jnp.bfloat16), DP_SEQ
    )
    stream = residual[0].astype(jnp.float32) + mixed
    normed = (stream * rms_scale(stream) * norm_gain.astype(jnp.float32)[None, :]).astype(
        jnp.bfloat16
    )
    pack_normed = rows_gathered(normed, DP_SEQ)
    rows = pack_normed.shape[0]
    width = pack_normed.shape[1]
    block_rows = routes.shape[1]
    topk = routes.shape[2]
    experts = router.shape[1]
    blocks = rows // block_rows
    group_size = lax.axis_size(EXPERT)
    capacity = min(block_rows, 2 * ((block_rows * topk + experts - 1) // experts))
    per_source = blocks * capacity
    slots = group_size * per_source
    logits = jnp.dot(pack_normed, router, preferred_element_type=jnp.float32)
    chosen = (pack_routes[:, :, None] == jnp.arange(experts, dtype=jnp.int32)[None, None, :]).astype(
        jnp.float32
    )
    picked = jnp.sum(chosen * logits[:, None, :], axis=2)
    gate_weight = jax.nn.softmax(picked, axis=-1)
    row_has = jnp.sum(chosen, axis=1).reshape(blocks, block_rows, experts)
    earlier = (jnp.cumsum(row_has, axis=1) - row_has).reshape(rows, experts)
    rank = jnp.sum(chosen * earlier[:, None, :], axis=2).astype(jnp.int32)
    block_of = (jnp.arange(rows, dtype=jnp.int32) // block_rows)[:, None]
    in_group = (pack_routes // group_size) == lax.axis_index("dp")
    dest_slot = (pack_routes % group_size) * per_source + block_of * capacity + rank
    slot_map = (
        (dest_slot[:, :, None] == jnp.arange(slots, dtype=jnp.int32)[None, None, :])
        & in_group[:, :, None]
    ).astype(jnp.float32)
    row_map = jnp.sum(slot_map, axis=1)
    weight_map = jnp.sum(gate_weight[:, :, None] * slot_map, axis=1)
    contract_rows = (((0,), (0,)), ((), ()))
    send_rows = lax.dot_general(
        row_map.astype(jnp.bfloat16), pack_normed, contract_rows, preferred_element_type=jnp.float32
    ).astype(jnp.bfloat16)
    arrived = across_group(send_rows.reshape(group_size, per_source, width)).reshape(slots, width)
    gate_act = jnp.dot(arrived, w_gate[0], preferred_element_type=jnp.float32)
    up_act = jnp.dot(arrived, w_up[0], preferred_element_type=jnp.float32)
    hidden = (jax.nn.silu(gate_act) * up_act).astype(jnp.bfloat16)
    partial_value = jnp.dot(hidden, w_down[0], preferred_element_type=jnp.float32)
    returned = across_group(
        partial_value.astype(jnp.bfloat16).reshape(group_size, per_source, width)
    ).reshape(slots, width)
    group_mix = lax.dot_general(
        weight_map,
        returned.astype(jnp.float32),
        (((1,), (0,)), ((), ())),
        precision=lax.Precision.HIGHEST,
    )
    expert_mix = rows_summed(group_mix.astype(jnp.bfloat16), DP_SEQ)
    final = stream + expert_mix
    head = head_vec.astype(jnp.float32)[None, :]
    rho = rms_scale(final)
    final_head = jnp.sum(final * head, axis=-1, keepdims=True)
    reward = (rho * final_head)[:, 0]
    target = labels[0].astype(jnp.float32)
    loss_term = jnp.sum(jax.nn.softplus(reward) - target * reward)
    logit_grad = (jax.nn.sigmoid(reward) - target)[:, None]
    final_grad = logit_grad * (rho * head - rho * rho * rho * final_head / final.shape[1] * final)
    d_mix = final_grad.astype(jnp.bfloat16)
    pack_grads = rows_gathered(d_mix, DP_SEQ)
    d_out = lax.dot_general(
        weight_map, pack_grads.astype(jnp.float32), contract_rows, precision=lax.Precision.HIGHEST
    ).astype(jnp.bfloat16)
    slot_grads = lax.dot_general(
        row_map.astype(jnp.bfloat16), pack_grads, contract_rows, preferred_element_type=jnp.float32
    )
    slot_dots = jnp.sum(slot_grads * returned.astype(jnp.float32), axis=1)
    dots_part = jnp.sum(slot_map * slot_dots[None, None, :], axis=2)
    own_row = jnp.arange(rows, dtype=jnp.int32) == lax.axis_index(DP_SEQ)
    payload = jnp.concatenate(
        [
            dots_part,
            jnp.where(own_row, loss_term, 0.0)[:, None],
            jnp.zeros((rows, HEAD_WIDTH // 8 - topk - 1), jnp.float32),
        ],
        axis=1,
    )
    summed = jnp.sum(
        from_everyone(payload.reshape(2, -1), DP_SEQ).reshape(lax.axis_size(DP_SEQ), rows, -1), axis=0
    )
    route_dot = summed[:, :topk]
    pack_loss = jnp.sum(summed[:, topk])
    pick_grad = gate_weight * (route_dot - jnp.sum(gate_weight * route_dot, axis=1, keepdims=True))
    d_logits = jnp.sum(chosen * pick_grad[:, :, None], axis=1)
    columns = pack_normed.reshape(rows, lax.axis_size(DP_SEQ), -1)
    my_columns = lax.dynamic_index_in_dim(columns, lax.axis_index(DP_SEQ), 1, keepdims=False)
    router_part = lax.dot_general(
        my_columns.astype(jnp.float32), d_logits, contract_rows, precision=lax.Precision.HIGHEST
    )
    router_part = router_part.reshape(group_size, -1)
    chunk = router_part.shape[1]
    router_hi, router_lo = split_pair(router_part)
    loss_hi, loss_lo = split_pair(pack_loss)
    side = jnp.concatenate(
        [
            router_hi,
            router_lo,
            jnp.broadcast_to(loss_hi, (group_size, 1)),
            jnp.broadcast_to(loss_lo, (group_size, 1)),
        ],
        axis=1,
    )
    side_width = -(-side.shape[1] // (per_source * HEAD_WIDTH)) * HEAD_WIDTH
    side = jnp.pad(side, ((0, 0), (0, per_source * side_width - side.shape[1])))
    sent = jnp.concatenate(
        [
            d_out.reshape(group_size, per_source, width),
            side.reshape(group_size, per_source, side_width),
        ],
        axis=2,
    )
    got = across_group(sent)
    grads_arrived = got[:, :, :width].reshape(slots, width)
    grad_down = lax.dot_general(
        hidden, grads_arrived, contract_rows, preferred_element_type=jnp.float32
    )
    grad_down = grad_down.astype(jnp.bfloat16).reshape((1,) + grad_down.shape)
    tail = got[:, :, width:].reshape(group_size, -1)
    grad_router = jnp.sum(join_pair(tail[:, :chunk], tail[:, chunk : 2 * chunk]), axis=0)
    grad_router = grad_router.reshape(-1, experts).astype(jnp.bfloat16)
    loss = jnp.sum(join_pair(tail[:, 2 * chunk], tail[:, 2 * chunk + 1]))
    return (loss, grad_down, grad_router)


def solution(mesh):
    finer = Mesh(
        mesh.devices.reshape(mesh.shape["dp"], 2, 2, 4, 4),
        ("dp", "seq_0", "seq_1", "expert_0", "expert_1"),
    )
    return jax.shard_map(
        shards,
        mesh=finer,
        in_specs=(
            P(EXPERT, DP_SEQ, None),
            P(EXPERT, DP_SEQ, None),
            P(EXPERT, DP_SEQ, None),
            P(EXPERT, DP_SEQ, None),
            P(DP_SEQ, None),
            P(),
            P(),
            P(DP_EXPERT, None, SEQ),
            P(DP_EXPERT, None, SEQ),
            P(DP_EXPERT, SEQ, None),
            P(),
            P(EXPERT, "dp", None),
            P(EXPERT, None),
            P(EXPERT, DP_SEQ),
            P(EXPERT, None),
        ),
        out_specs=(P(), P(DP_EXPERT, SEQ, None), P(DP_SEQ_EXPERT, None)),
        check_vma=False,
    )
```

```python
import jax
import jax.numpy as jnp
from jax import lax
from jax.sharding import Mesh
from jax.sharding import PartitionSpec as P

QUERY_HEADS = 32
KEY_VALUE_HEADS = 4
HEAD_WIDTH = 128
DP_EXPERT = ("dp", "expert_0", "expert_1")
DP_SEQ = ("dp", "seq_0", "seq_1")
SEQ = ("seq_0", "seq_1")
DP_SEQ_EXPERT = ("dp", "seq_0", "seq_1", "expert_0", "expert_1")
EXPERT = ("expert_0", "expert_1")


MASKED = -1e30
EPSILON = 1e-06


def joined_along(blocks, dim):
    blocks = jnp.moveaxis(blocks, 0, dim)
    lengths = blocks.shape
    return blocks.reshape(*lengths[:dim], lengths[dim] * lengths[dim + 1], *lengths[dim + 2 :])


def from_everyone(array, axis):
    copies = jnp.broadcast_to(array, (lax.axis_size(axis), *array.shape))
    return lax.all_to_all(copies, axis, split_axis=0, concat_axis=0, tiled=True)


def gather_directly(array, axis, dim):
    return joined_along(from_everyone(array, axis), dim)


def in_blocks(array, dim, count):
    lengths = array.shape
    blocks = array.reshape(*lengths[:dim], count, lengths[dim] // count, *lengths[dim + 1 :])
    return jnp.moveaxis(blocks, dim, 0)


def sent_and_summed(array, axis, dim):
    count = lax.axis_size(axis)
    blocks = lax.all_to_all(in_blocks(array, dim, count), axis, 0, 0, tiled=True)
    return jnp.sum(blocks.astype(jnp.float32), axis=0)


def rows_summed(array, axis):
    count = lax.axis_size(axis)
    blocks = lax.all_to_all(array.reshape(count, 2, -1), axis, 0, 0, tiled=True)
    return jnp.sum(blocks.astype(jnp.float32), axis=0).reshape(1, -1)


def rows_gathered(row, axis):
    return from_everyone(row.reshape(2, -1), axis).reshape(lax.axis_size(axis), -1)


def rms_scale(stream):
    return lax.rsqrt(jnp.mean(stream * stream, axis=-1, keepdims=True) + EPSILON)


def head_logit(final, head_vec):
    return jnp.sum(final * rms_scale(final) * head_vec.astype(jnp.float32)[None, :], axis=1)


def across_group(buffer):
    return lax.all_to_all(buffer, EXPERT, split_axis=0, concat_axis=0, tiled=True)


def taken_together(array, axis):
    return from_everyone(array, axis).sum(axis=0)


def split_pair(value):
    high = value.astype(jnp.bfloat16)
    low = (value - high.astype(jnp.float32)).astype(jnp.bfloat16)
    return high, low


def paired_dot(wide, narrow, dims):
    high, low = split_pair(wide)
    return lax.dot_general(high, narrow, dims, preferred_element_type=jnp.float32) + lax.dot_general(
        low, narrow, dims, preferred_element_type=jnp.float32
    )


def join_pair(high, low):
    return high.astype(jnp.float32) + low.astype(jnp.float32)


def merge_heads(weighted_r, totals_r, peak_r):
    peak_all = jnp.max(peak_r, axis=0)
    factor = jnp.exp(peak_r - peak_all[None])
    weighted_sum = jnp.sum(weighted_r * factor[..., None], axis=0)
    totals_sum = jnp.sum(totals_r * factor, axis=0)
    merged = weighted_sum / totals_sum[..., None]
    return merged.reshape(merged.shape[0], -1).astype(jnp.bfloat16)


def shards(
    keys,
    values,
    queries,
    residual,
    out_proj,
    norm_gain,
    router,
    w_gate,
    w_up,
    w_down,
    head_vec,
    routes,
    step_pos,
    labels,
    trace_len,
):
    count_of_keys = keys.shape[1]
    query_groups = QUERY_HEADS // KEY_VALUE_HEADS
    query_width = queries.shape[2]
    own_routes = lax.dynamic_index_in_dim(routes[0], lax.axis_index(SEQ), 0, keepdims=False)
    query_row = jnp.concatenate(
        [
            queries[0],
            own_routes.astype(jnp.bfloat16)[None, :],
            jnp.zeros((1, 2 * HEAD_WIDTH - own_routes.shape[0]), jnp.bfloat16),
        ],
        axis=1,
    )
    query_rows = from_everyone(query_row.reshape(2, -1), DP_SEQ).reshape(lax.axis_size(DP_SEQ), -1)
    query_all = query_rows[:, :query_width]
    pack_routes = query_rows[:, query_width : query_width + routes.shape[2]].astype(jnp.int32)
    positions = step_pos[0]
    number_of_steps = positions.shape[0]
    lengths = trace_len[0]
    trace_ends = jnp.cumsum(lengths)
    starts = jnp.sum(
        jnp.where(trace_ends[None, :] <= positions[:, None], lengths[None, :], 0), axis=1
    )
    key_pos = lax.axis_index(DP_SEQ) * count_of_keys + jnp.arange(count_of_keys, dtype=jnp.int32)
    allowed = (key_pos[None, :] <= positions[:, None]) & (key_pos[None, :] >= starts[:, None])
    score_list = []
    for head_cluster in range(KEY_VALUE_HEADS):
        query_part = query_all[
            :,
            head_cluster
            * query_groups
            * HEAD_WIDTH : (head_cluster + 1)
            * query_groups
            * HEAD_WIDTH,
        ].reshape(number_of_steps * query_groups, HEAD_WIDTH)
        key_part = keys[0, :, head_cluster * HEAD_WIDTH : (head_cluster + 1) * HEAD_WIDTH]
        score_part = lax.dot_general(
            query_part, key_part, (((1,), (1,)), ((), ())), preferred_element_type=jnp.float32
        ) * HEAD_WIDTH ** (-0.5)
        score_part = score_part.reshape(number_of_steps, query_groups, count_of_keys)
        score_list.append(jnp.where(allowed[:, None, :], score_part, MASKED))
    scores = jnp.stack(score_list, axis=1).reshape(number_of_steps, QUERY_HEADS, count_of_keys)
    local_peak = jnp.max(scores, axis=2)
    heads_of_values = values[0].reshape(count_of_keys, KEY_VALUE_HEADS, HEAD_WIDTH)
    shift = local_peak.astype(jnp.bfloat16)
    complete_weight_rows = jnp.where(
        allowed[:, None, :], jnp.exp(scores - shift.astype(jnp.float32)[:, :, None]), 0.0
    )
    totals = jnp.sum(complete_weight_rows, axis=2)
    reduced_weight_rows = complete_weight_rows.astype(jnp.bfloat16).reshape(
        number_of_steps, KEY_VALUE_HEADS, query_groups, count_of_keys
    )
    weighted = jnp.einsum(
        "skgt,tkd->kgsd", reduced_weight_rows, heads_of_values, preferred_element_type=jnp.float32
    ).reshape(QUERY_HEADS, number_of_steps, HEAD_WIDTH)
    totals_hi, totals_lo = split_pair(totals)
    stats = jnp.stack([totals_hi, totals_lo, shift, jnp.zeros_like(shift)], axis=-1)
    stats = jnp.swapaxes(stats, 0, 1).reshape(QUERY_HEADS, 1, -1)
    filler = jnp.zeros((QUERY_HEADS, 1, HEAD_WIDTH), jnp.bfloat16)
    packed = jnp.concatenate([weighted.astype(jnp.bfloat16), stats, filler], axis=1)
    packed = packed.reshape(QUERY_HEADS, 2, -1)
    arrived = lax.all_to_all(packed, DP_SEQ, split_axis=0, concat_axis=0, tiled=True)
    arrived = arrived.reshape(arrived.shape[0], number_of_steps + 2, 1, HEAD_WIDTH)
    got_stats = arrived[:, number_of_steps].reshape(arrived.shape[0], number_of_steps, 1, 4)
    attn = merge_heads(
        arrived[:, :number_of_steps].astype(jnp.float32),
        join_pair(got_stats[..., 0], got_stats[..., 1]),
        got_stats[..., 2].astype(jnp.float32),
    )
    mixed = rows_summed(
        jnp.dot(attn, out_proj, preferred_element_type=jnp.float32).astype(jnp.bfloat16), DP_SEQ
    )
    stream = residual[0].astype(jnp.float32) + mixed
    normed = (stream * rms_scale(stream) * norm_gain.astype(jnp.float32)[None, :]).astype(
        jnp.bfloat16
    )
    pack_normed = rows_gathered(normed, DP_SEQ)
    rows = pack_normed.shape[0]
    width = pack_normed.shape[1]
    block_rows = routes.shape[1]
    topk = routes.shape[2]
    experts = router.shape[1]
    blocks = rows // block_rows
    group_size = lax.axis_size(EXPERT)
    capacity = min(block_rows, 2 * ((block_rows * topk + experts - 1) // experts))
    per_source = blocks * capacity
    slots = group_size * per_source
    logits = jnp.dot(pack_normed, router, preferred_element_type=jnp.float32)
    chosen = (pack_routes[:, :, None] == jnp.arange(experts, dtype=jnp.int32)[None, None, :]).astype(
        jnp.float32
    )
    picked = jnp.sum(chosen * logits[:, None, :], axis=2)
    gate_weight = jax.nn.softmax(picked, axis=-1)
    row_has = jnp.sum(chosen, axis=1).reshape(blocks, block_rows, experts)
    earlier = (jnp.cumsum(row_has, axis=1) - row_has).reshape(rows, experts)
    rank = jnp.sum(chosen * earlier[:, None, :], axis=2).astype(jnp.int32)
    block_of = (jnp.arange(rows, dtype=jnp.int32) // block_rows)[:, None]
    in_group = (pack_routes // group_size) == lax.axis_index("dp")
    dest_slot = (pack_routes % group_size) * per_source + block_of * capacity + rank
    slot_map = (
        (dest_slot[:, :, None] == jnp.arange(slots, dtype=jnp.int32)[None, None, :])
        & in_group[:, :, None]
    ).astype(jnp.float32)
    row_map = jnp.sum(slot_map, axis=1)
    weight_map = jnp.sum(gate_weight[:, :, None] * slot_map, axis=1)
    contract_rows = (((0,), (0,)), ((), ()))
    send_rows = lax.dot_general(
        row_map.astype(jnp.bfloat16), pack_normed, contract_rows, preferred_element_type=jnp.float32
    ).astype(jnp.bfloat16)
    arrived = across_group(send_rows.reshape(group_size, per_source, width)).reshape(slots, width)
    gate_act = jnp.dot(arrived, w_gate[0], preferred_element_type=jnp.float32)
    up_act = jnp.dot(arrived, w_up[0], preferred_element_type=jnp.float32)
    hidden = (jax.nn.silu(gate_act) * up_act).astype(jnp.bfloat16)
    partial_value = jnp.dot(hidden, w_down[0], preferred_element_type=jnp.float32)
    returned = across_group(
        partial_value.astype(jnp.bfloat16).reshape(group_size, per_source, width)
    ).reshape(slots, width)
    group_mix = paired_dot(weight_map, returned, (((1,), (0,)), ((), ())))
    expert_mix = rows_summed(group_mix.astype(jnp.bfloat16), DP_SEQ)
    final = stream + expert_mix
    head = head_vec.astype(jnp.float32)[None, :]
    rho = rms_scale(final)
    final_head = jnp.sum(final * head, axis=-1, keepdims=True)
    reward = (rho * final_head)[:, 0]
    target = labels[0].astype(jnp.float32)
    loss_term = jnp.sum(jax.nn.softplus(reward) - target * reward)
    logit_grad = (jax.nn.sigmoid(reward) - target)[:, None]
    final_grad = logit_grad * (rho * head - rho * rho * rho * final_head / final.shape[1] * final)
    d_mix = final_grad.astype(jnp.bfloat16)
    pack_grads = rows_gathered(d_mix, DP_SEQ)
    d_out = paired_dot(weight_map, pack_grads, contract_rows).astype(jnp.bfloat16)
    slot_grads = lax.dot_general(
        row_map.astype(jnp.bfloat16), pack_grads, contract_rows, preferred_element_type=jnp.float32
    )
    slot_dots = jnp.sum(slot_grads * returned.astype(jnp.float32), axis=1)
    dots_part = jnp.sum(slot_map * slot_dots[None, None, :], axis=2)
    own_row = jnp.arange(rows, dtype=jnp.int32) == lax.axis_index(DP_SEQ)
    payload = jnp.concatenate(
        [
            dots_part,
            jnp.where(own_row, loss_term, 0.0)[:, None],
            jnp.zeros((rows, HEAD_WIDTH // 8 - topk - 1), jnp.float32),
        ],
        axis=1,
    )
    summed = jnp.sum(
        from_everyone(payload.reshape(2, -1), DP_SEQ).reshape(lax.axis_size(DP_SEQ), rows, -1), axis=0
    )
    route_dot = summed[:, :topk]
    pack_loss = jnp.sum(summed[:, topk])
    pick_grad = gate_weight * (route_dot - jnp.sum(gate_weight * route_dot, axis=1, keepdims=True))
    d_logits = jnp.sum(chosen * pick_grad[:, :, None], axis=1)
    columns = pack_normed.reshape(rows, lax.axis_size(DP_SEQ), -1)
    my_columns = lax.dynamic_index_in_dim(columns, lax.axis_index(DP_SEQ), 1, keepdims=False)
    router_part = paired_dot(d_logits, my_columns, contract_rows).T
    router_part = router_part.reshape(group_size, -1)
    chunk = router_part.shape[1]
    router_hi, router_lo = split_pair(router_part)
    loss_hi, loss_lo = split_pair(pack_loss)
    side = jnp.concatenate(
        [
            router_hi,
            router_lo,
            jnp.broadcast_to(loss_hi, (group_size, 1)),
            jnp.broadcast_to(loss_lo, (group_size, 1)),
        ],
        axis=1,
    )
    side_width = -(-side.shape[1] // (per_source * HEAD_WIDTH)) * HEAD_WIDTH
    side = jnp.pad(side, ((0, 0), (0, per_source * side_width - side.shape[1])))
    sent = jnp.concatenate(
        [
            d_out.reshape(group_size, per_source, width),
            side.reshape(group_size, per_source, side_width),
        ],
        axis=2,
    )
    got = across_group(sent)
    grads_arrived = got[:, :, :width].reshape(slots, width)
    grad_down = lax.dot_general(
        hidden, grads_arrived, contract_rows, preferred_element_type=jnp.float32
    )
    grad_down = grad_down.astype(jnp.bfloat16).reshape((1,) + grad_down.shape)
    tail = got[:, :, width:].reshape(group_size, -1)
    grad_router = jnp.sum(join_pair(tail[:, :chunk], tail[:, chunk : 2 * chunk]), axis=0)
    grad_router = grad_router.reshape(-1, experts).astype(jnp.bfloat16)
    loss = jnp.sum(join_pair(tail[:, 2 * chunk], tail[:, 2 * chunk + 1]))
    return (loss, grad_down, grad_router)


def solution(mesh):
    finer = Mesh(
        mesh.devices.reshape(mesh.shape["dp"], 2, 2, 4, 4),
        ("dp", "seq_0", "seq_1", "expert_0", "expert_1"),
    )
    return jax.shard_map(
        shards,
        mesh=finer,
        in_specs=(
            P(EXPERT, DP_SEQ, None),
            P(EXPERT, DP_SEQ, None),
            P(EXPERT, DP_SEQ, None),
            P(EXPERT, DP_SEQ, None),
            P(DP_SEQ, None),
            P(),
            P(),
            P(DP_EXPERT, None, SEQ),
            P(DP_EXPERT, None, SEQ),
            P(DP_EXPERT, SEQ, None),
            P(),
            P(EXPERT, "dp", None),
            P(EXPERT, None),
            P(EXPERT, DP_SEQ),
            P(EXPERT, None),
        ),
        out_specs=(P(), P(DP_EXPERT, SEQ, None), P(DP_SEQ_EXPERT, None)),
        check_vma=False,
    )
```
